32 devices in a mesh: east: 4 (over x, core), north: 2 (over y), depth: 4 (over z).
Axes of the slice: x: 2, y: 2, z: 4, core: 2. Of those that a mesh axis runs over, the one named last changes fastest.
Arguments:
- thermal_field: float32 [256, 32, 256], P('depth', 'east', 'north'), may hold values from 0.2 to 1.6, as said below
- liquid_fraction: float32 [256, 32, 256], P('depth', 'east', 'north'), may hold values from 0 to 0.6
- steam_content_grid: float32 [256, 32, 256], P('depth', 'east', 'north'), may hold values from 0 to 1
- carbonic_gas_grid: float32 [256, 32, 256], P('depth', 'east', 'north'), may hold values from 0 to 0.5
- stratum_number_grid: int32 [256, 32, 256], P('depth', 'east', 'north'), may hold values from 0 to 11, as said below
- injection_flags: int32 [256, 32, 256], P('depth', 'east', 'north'), may hold values 0 or 1
- lateral_transmissivity: float32 [2, 12], replicated, may hold values from 0.02 to 0.12
- vertical_transmissivity: float32 [12], replicated, may hold values from 20 to 2000
- stratum_advection_offsets: float32 [2, 12], replicated, may hold values from -0.45 to 0.45
Outputs:
- thermal_field_next: float32 [256, 32, 256], P('depth', 'east', 'north')
- liquid_fraction_next: float32 [256, 32, 256], P('depth', 'east', 'north')
- steam_content_next: float32 [256, 32, 256], P('depth', 'east', 'north')
- carbonic_gas_next: float32 [256, 32, 256], P('depth', 'east', 'north')
The draws below stay inside these ranges and needn't reach their ends.
Inputs may be any that keep to these rules, and one draw needn't show every extreme that they name: `thermal_field`: drawn per cell. `stratum_number_grid`: every layer number occurs.
All inputs are finite; a program needn't handle non-finite values. No bound on the sum of `injection_flags` on one device may be relied on, other than what follows from the above.
Results may differ from the reference program's by a relative error of at most 0.0003.
Values sent between devices are 32-bit elements; how exact they have to be, the bound alone decides.
No kernel may reach another device: no remote copies, remote signals or barrier semaphores. Data moves between devices by JAX's collectives and lax.ppermute only.
A program may use at most 64 MiB of HBM per device.

```python
import math
import jax
import jax.numpy as jnp
from jax import lax

SECTIONS = 4
LAYERS = 12
NX = 32
NY = 256
NZ = 256


def draw_thermal_field(key, part):
    return jax.random.uniform(key, (NZ, NX, NY), jnp.float32, 0.2, 1.6)


def draw_stratum_number_grid(key, part):
    slope_key, thick_key, jitter_key = jax.random.split(key, 3)
    slopes = jax.random.randint(slope_key, (2,), -3, 4)
    thickness = jax.random.randint(thick_key, (), 3, 7)
    jitter = jax.random.randint(jitter_key, (NZ, NX, NY), 0, 2)
    depth_rank = jnp.arange(NZ, dtype=jnp.int32)[:, None, None]
    east_rank = jnp.arange(NX, dtype=jnp.int32)[None, :, None]
    north_rank = jnp.arange(NY, dtype=jnp.int32)[None, None, :]
    height = depth_rank * 8 + slopes[0] * east_rank + slopes[1] * north_rank + jitter * 4
    return (height // (8 * thickness) % LAYERS).astype(jnp.int32)


def place_ends(array, key, low, high):
    dims = array.shape
    place = [jax.random.randint(jax.random.fold_in(key, axis), (), 0, dims[axis]) for axis in range(len(dims))]
    array = array.at[tuple(place)].set(low)
    longest = dims.index(max(dims))
    place[longest] = (place[longest] + 1) % dims[longest]
    return array.at[tuple(place)].set(high)


def steps_of(stream_key, dims, shards, least, high):
    loudness = 1.0
    for dim, parts in shards:
        draws = jax.random.uniform(jax.random.fold_in(jax.random.fold_in(stream_key, 6), dim), (parts,), jnp.float32, least / len(shards), high / len(shards))
        loudness = loudness * jnp.repeat(jnp.exp(draws), dims[dim] // parts).reshape((-1,) + (1,) * (len(dims) - 1 - dim))
    return loudness


def setup_inputs(seed: int = 0) -> dict:
    streams_of = jax.random.split(jax.random.key(seed), 10)
    thermal_field = draw_thermal_field(jax.random.fold_in(streams_of[9], 71), 0)
    liquid_fraction = jnp.clip(0.6 * jax.random.uniform(streams_of[1], (NZ, NX, NY), jnp.float32) ** steps_of(streams_of[1], (NZ, NX, NY), ((0, 4), (1, 4), (2, 2)), -0.2, 0.2), 0.0, 0.6)
    steam_content_grid = jnp.clip(1.0 * jax.random.uniform(streams_of[2], (NZ, NX, NY), jnp.float32) ** steps_of(streams_of[2], (NZ, NX, NY), ((0, 4), (1, 4), (2, 2)), -0.2, 0.2), 0.0, 1.0)
    carbonic_gas_grid = jnp.clip(0.5 * jax.random.uniform(streams_of[3], (NZ, NX, NY), jnp.float32) ** steps_of(streams_of[3], (NZ, NX, NY), ((0, 4), (1, 4), (2, 2)), -0.2, 0.2), 0.0, 0.5)
    stratum_number_grid = draw_stratum_number_grid(jax.random.fold_in(streams_of[9], 71), 0)
    injection_flags = place_ends((jax.random.randint(streams_of[5], (NZ, NX, NY), 0, 8) < 1).astype(jnp.int32), jax.random.fold_in(streams_of[5], 1), 0, 1)
    lateral_transmissivity = jnp.clip(jnp.exp(jax.random.uniform(streams_of[6], (2, LAYERS), jnp.float32, math.log(0.02), math.log(0.12))), 0.02, 0.12)
    vertical_transmissivity = jnp.clip(jnp.exp(jax.random.uniform(streams_of[7], (LAYERS,), jnp.float32, math.log(20.0), math.log(2000.0))), 20.0, 2000.0)
    stratum_advection_offsets = jnp.clip(jax.random.uniform(streams_of[8], (2, LAYERS), jnp.float32, -0.45, 0.45), -0.45, 0.45)
    return {"thermal_field": thermal_field, "liquid_fraction": liquid_fraction, "steam_content_grid": steam_content_grid, "carbonic_gas_grid": carbonic_gas_grid, "stratum_number_grid": stratum_number_grid, "injection_flags": injection_flags, "lateral_transmissivity": lateral_transmissivity, "vertical_transmissivity": vertical_transmissivity, "stratum_advection_offsets": stratum_advection_offsets}


SOFTEN = 0.5
HEAT_CARRY = 0.5
SILL_RATE = 0.3
SILL_HEAT = 2.5
WATER_INPUT = 0.2
CARBON_INPUT = 0.1
MELT_SHARPNESS = 4.0
SOLIDUS = 1.0
DEPRESSION = 0.5
MELT_RATE = 0.5
LATENT = 0.3


def lateral_section(padded, coeffs, sill):
    soften = jnp.exp(-SOFTEN * padded[0])
    cond_x = (coeffs[0] * soften)[..., 1:-1]
    cond_y = (coeffs[1] * soften)[..., 1:-1, :]
    drift_x = coeffs[2][..., 1:-1]
    drift_y = coeffs[3][..., 1:-1, :]
    mobile_x = padded[:3, ..., 1:-1]
    mobile_y = padded[:3, ..., 1:-1, :]
    face_cx = 0.5 * (cond_x[..., :-1, :] + cond_x[..., 1:, :])
    face_cy = 0.5 * (cond_y[..., :-1] + cond_y[..., 1:])
    face_vx = 0.5 * (drift_x[..., :-1, :] + drift_x[..., 1:, :])
    face_vy = 0.5 * (drift_y[..., :-1] + drift_y[..., 1:])
    flux_x = face_cx * (mobile_x[0, ..., 1:, :] - mobile_x[0, ..., :-1, :])
    flux_y = face_cy * (mobile_y[0, ..., 1:] - mobile_y[0, ..., :-1])
    diffused = flux_x[..., 1:, :] - flux_x[..., :-1, :] + flux_y[..., 1:] - flux_y[..., :-1]
    carried_x = jnp.maximum(face_vx, 0.0) * mobile_x[..., :-1, :] + jnp.minimum(face_vx, 0.0) * mobile_x[..., 1:, :]
    carried_y = jnp.maximum(face_vy, 0.0) * mobile_y[..., :-1] + jnp.minimum(face_vy, 0.0) * mobile_y[..., 1:]
    inflow = carried_x[..., :-1, :] - carried_x[..., 1:, :] + carried_y[..., :-1] - carried_y[..., 1:]
    inner = padded[..., 1:-1, 1:-1]
    heat_one = inner[0] + diffused + HEAT_CARRY * inflow[0]
    water_two = inner[1] + inflow[1] + sill * WATER_INPUT
    carbon_two = inner[2] + inflow[2] + sill * CARBON_INPUT
    heat_two = heat_one + sill * SILL_RATE * (SILL_HEAT - heat_one)
    target = jax.nn.sigmoid(MELT_SHARPNESS * (heat_two - SOLIDUS + DEPRESSION * water_two))
    melt_two = inner[3] + MELT_RATE * (target - inner[3])
    heat_three = heat_two - LATENT * (melt_two - inner[3])
    return jnp.stack([heat_three, water_two, carbon_two, melt_two])


def column_faces(cond_col):
    roof_boundary_face = jnp.concatenate([cond_col[:1], 0.5 * (cond_col[:-1] + cond_col[1:])], 0)
    floor_boundary_face = jnp.concatenate([roof_boundary_face[1:], jnp.zeros_like(cond_col[:1])], 0)
    return roof_boundary_face, floor_boundary_face


def banded_system_inverter(lower_band, main_band, upper_band, right_side):
    zero_plane = jnp.zeros(right_side.shape[1:], right_side.dtype)

    def forward(carry, row):
        ratio_prev, value_prev = carry
        low_row, main_row, up_row, side_row = row
        pivot = main_row - low_row * ratio_prev
        ratio = up_row / pivot
        value = (side_row - low_row * value_prev) / pivot
        return (ratio, value), (ratio, value)

    unused, (ratios, values) = lax.scan(forward, (zero_plane, zero_plane), (lower_band, main_band, upper_band, right_side))

    def backward(following, row):
        ratio, value = row
        solved = value - ratio * following
        return solved, solved

    unused_last, solution = lax.scan(backward, zero_plane, (ratios, values), reverse=True)
    return solution


def reference(thermal_field, liquid_fraction, steam_content_grid, carbonic_gas_grid, stratum_number_grid, injection_flags, lateral_transmissivity, vertical_transmissivity, stratum_advection_offsets):
    table = jnp.concatenate([lateral_transmissivity, stratum_advection_offsets, vertical_transmissivity[None]], 0)
    widths = ((0, 0), (1, 1), (1, 1))

    def burial_rank(inputs):
        heat, melt, water, carbon, layers, sill_int = inputs
        coeffs = table[:, layers]
        lateral_pad = jnp.pad(coeffs[:4], widths, mode="wrap")
        sill = sill_int.astype(jnp.float32)
        chamber_state = jnp.stack([heat, water, carbon, melt])
        for section_no in range(SECTIONS):
            chamber_state = lateral_section(jnp.pad(chamber_state, widths, mode="wrap"), lateral_pad, sill)
        conduct = coeffs[4] * jnp.exp(-SOFTEN * chamber_state[0])
        return chamber_state[0], chamber_state[3], chamber_state[1], chamber_state[2], conduct

    lateral_thermal_diffusion, liquid_fraction_next, steam_content_next, carbonic_gas_next, conduct = lax.map(
        burial_rank, (thermal_field, liquid_fraction, steam_content_grid, carbonic_gas_grid, stratum_number_grid, injection_flags))
    roof_boundary_face, floor_boundary_face = column_faces(conduct)
    thermal_field_next = banded_system_inverter(-roof_boundary_face, 1.0 + roof_boundary_face + floor_boundary_face, -floor_boundary_face, lateral_thermal_diffusion)
    return thermal_field_next, liquid_fraction_next, steam_content_next, carbonic_gas_next
```

```python
import jax
import jax.numpy as jnp
from jax import lax
from jax.experimental import pallas as pl
from jax.experimental.pallas import tpu as pltpu
from jax.sharding import PartitionSpec as P

SECTIONS = 4


SOFTEN = 0.5
HEAT_CARRY = 0.5
SILL_RATE = 0.3
SILL_HEAT = 2.5
WATER_INPUT = 0.2
CARBON_INPUT = 0.1
MELT_SHARPNESS = 4.0
SOLIDUS = 1.0
DEPRESSION = 0.5
MELT_RATE = 0.5
LATENT = 0.3


def ring_perms(axis):
    count = lax.axis_size(axis)
    forward = [(i, (i + 1) % count) for i in range(count)]
    backward = [((i + 1) % count, i) for i in range(count)]
    return forward, backward


def edges(block, axis, dim):
    forward, backward = ring_perms(axis)
    last = lax.index_in_dim(block, block.shape[dim] - 1, axis=dim, keepdims=False)
    first = lax.index_in_dim(block, 0, axis=dim, keepdims=False)
    low = lax.ppermute(last, axis, forward)
    high = lax.ppermute(first, axis, backward)
    return low, high


def shifted(block, low, high, dim):
    n = block.shape[dim]
    lo = jnp.expand_dims(low, dim)
    hi = jnp.expand_dims(high, dim)
    minus = jnp.concatenate([lo, lax.slice_in_dim(block, 0, n - 1, axis=dim)], axis=dim)
    plus = jnp.concatenate([lax.slice_in_dim(block, 1, n, axis=dim), hi], axis=dim)
    return minus, plus


def lookup(layers, row):
    result = jnp.zeros(layers.shape, jnp.float32)
    for layer_no in range(row.shape[0]):
        result = jnp.where(layers == layer_no, row[layer_no], result)
    return result


def lateral_step(state, coef, halos, sill):
    heat, water, carbon, melt = state
    cx, cx_m, cx_p, cy, cy_m, cy_p, vfx_m, vfx_p, vfy_m, vfy_p = coef
    xs_lo, xs_hi, ys_lo, ys_hi = halos
    mobile = jnp.stack([heat, water, carbon])
    q_xm, q_xp = shifted(mobile, xs_lo, xs_hi, 2)
    q_ym, q_yp = shifted(mobile, ys_lo, ys_hi, 3)
    soft = jnp.exp(-SOFTEN * heat)
    kx = cx * soft
    ky = cy * soft
    kx_m = cx_m * jnp.exp(-SOFTEN * q_xm[0])
    kx_p = cx_p * jnp.exp(-SOFTEN * q_xp[0])
    ky_m = cy_m * jnp.exp(-SOFTEN * q_ym[0])
    ky_p = cy_p * jnp.exp(-SOFTEN * q_yp[0])
    flux_x_lo = 0.5 * (kx_m + kx) * (heat - q_xm[0])
    flux_x_hi = 0.5 * (kx + kx_p) * (q_xp[0] - heat)
    flux_y_lo = 0.5 * (ky_m + ky) * (heat - q_ym[0])
    flux_y_hi = 0.5 * (ky + ky_p) * (q_yp[0] - heat)
    diffused = flux_x_hi - flux_x_lo + flux_y_hi - flux_y_lo
    carried_x_lo = jnp.maximum(vfx_m, 0.0) * q_xm + jnp.minimum(vfx_m, 0.0) * mobile
    carried_x_hi = jnp.maximum(vfx_p, 0.0) * mobile + jnp.minimum(vfx_p, 0.0) * q_xp
    carried_y_lo = jnp.maximum(vfy_m, 0.0) * q_ym + jnp.minimum(vfy_m, 0.0) * mobile
    carried_y_hi = jnp.maximum(vfy_p, 0.0) * mobile + jnp.minimum(vfy_p, 0.0) * q_yp
    inflow = carried_x_lo - carried_x_hi + carried_y_lo - carried_y_hi
    heat_one = heat + diffused + HEAT_CARRY * inflow[0]
    water_two = water + inflow[1] + sill * WATER_INPUT
    carbon_two = carbon + inflow[2] + sill * CARBON_INPUT
    heat_two = heat_one + sill * SILL_RATE * (SILL_HEAT - heat_one)
    target = jax.nn.sigmoid(MELT_SHARPNESS * (heat_two - SOLIDUS + DEPRESSION * water_two))
    melt_two = melt + MELT_RATE * (target - melt)
    heat_three = heat_two - LATENT * (melt_two - melt)
    return heat_three, water_two, carbon_two, melt_two


def sweep_kernel(r_ref, c_ref, y_ref, a_ref, b_ref, red_ref, g_s, vy_s, va_s):
    n = r_ref.shape[0]
    zero = jnp.zeros(r_ref.shape[1:], jnp.float32)
    one = jnp.ones(r_ref.shape[1:], jnp.float32)

    def forward(i, carry):
        g_prev, vy_prev, va_prev = carry
        up = 0.5 * (c_ref[i - 1] + c_ref[i])
        down = 0.5 * (c_ref[i] + c_ref[i + 1])
        inv = 1.0 / (1.0 + up + down - up * g_prev)
        g = down * inv
        vy = (r_ref[i] + up * vy_prev) * inv
        va = (up * va_prev) * inv
        g_s[i] = g
        vy_s[i] = vy
        va_s[i] = va
        return g, vy, va

    lax.fori_loop(1, n - 1, forward, (zero, zero, one))

    def backward(k, carry):
        i = n - 2 - k
        y_next, a_next, b_next = carry
        g = g_s[i]
        y = vy_s[i] + g * y_next
        a = va_s[i] + g * a_next
        b = g * b_next
        y_ref[i] = y
        a_ref[i] = a
        b_ref[i] = b
        return y, a, b

    lax.fori_loop(0, n - 2, backward, (zero, zero, one))
    y_ref[0] = zero
    a_ref[0] = one
    b_ref[0] = zero
    y_ref[n - 1] = zero
    a_ref[n - 1] = zero
    b_ref[n - 1] = one
    up_first = 0.5 * (c_ref[0] + c_ref[1])
    up_last = 0.5 * (c_ref[n - 2] + c_ref[n - 1])
    red_ref[0] = 1.0 + up_first * (1.0 - a_ref[1])
    red_ref[1] = up_first * b_ref[1]
    red_ref[2] = r_ref[0] + up_first * y_ref[1]
    red_ref[3] = 1.0 + up_last * (1.0 - b_ref[n - 2])
    red_ref[4] = up_last * a_ref[n - 2]
    red_ref[5] = r_ref[n - 1] + up_last * y_ref[n - 2]
    red_ref[6] = c_ref[0]
    red_ref[7] = c_ref[n - 1]


def local_sweep(heat, cond):
    shape = heat.shape
    plane = shape[1:]
    out_shape = (
        jax.ShapeDtypeStruct(shape, jnp.float32),
        jax.ShapeDtypeStruct(shape, jnp.float32),
        jax.ShapeDtypeStruct(shape, jnp.float32),
        jax.ShapeDtypeStruct((8,) + plane, jnp.float32),
    )
    return pl.pallas_call(
        sweep_kernel,
        out_shape=out_shape,
        scratch_shapes=[pltpu.VMEM(shape, jnp.float32)] * 3,
    )(heat, cond)


def reduced_solve(red_all):
    count = red_all.shape[0]
    lower, diag, upper, side = [], [], [], []
    for j in range(count):
        p0, q0, s0, p1, q1, s1, c_first, c_last = [red_all[j, k] for k in range(8)]
        if j == 0:
            face = c_first
            lower.append(jnp.zeros_like(face))
        else:
            face = 0.5 * (red_all[j - 1, 7] + c_first)
            lower.append(face)
        diag.append(p0 + face)
        upper.append(q0)
        side.append(s0)
        if j + 1 < count:
            below = 0.5 * (c_last + red_all[j + 1, 6])
        else:
            below = jnp.zeros_like(c_last)
        lower.append(q1)
        diag.append(p1 + below)
        upper.append(below)
        side.append(s1)
    size = len(diag)
    ratios, values = [], []
    g_prev = jnp.zeros_like(diag[0])
    v_prev = jnp.zeros_like(diag[0])
    for k in range(size):
        inv = 1.0 / (diag[k] - lower[k] * g_prev)
        g_prev = upper[k] * inv
        v_prev = (side[k] + lower[k] * v_prev) * inv
        ratios.append(g_prev)
        values.append(v_prev)
    solved = [None] * size
    following = jnp.zeros_like(diag[0])
    for k in reversed(range(size)):
        following = values[k] + ratios[k] * following
        solved[k] = following
    return jnp.stack(solved)


def local(
    thermal_field,
    liquid_fraction,
    steam_content_grid,
    carbonic_gas_grid,
    stratum_number_grid,
    injection_flags,
    lateral_transmissivity,
    vertical_transmissivity,
    stratum_advection_offsets,
):
    sill = injection_flags.astype(jnp.float32)
    layers = stratum_number_grid
    lx_lo, lx_hi = edges(layers, "east", 1)
    ly_lo, ly_hi = edges(layers, "north", 2)

    def coef_pair(table_row, dim, low, high):
        own = lookup(layers, table_row)
        minus, plus = shifted(own, lookup(low, table_row), lookup(high, table_row), dim)
        return own, minus, plus

    cx, cx_m, cx_p = coef_pair(lateral_transmissivity[0], 1, lx_lo, lx_hi)
    cy, cy_m, cy_p = coef_pair(lateral_transmissivity[1], 2, ly_lo, ly_hi)
    vx, vx_m, vx_p = coef_pair(stratum_advection_offsets[0], 1, lx_lo, lx_hi)
    vy, vy_m, vy_p = coef_pair(stratum_advection_offsets[1], 2, ly_lo, ly_hi)
    coef = (
        cx, cx_m, cx_p, cy, cy_m, cy_p,
        0.5 * (vx_m + vx), 0.5 * (vx + vx_p), 0.5 * (vy_m + vy), 0.5 * (vy + vy_p),
    )
    cz = lookup(layers, vertical_transmissivity)

    state = (thermal_field, steam_content_grid, carbonic_gas_grid, liquid_fraction)
    for section_no in range(SECTIONS):
        mobile = jnp.stack(state[:3])
        xs_lo, xs_hi = edges(mobile, "east", 2)
        ys_lo, ys_hi = edges(mobile, "north", 3)
        state = lateral_step(state, coef, (xs_lo, xs_hi, ys_lo, ys_hi), sill)
    heat = state[0]
    cond = cz * jnp.exp(-SOFTEN * heat)

    y, a, b, red = local_sweep(heat, cond)
    red_all = lax.all_gather(red, "depth")
    solved = reduced_solve(red_all)
    rank = lax.axis_index("depth")
    first = lax.dynamic_index_in_dim(solved, 2 * rank, keepdims=False)
    last = lax.dynamic_index_in_dim(solved, 2 * rank + 1, keepdims=False)
    heat_next = y + a * first[None] + b * last[None]
    return (heat_next, state[3], state[1], state[2])


def solution(mesh):
    placed = (
        P("depth", "east", "north"),
        P("depth", "east", "north"),
        P("depth", "east", "north"),
        P("depth", "east", "north"),
        P("depth", "east", "north"),
        P("depth", "east", "north"),
        P(),
        P(),
        P(),
    )
    return jax.shard_map(
        local,
        mesh=mesh,
        in_specs=placed,
        out_specs=(
            P("depth", "east", "north"),
            P("depth", "east", "north"),
            P("depth", "east", "north"),
            P("depth", "east", "north"),
        ),
        check_vma=False,
    )
```

```python
import jax
import jax.numpy as jnp
from jax import lax
from jax.experimental import pallas as pl
from jax.experimental.pallas import tpu as pltpu
from jax.sharding import PartitionSpec as P

SECTIONS = 4


SOFTEN = 0.5
HEAT_CARRY = 0.5
SILL_RATE = 0.3
SILL_HEAT = 2.5
WATER_INPUT = 0.2
CARBON_INPUT = 0.1
MELT_SHARPNESS = 4.0
SOLIDUS = 1.0
DEPRESSION = 0.5
MELT_RATE = 0.5
LATENT = 0.3

ROWS = 8
LANES = 128
f32 = jnp.float32


def ring_perms(axis):
    count = lax.axis_size(axis)
    forward = [(i, (i + 1) % count) for i in range(count)]
    backward = [((i + 1) % count, i) for i in range(count)]
    return forward, backward


def iotas():
    sub = lax.broadcasted_iota(jnp.int32, (ROWS, LANES), 0)
    lane = lax.broadcasted_iota(jnp.int32, (ROWS, LANES), 1)
    return sub, lane


class EdgeAcc:
    def __init__(self, count, y_first, y_last):
        zero = jnp.zeros((ROWS, LANES), f32)
        self.xf = [zero] * count
        self.xl = [zero] * count
        self.yf = list(y_first)
        self.yl = list(y_last)

    def add(self, planes, b, d, sub, lane):
        at_b = sub == b
        at_d = lane == d
        for f, v in enumerate(planes):
            self.xf[f] = jnp.where(at_b, pltpu.roll(v, b, 0), self.xf[f])
            self.xl[f] = jnp.where(at_b, pltpu.roll(v, (b + 1) % ROWS, 0), self.xl[f])
            self.yf[f] = jnp.where(at_d, pltpu.roll(v, d % LANES, 1), self.yf[f])
            self.yl[f] = jnp.where(at_d, pltpu.roll(v, (d + 1) % LANES, 1), self.yl[f])


def x_minus(v, lo_tile, b, sub):
    return jnp.where(sub == 0, pltpu.roll(lo_tile, (ROWS - b) % ROWS, 0), pltpu.roll(v, 1, 0))


def x_plus(v, hi_tile, b, sub):
    return jnp.where(
        sub == ROWS - 1, pltpu.roll(hi_tile, (ROWS - 1 - b) % ROWS, 0), pltpu.roll(v, ROWS - 1, 0)
    )


def y_minus(v, lo_cols, d, lane):
    return jnp.where(lane == 0, pltpu.roll(lo_cols, (LANES - d) % LANES, 1), pltpu.roll(v, 1, 1))


def y_plus(v, hi_cols, d, lane):
    return jnp.where(
        lane == LANES - 1,
        pltpu.roll(hi_cols, (LANES - 1 - d) % LANES, 1),
        pltpu.roll(v, LANES - 1, 1),
    )


def prep_kernel(tab_ref, layer_ref, h_ref, w_ref, c_ref,
                co_ref, sxf_ref, sxl_ref, syf_ref, syl_ref, cxf_ref, cxl_ref, cyf_ref, cyl_ref):
    groups = layer_ref.shape[0] // ROWS
    layers_count = tab_ref.shape[1]
    sub, lane = iotas()
    zero = jnp.zeros((ROWS, LANES), f32)

    def group(a, carry):
        sy_f, sy_l, cy_f, cy_l = carry
        s_acc = EdgeAcc(3, sy_f, sy_l)
        cx_acc = EdgeAcc(2, [zero, zero], [zero, zero])
        cy_acc = EdgeAcc(2, cy_f, cy_l)
        for b in range(ROWS):
            d = a * ROWS + b
            layer = layer_ref[d]
            vals = [zero] * 5
            for l in range(layers_count):
                hit = layer == l
                vals = [jnp.where(hit, tab_ref[k, l], vals[k]) for k in range(5)]
            for k in range(5):
                co_ref[k, d] = vals[k]
            s_acc.add([h_ref[d], w_ref[d], c_ref[d]], b, d, sub, lane)
            cx_acc.add([vals[0], vals[2]], b, d, sub, lane)
            cy_acc.add([vals[1], vals[3]], b, d, sub, lane)
        for f in range(3):
            sxf_ref[f, a] = s_acc.xf[f]
            sxl_ref[f, a] = s_acc.xl[f]
        for f in range(2):
            cxf_ref[f, a] = cx_acc.xf[f]
            cxl_ref[f, a] = cx_acc.xl[f]
        return (tuple(s_acc.yf), tuple(s_acc.yl), tuple(cy_acc.yf), tuple(cy_acc.yl))

    init = ((zero,) * 3, (zero,) * 3, (zero,) * 2, (zero,) * 2)
    sy_f, sy_l, cy_f, cy_l = lax.fori_loop(0, groups, group, init)
    for f in range(3):
        syf_ref[f] = sy_f[f]
        syl_ref[f] = sy_l[f]
    for f in range(2):
        cyf_ref[f] = cy_f[f]
        cyl_ref[f] = cy_l[f]


def section_kernel(h_ref, w_ref, c_ref, m_ref, sill_ref, co_ref,
                   sxlo_ref, sxhi_ref, sylo_ref, syhi_ref, cxlo_ref, cxhi_ref, cylo_ref, cyhi_ref,
                   ho_ref, wo_ref, co_out_ref, mo_ref, sxf_ref, sxl_ref, syf_ref, syl_ref):
    groups = h_ref.shape[0] // ROWS
    sub, lane = iotas()
    zero = jnp.zeros((ROWS, LANES), f32)
    sylo = [sylo_ref[f] for f in range(3)]
    syhi = [syhi_ref[f] for f in range(3)]
    cylo = [cylo_ref[f] for f in range(2)]
    cyhi = [cyhi_ref[f] for f in range(2)]

    def group(a, carry):
        y_f, y_l = carry
        acc = EdgeAcc(3, y_f, y_l)
        sxlo = [sxlo_ref[f, a] for f in range(3)]
        sxhi = [sxhi_ref[f, a] for f in range(3)]
        cxlo = [cxlo_ref[f, a] for f in range(2)]
        cxhi = [cxhi_ref[f, a] for f in range(2)]
        for b in range(ROWS):
            d = a * ROWS + b
            heat = h_ref[d]
            water = w_ref[d]
            carbon = c_ref[d]
            melt = m_ref[d]
            sill = sill_ref[d].astype(f32)
            cx = co_ref[0, d]
            cy = co_ref[1, d]
            vx = co_ref[2, d]
            vy = co_ref[3, d]
            mobile = [heat, water, carbon]
            q_xm = [x_minus(mobile[f], sxlo[f], b, sub) for f in range(3)]
            q_xp = [x_plus(mobile[f], sxhi[f], b, sub) for f in range(3)]
            q_ym = [y_minus(mobile[f], sylo[f], d, lane) for f in range(3)]
            q_yp = [y_plus(mobile[f], syhi[f], d, lane) for f in range(3)]
            cx_m = x_minus(cx, cxlo[0], b, sub)
            cx_p = x_plus(cx, cxhi[0], b, sub)
            vx_m = x_minus(vx, cxlo[1], b, sub)
            vx_p = x_plus(vx, cxhi[1], b, sub)
            cy_m = y_minus(cy, cylo[0], d, lane)
            cy_p = y_plus(cy, cyhi[0], d, lane)
            vy_m = y_minus(vy, cylo[1], d, lane)
            vy_p = y_plus(vy, cyhi[1], d, lane)
            soft = jnp.exp(-SOFTEN * heat)
            kx = cx * soft
            ky = cy * soft
            kx_m = cx_m * jnp.exp(-SOFTEN * q_xm[0])
            kx_p = cx_p * jnp.exp(-SOFTEN * q_xp[0])
            ky_m = cy_m * jnp.exp(-SOFTEN * q_ym[0])
            ky_p = cy_p * jnp.exp(-SOFTEN * q_yp[0])
            flux_x_lo = 0.5 * (kx_m + kx) * (heat - q_xm[0])
            flux_x_hi = 0.5 * (kx + kx_p) * (q_xp[0] - heat)
            flux_y_lo = 0.5 * (ky_m + ky) * (heat - q_ym[0])
            flux_y_hi = 0.5 * (ky + ky_p) * (q_yp[0] - heat)
            diffused = flux_x_hi - flux_x_lo + flux_y_hi - flux_y_lo
            fvx_m = 0.5 * (vx_m + vx)
            fvx_p = 0.5 * (vx + vx_p)
            fvy_m = 0.5 * (vy_m + vy)
            fvy_p = 0.5 * (vy + vy_p)
            inflow = []
            for f in range(3):
                lo_x = jnp.maximum(fvx_m, 0.0) * q_xm[f] + jnp.minimum(fvx_m, 0.0) * mobile[f]
                hi_x = jnp.maximum(fvx_p, 0.0) * mobile[f] + jnp.minimum(fvx_p, 0.0) * q_xp[f]
                lo_y = jnp.maximum(fvy_m, 0.0) * q_ym[f] + jnp.minimum(fvy_m, 0.0) * mobile[f]
                hi_y = jnp.maximum(fvy_p, 0.0) * mobile[f] + jnp.minimum(fvy_p, 0.0) * q_yp[f]
                inflow.append(lo_x - hi_x + lo_y - hi_y)
            heat_one = heat + diffused + HEAT_CARRY * inflow[0]
            water_two = water + inflow[1] + sill * WATER_INPUT
            carbon_two = carbon + inflow[2] + sill * CARBON_INPUT
            heat_two = heat_one + sill * SILL_RATE * (SILL_HEAT - heat_one)
            z = MELT_SHARPNESS * (heat_two - SOLIDUS + DEPRESSION * water_two)
            target = 1.0 / (1.0 + jnp.exp(-z))
            melt_two = melt + MELT_RATE * (target - melt)
            heat_three = heat_two - LATENT * (melt_two - melt)
            ho_ref[d] = heat_three
            wo_ref[d] = water_two
            co_out_ref[d] = carbon_two
            mo_ref[d] = melt_two
            acc.add([heat_three, water_two, carbon_two], b, d, sub, lane)
        for f in range(3):
            sxf_ref[f, a] = acc.xf[f]
            sxl_ref[f, a] = acc.xl[f]
        return (tuple(acc.yf), tuple(acc.yl))

    y_f, y_l = lax.fori_loop(0, groups, group, ((zero,) * 3, (zero,) * 3))
    for f in range(3):
        syf_ref[f] = y_f[f]
        syl_ref[f] = y_l[f]


def sweep_kernel(r_ref, cz_ref, y_ref, a_ref, b_ref, red_ref, c_s, g_s, vy_s, va_s):
    n = r_ref.shape[0]
    zero = jnp.zeros(r_ref.shape[1:], f32)
    one = jnp.ones(r_ref.shape[1:], f32)

    def conduct(i, carry):
        c_s[i] = cz_ref[i] * jnp.exp(-SOFTEN * r_ref[i])
        return carry

    lax.fori_loop(0, n, conduct, 0)

    def forward(i, carry):
        g_prev, vy_prev, va_prev = carry
        up = 0.5 * (c_s[i - 1] + c_s[i])
        down = 0.5 * (c_s[i] + c_s[i + 1])
        inv = 1.0 / (1.0 + up + down - up * g_prev)
        g = down * inv
        vy = (r_ref[i] + up * vy_prev) * inv
        va = (up * va_prev) * inv
        g_s[i] = g
        vy_s[i] = vy
        va_s[i] = va
        return g, vy, va

    lax.fori_loop(1, n - 1, forward, (zero, zero, one))

    def backward(k, carry):
        i = n - 2 - k
        y_next, a_next, b_next = carry
        g = g_s[i]
        y = vy_s[i] + g * y_next
        a = va_s[i] + g * a_next
        b = g * b_next
        y_ref[i] = y
        a_ref[i] = a
        b_ref[i] = b
        return y, a, b

    lax.fori_loop(0, n - 2, backward, (zero, zero, one))
    y_ref[0] = zero
    a_ref[0] = one
    b_ref[0] = zero
    y_ref[n - 1] = zero
    a_ref[n - 1] = zero
    b_ref[n - 1] = one
    up_first = 0.5 * (c_s[0] + c_s[1])
    up_last = 0.5 * (c_s[n - 2] + c_s[n - 1])
    red_ref[0] = 1.0 + up_first * (1.0 - a_ref[1])
    red_ref[1] = up_first * b_ref[1]
    red_ref[2] = r_ref[0] + up_first * y_ref[1]
    red_ref[3] = 1.0 + up_last * (1.0 - b_ref[n - 2])
    red_ref[4] = up_last * a_ref[n - 2]
    red_ref[5] = r_ref[n - 1] + up_last * y_ref[n - 2]
    red_ref[6] = c_s[0]
    red_ref[7] = c_s[n - 1]


def reduced_solve(red_all):
    count = red_all.shape[0]
    lower, diag, upper, side = [], [], [], []
    for j in range(count):
        p0, q0, s0, p1, q1, s1, c_first, c_last = [red_all[j, k] for k in range(8)]
        if j == 0:
            face = c_first
            lower.append(jnp.zeros_like(face))
        else:
            face = 0.5 * (red_all[j - 1, 7] + c_first)
            lower.append(face)
        diag.append(p0 + face)
        upper.append(q0)
        side.append(s0)
        if j + 1 < count:
            below = 0.5 * (c_last + red_all[j + 1, 6])
        else:
            below = jnp.zeros_like(c_last)
        lower.append(q1)
        diag.append(p1 + below)
        upper.append(below)
        side.append(s1)
    size = len(diag)
    ratios, values = [], []
    g_prev = jnp.zeros_like(diag[0])
    v_prev = jnp.zeros_like(diag[0])
    for k in range(size):
        inv = 1.0 / (diag[k] - lower[k] * g_prev)
        g_prev = upper[k] * inv
        v_prev = (side[k] + lower[k] * v_prev) * inv
        ratios.append(g_prev)
        values.append(v_prev)
    solved = [None] * size
    following = jnp.zeros_like(diag[0])
    for k in reversed(range(size)):
        following = values[k] + ratios[k] * following
        solved[k] = following
    return jnp.stack(solved)


def sds(shape):
    return jax.ShapeDtypeStruct(shape, f32)


def exchange(xf, xl, yf, yl):
    east_fwd, east_bwd = ring_perms("east")
    north_fwd, north_bwd = ring_perms("north")
    xlo = lax.ppermute(xl, "east", east_fwd)
    xhi = lax.ppermute(xf, "east", east_bwd)
    ylo = lax.ppermute(yl, "north", north_fwd)
    yhi = lax.ppermute(yf, "north", north_bwd)
    return xlo, xhi, ylo, yhi


def local(
    thermal_field,
    liquid_fraction,
    steam_content_grid,
    carbonic_gas_grid,
    stratum_number_grid,
    injection_flags,
    lateral_transmissivity,
    vertical_transmissivity,
    stratum_advection_offsets,
):
    shape = thermal_field.shape
    n = shape[0]
    groups = n // ROWS
    assert shape[1:] == (ROWS, LANES) and n % ROWS == 0 and n <= LANES
    table = jnp.concatenate(
        [lateral_transmissivity, stratum_advection_offsets, vertical_transmissivity[None]], 0
    )
    vmem = pltpu.MemorySpace.VMEM
    smem_spec = pl.BlockSpec(memory_space=pltpu.SMEM)
    vspec = pl.BlockSpec(memory_space=vmem)
    xs3 = sds((3, groups, ROWS, LANES))
    ys3 = sds((3, ROWS, LANES))
    xs2 = sds((2, groups, ROWS, LANES))
    ys2 = sds((2, ROWS, LANES))
    co, sxf, sxl, syf, syl, cxf, cxl, cyf, cyl = pl.pallas_call(
        prep_kernel,
        out_shape=(sds((5,) + shape), xs3, xs3, ys3, ys3, xs2, xs2, ys2, ys2),
        in_specs=[smem_spec, vspec, vspec, vspec, vspec],
    )(table, stratum_number_grid, thermal_field, steam_content_grid, carbonic_gas_grid)
    cxlo, cxhi, cylo, cyhi = exchange(cxf, cxl, cyf, cyl)

    heat, water, carbon, melt = thermal_field, steam_content_grid, carbonic_gas_grid, liquid_fraction
    for section_no in range(SECTIONS):
        sxlo, sxhi, sylo, syhi = exchange(sxf, sxl, syf, syl)
        heat, water, carbon, melt, sxf, sxl, syf, syl = pl.pallas_call(
            section_kernel,
            out_shape=(sds(shape), sds(shape), sds(shape), sds(shape), xs3, xs3, ys3, ys3),
        )(heat, water, carbon, melt, injection_flags, co,
          sxlo, sxhi, sylo, syhi, cxlo, cxhi, cylo, cyhi)

    y, a, b, red = pl.pallas_call(
        sweep_kernel,
        out_shape=(sds(shape), sds(shape), sds(shape), sds((8,) + shape[1:])),
        scratch_shapes=[pltpu.VMEM(shape, f32)] * 4,
    )(heat, co[4])
    count = lax.axis_size("depth")
    rank = lax.axis_index("depth")
    received = [red]
    for k in range(1, count):
        received.append(lax.ppermute(red, "depth", [(i, (i + k) % count) for i in range(count)]))
    stacked = jnp.stack(received)
    red_all = jnp.take(stacked, (rank - jnp.arange(count)) % count, axis=0)
    solved = reduced_solve(red_all)
    first = lax.dynamic_index_in_dim(solved, 2 * rank, keepdims=False)
    last = lax.dynamic_index_in_dim(solved, 2 * rank + 1, keepdims=False)
    heat_next = y + a * first[None] + b * last[None]
    return (heat_next, melt, water, carbon)


def solution(mesh):
    placed = (
        P("depth", "east", "north"),
        P("depth", "east", "north"),
        P("depth", "east", "north"),
        P("depth", "east", "north"),
        P("depth", "east", "north"),
        P("depth", "east", "north"),
        P(),
        P(),
        P(),
    )
    return jax.shard_map(
        local,
        mesh=mesh,
        in_specs=placed,
        out_specs=(
            P("depth", "east", "north"),
            P("depth", "east", "north"),
            P("depth", "east", "north"),
            P("depth", "east", "north"),
        ),
        check_vma=False,
    )
```

```python
import jax
import jax.numpy as jnp
from jax import lax
from jax.experimental import pallas as pl
from jax.experimental.pallas import tpu as pltpu
from jax.sharding import PartitionSpec as P

SECTIONS = 4


SOFTEN = 0.5
HEAT_CARRY = 0.5
SILL_RATE = 0.3
SILL_HEAT = 2.5
WATER_INPUT = 0.2
CARBON_INPUT = 0.1
MELT_SHARPNESS = 4.0
SOLIDUS = 1.0
DEPRESSION = 0.5
MELT_RATE = 0.5
LATENT = 0.3

ROWS = 8
CHUNKS = 2
LANES = 128
f32 = jnp.float32


def ring_perms(axis):
    count = lax.axis_size(axis)
    forward = [(i, (i + 1) % count) for i in range(count)]
    backward = [((i + 1) % count, i) for i in range(count)]
    return forward, backward


def iotas():
    sub = lax.broadcasted_iota(jnp.int32, (ROWS, LANES), 0)
    lane = lax.broadcasted_iota(jnp.int32, (ROWS, LANES), 1)
    return sub, lane


class EdgeAcc:
    def __init__(self, count, y_first, y_last):
        zero = jnp.zeros((ROWS, LANES), f32)
        self.xf = [zero] * count
        self.xl = [zero] * count
        self.yf = list(y_first)
        self.yl = list(y_last)

    def add_x(self, planes, b):
        at_b = lax.broadcasted_iota(jnp.int32, (ROWS, LANES), 0) == b
        for f, v in enumerate(planes):
            self.xf[f] = jnp.where(at_b, pltpu.roll(v, b, 0), self.xf[f])
            self.xl[f] = jnp.where(at_b, pltpu.roll(v, (b + 1) % ROWS, 0), self.xl[f])

    def add_y(self, planes, d, lane):
        at_d = lane == d
        for f, v in enumerate(planes):
            self.yf[f] = jnp.where(at_d, pltpu.roll(v, d % LANES, 1), self.yf[f])
            self.yl[f] = jnp.where(at_d, pltpu.roll(v, (d + 1) % LANES, 1), self.yl[f])


def x_minus(v, lo_tile, b, sub):
    return jnp.where(sub == 0, pltpu.roll(lo_tile, (ROWS - b) % ROWS, 0), pltpu.roll(v, 1, 0))


def x_plus(v, hi_tile, b, sub):
    return jnp.where(
        sub == ROWS - 1, pltpu.roll(hi_tile, (ROWS - 1 - b) % ROWS, 0), pltpu.roll(v, ROWS - 1, 0)
    )


def y_minus(v, lo_cols, d, lane):
    return jnp.where(lane == 0, pltpu.roll(lo_cols, (LANES - d) % LANES, 1), pltpu.roll(v, 1, 1))


def y_plus(v, hi_cols, d, lane):
    return jnp.where(
        lane == LANES - 1,
        pltpu.roll(hi_cols, (LANES - 1 - d) % LANES, 1),
        pltpu.roll(v, LANES - 1, 1),
    )


def prep_kernel(tab_ref, layer_ref, h_ref, w_ref, c_ref, m_ref,
                ho_ref, wo_ref, cbo_ref, mo_ref, co_ref, xf_ref, xl_ref, y_ref):
    groups = layer_ref.shape[0] // ROWS
    layers_count = tab_ref.shape[1]
    sub, lane = iotas()
    zero = jnp.zeros((ROWS, LANES), f32)

    def group(a, carry):
        y_f, y_l = carry
        acc = EdgeAcc(5, y_f, y_l)
        for b in range(ROWS):
            d = a * ROWS + b
            layer = layer_ref[d]
            vals = [zero] * 5
            for l in range(layers_count):
                hit = layer == l
                vals = [jnp.where(hit, tab_ref[k, l], vals[k]) for k in range(5)]
            for k in range(5):
                co_ref[k, d] = vals[k]
            heat, water, carbon = h_ref[d], w_ref[d], c_ref[d]
            ho_ref[d] = heat
            wo_ref[d] = water
            cbo_ref[d] = carbon
            mo_ref[d] = m_ref[d]
            acc.add_x([heat, water, carbon, vals[0], vals[2]], b)
            acc.add_y([heat, water, carbon, vals[1], vals[3]], d, lane)
        for f in range(5):
            xf_ref[f, a] = acc.xf[f]
            xl_ref[f, a] = acc.xl[f]
        return (tuple(acc.yf), tuple(acc.yl))

    y_f, y_l = lax.fori_loop(0, groups, group, ((zero,) * 5, (zero,) * 5))
    for f in range(5):
        y_ref[0, f] = y_f[f]
        y_ref[1, f] = y_l[f]


def make_section_kernel(chunk, first):
    def kernel(h_ref, w_ref, c_ref, m_ref, sill_ref, co_ref, xflo_ref, xfhi_ref, yflo_ref, yfhi_ref,
               *rest):
        if first:
            ho_ref, wo_ref, cbo_ref, mo_ref, xf_ref, xl_ref, y_ref = rest
            xslo_ref, xshi_ref, yslo_ref, yshi_ref = xflo_ref, xfhi_ref, yflo_ref, yfhi_ref
        else:
            xslo_ref, xshi_ref, yslo_ref, yshi_ref = rest[:4]
            ho_ref, wo_ref, cbo_ref, mo_ref, xf_ref, xl_ref, y_ref = rest[4:]
        depth = h_ref.shape[0]
        groups = depth // ROWS
        sub, lane = iotas()
        zero = jnp.zeros((ROWS, LANES), f32)
        sylo = [yslo_ref[1, f] for f in range(3)]
        syhi = [yshi_ref[0, f] for f in range(3)]
        cylo = [yflo_ref[1, f] for f in (3, 4)]
        cyhi = [yfhi_ref[0, f] for f in (3, 4)]

        def group(a, carry):
            y_f, y_l = carry
            acc = EdgeAcc(3, y_f, y_l)
            sxlo = [xslo_ref[f, a] for f in range(3)]
            sxhi = [xshi_ref[f, a] for f in range(3)]
            cxlo = [xflo_ref[f, a] for f in (3, 4)]
            cxhi = [xfhi_ref[f, a] for f in (3, 4)]
            for b in range(ROWS):
                i = a * ROWS + b
                d = chunk * depth + i
                heat = h_ref[i]
                water = w_ref[i]
                carbon = c_ref[i]
                melt = m_ref[i]
                sill = sill_ref[i].astype(f32)
                cx = co_ref[0, i]
                cy = co_ref[1, i]
                vx = co_ref[2, i]
                vy = co_ref[3, i]
                mobile = [heat, water, carbon]
                q_xm = [x_minus(mobile[f], sxlo[f], b, sub) for f in range(3)]
                q_xp = [x_plus(mobile[f], sxhi[f], b, sub) for f in range(3)]
                q_ym = [y_minus(mobile[f], sylo[f], d, lane) for f in range(3)]
                q_yp = [y_plus(mobile[f], syhi[f], d, lane) for f in range(3)]
                cx_m = x_minus(cx, cxlo[0], b, sub)
                cx_p = x_plus(cx, cxhi[0], b, sub)
                vx_m = x_minus(vx, cxlo[1], b, sub)
                vx_p = x_plus(vx, cxhi[1], b, sub)
                cy_m = y_minus(cy, cylo[0], d, lane)
                cy_p = y_plus(cy, cyhi[0], d, lane)
                vy_m = y_minus(vy, cylo[1], d, lane)
                vy_p = y_plus(vy, cyhi[1], d, lane)
                soft = jnp.exp(-SOFTEN * heat)
                kx = cx * soft
                ky = cy * soft
                kx_m = cx_m * jnp.exp(-SOFTEN * q_xm[0])
                kx_p = cx_p * jnp.exp(-SOFTEN * q_xp[0])
                ky_m = cy_m * jnp.exp(-SOFTEN * q_ym[0])
                ky_p = cy_p * jnp.exp(-SOFTEN * q_yp[0])
                flux_x_lo = 0.5 * (kx_m + kx) * (heat - q_xm[0])
                flux_x_hi = 0.5 * (kx + kx_p) * (q_xp[0] - heat)
                flux_y_lo = 0.5 * (ky_m + ky) * (heat - q_ym[0])
                flux_y_hi = 0.5 * (ky + ky_p) * (q_yp[0] - heat)
                diffused = flux_x_hi - flux_x_lo + flux_y_hi - flux_y_lo
                fvx_m = 0.5 * (vx_m + vx)
                fvx_p = 0.5 * (vx + vx_p)
                fvy_m = 0.5 * (vy_m + vy)
                fvy_p = 0.5 * (vy + vy_p)
                inflow = []
                for f in range(3):
                    lo_x = jnp.maximum(fvx_m, 0.0) * q_xm[f] + jnp.minimum(fvx_m, 0.0) * mobile[f]
                    hi_x = jnp.maximum(fvx_p, 0.0) * mobile[f] + jnp.minimum(fvx_p, 0.0) * q_xp[f]
                    lo_y = jnp.maximum(fvy_m, 0.0) * q_ym[f] + jnp.minimum(fvy_m, 0.0) * mobile[f]
                    hi_y = jnp.maximum(fvy_p, 0.0) * mobile[f] + jnp.minimum(fvy_p, 0.0) * q_yp[f]
                    inflow.append(lo_x - hi_x + lo_y - hi_y)
                heat_one = heat + diffused + HEAT_CARRY * inflow[0]
                water_two = water + inflow[1] + sill * WATER_INPUT
                carbon_two = carbon + inflow[2] + sill * CARBON_INPUT
                heat_two = heat_one + sill * SILL_RATE * (SILL_HEAT - heat_one)
                z = MELT_SHARPNESS * (heat_two - SOLIDUS + DEPRESSION * water_two)
                target = 1.0 / (1.0 + jnp.exp(-z))
                melt_two = melt + MELT_RATE * (target - melt)
                heat_three = heat_two - LATENT * (melt_two - melt)
                ho_ref[i] = heat_three
                wo_ref[i] = water_two
                cbo_ref[i] = carbon_two
                mo_ref[i] = melt_two
                acc.add_x([heat_three, water_two, carbon_two], b)
                acc.add_y([heat_three, water_two, carbon_two], d, lane)
            for f in range(3):
                xf_ref[f, a] = acc.xf[f]
                xl_ref[f, a] = acc.xl[f]
            return (tuple(acc.yf), tuple(acc.yl))

        y_f, y_l = lax.fori_loop(0, groups, group, ((zero,) * 3, (zero,) * 3))
        for f in range(3):
            y_ref[0, f] = y_f[f]
            y_ref[1, f] = y_l[f]

    return kernel


def sweep_kernel(r_ref, cz_ref, y_ref, a_ref, b_ref, red_ref, c_s, g_s, vy_s, va_s):
    n = r_ref.shape[0]
    zero = jnp.zeros(r_ref.shape[1:], f32)
    one = jnp.ones(r_ref.shape[1:], f32)

    def conduct(i, carry):
        c_s[i] = cz_ref[0, i] * jnp.exp(-SOFTEN * r_ref[i])
        return carry

    lax.fori_loop(0, n, conduct, 0)

    def forward(i, carry):
        g_prev, vy_prev, va_prev = carry
        up = 0.5 * (c_s[i - 1] + c_s[i])
        down = 0.5 * (c_s[i] + c_s[i + 1])
        inv = 1.0 / (1.0 + up + down - up * g_prev)
        g = down * inv
        vy = (r_ref[i] + up * vy_prev) * inv
        va = (up * va_prev) * inv
        g_s[i] = g
        vy_s[i] = vy
        va_s[i] = va
        return g, vy, va

    lax.fori_loop(1, n - 1, forward, (zero, zero, one))

    def backward(k, carry):
        i = n - 2 - k
        y_next, a_next, b_next = carry
        g = g_s[i]
        y = vy_s[i] + g * y_next
        a = va_s[i] + g * a_next
        b = g * b_next
        y_ref[i] = y
        a_ref[i] = a
        b_ref[i] = b
        return y, a, b

    lax.fori_loop(0, n - 2, backward, (zero, zero, one))
    y_ref[0] = zero
    a_ref[0] = one
    b_ref[0] = zero
    y_ref[n - 1] = zero
    a_ref[n - 1] = zero
    b_ref[n - 1] = one
    up_first = 0.5 * (c_s[0] + c_s[1])
    up_last = 0.5 * (c_s[n - 2] + c_s[n - 1])
    red_ref[0] = 1.0 + up_first * (1.0 - a_ref[1])
    red_ref[1] = up_first * b_ref[1]
    red_ref[2] = r_ref[0] + up_first * y_ref[1]
    red_ref[3] = 1.0 + up_last * (1.0 - b_ref[n - 2])
    red_ref[4] = up_last * a_ref[n - 2]
    red_ref[5] = r_ref[n - 1] + up_last * y_ref[n - 2]
    red_ref[6] = c_s[0]
    red_ref[7] = c_s[n - 1]


def reduced_solve(red_all):
    count = red_all.shape[0]
    lower, diag, upper, side = [], [], [], []
    for j in range(count):
        p0, q0, s0, p1, q1, s1, c_first, c_last = [red_all[j, k] for k in range(8)]
        if j == 0:
            face = c_first
            lower.append(jnp.zeros_like(face))
        else:
            face = 0.5 * (red_all[j - 1, 7] + c_first)
            lower.append(face)
        diag.append(p0 + face)
        upper.append(q0)
        side.append(s0)
        if j + 1 < count:
            below = 0.5 * (c_last + red_all[j + 1, 6])
        else:
            below = jnp.zeros_like(c_last)
        lower.append(q1)
        diag.append(p1 + below)
        upper.append(below)
        side.append(s1)
    size = len(diag)
    ratios, values = [], []
    g_prev = jnp.zeros_like(diag[0])
    v_prev = jnp.zeros_like(diag[0])
    for k in range(size):
        inv = 1.0 / (diag[k] - lower[k] * g_prev)
        g_prev = upper[k] * inv
        v_prev = (side[k] + lower[k] * v_prev) * inv
        ratios.append(g_prev)
        values.append(v_prev)
    solved = [None] * size
    following = jnp.zeros_like(diag[0])
    for k in reversed(range(size)):
        following = values[k] + ratios[k] * following
        solved[k] = following
    return jnp.stack(solved)


def sds(shape):
    return jax.ShapeDtypeStruct(shape, f32)


def exchange(xf, xl, ys):
    east_fwd, east_bwd = ring_perms("east")
    north_fwd, north_bwd = ring_perms("north")
    xlo = lax.ppermute(xl, "east", east_fwd)
    xhi = lax.ppermute(xf, "east", east_bwd)
    ylo = lax.ppermute(ys, "north", north_fwd)
    if lax.axis_size("north") == 2:
        yhi = ylo
    else:
        yhi = lax.ppermute(ys, "north", north_bwd)
    return xlo, xhi, ylo, yhi


def full_spec(shape):
    zeros = (0,) * len(shape)
    return pl.BlockSpec(shape, lambda i: zeros)


def local(
    thermal_field,
    liquid_fraction,
    steam_content_grid,
    carbonic_gas_grid,
    stratum_number_grid,
    injection_flags,
    lateral_transmissivity,
    vertical_transmissivity,
    stratum_advection_offsets,
):
    shape = thermal_field.shape
    n = shape[0]
    groups = n // ROWS
    assert shape[1:] == (ROWS, LANES) and n % ROWS == 0 and n <= LANES
    chunks = CHUNKS if groups % CHUNKS == 0 else 1
    depth = n // chunks
    cgroups = depth // ROWS
    table = jnp.concatenate(
        [lateral_transmissivity, stratum_advection_offsets, vertical_transmissivity[None]], 0
    )
    smem_spec = pl.BlockSpec(memory_space=pltpu.SMEM)
    vspec = pl.BlockSpec(memory_space=pltpu.MemorySpace.VMEM)
    heat, water, carbon, melt, co, xf0, xl0, y0 = pl.pallas_call(
        prep_kernel,
        out_shape=(sds(shape), sds(shape), sds(shape), sds(shape), sds((5,) + shape),
                   sds((5, groups, ROWS, LANES)), sds((5, groups, ROWS, LANES)),
                   sds((2, 5, ROWS, LANES))),
        in_specs=[smem_spec, vspec, vspec, vspec, vspec, vspec],
    )(table, stratum_number_grid, thermal_field, steam_content_grid, carbonic_gas_grid,
      liquid_fraction)
    xflo, xfhi, yflo, yfhi = exchange(xf0, xl0, y0)

    def block_spec(k):
        return pl.BlockSpec((depth, ROWS, LANES), lambda i: (k, 0, 0))

    halos = [None] * chunks
    for section_no in range(SECTIONS):
        first = section_no == 0
        for k in range(chunks):
            x5 = pl.BlockSpec((5, cgroups, ROWS, LANES), lambda i, k=k: (0, k, 0, 0))
            y5 = full_spec((2, 5, ROWS, LANES))
            in_specs = [block_spec(k)] * 5 + [
                pl.BlockSpec((4, depth, ROWS, LANES), lambda i, k=k: (0, k, 0, 0)),
                x5, x5, y5, y5,
            ]
            args = [heat, water, carbon, melt, injection_flags, co, xflo, xfhi, yflo, yfhi]
            if not first:
                in_specs += [full_spec((3, cgroups, ROWS, LANES))] * 2
                in_specs += [full_spec((2, 3, ROWS, LANES))] * 2
                args += list(halos[k])
            heat, water, carbon, melt, xf, xl, ys = pl.pallas_call(
                make_section_kernel(k, first),
                grid=(1,),
                out_shape=(sds(shape), sds(shape), sds(shape), sds(shape),
                           sds((3, cgroups, ROWS, LANES)), sds((3, cgroups, ROWS, LANES)),
                           sds((2, 3, ROWS, LANES))),
                in_specs=in_specs,
                out_specs=[block_spec(k)] * 4 + [
                    full_spec((3, cgroups, ROWS, LANES)), full_spec((3, cgroups, ROWS, LANES)),
                    full_spec((2, 3, ROWS, LANES)),
                ],
                input_output_aliases={0: 0, 1: 1, 2: 2, 3: 3},
            )(*args)
            if section_no + 1 < SECTIONS:
                halos[k] = exchange(xf, xl, ys)

    y, a, b, red = pl.pallas_call(
        sweep_kernel,
        grid=(1,),
        out_shape=(sds(shape), sds(shape), sds(shape), sds((8,) + shape[1:])),
        in_specs=[full_spec(shape), pl.BlockSpec((1,) + shape, lambda i: (4, 0, 0, 0))],
        out_specs=[full_spec(shape)] * 3 + [full_spec((8,) + shape[1:])],
        scratch_shapes=[pltpu.VMEM(shape, f32)] * 4,
    )(heat, co)
    count = lax.axis_size("depth")
    rank = lax.axis_index("depth")
    received = [red]
    for k in range(1, count):
        received.append(lax.ppermute(red, "depth", [(i, (i + k) % count) for i in range(count)]))
    stacked = jnp.stack(received)
    red_all = jnp.take(stacked, (rank - jnp.arange(count)) % count, axis=0)
    solved = reduced_solve(red_all)
    first = lax.dynamic_index_in_dim(solved, 2 * rank, keepdims=False)
    last = lax.dynamic_index_in_dim(solved, 2 * rank + 1, keepdims=False)
    heat_next = y + a * first[None] + b * last[None]
    return (heat_next, melt, water, carbon)


def solution(mesh):
    placed = (
        P("depth", "east", "north"),
        P("depth", "east", "north"),
        P("depth", "east", "north"),
        P("depth", "east", "north"),
        P("depth", "east", "north"),
        P("depth", "east", "north"),
        P(),
        P(),
        P(),
    )
    return jax.shard_map(
        local,
        mesh=mesh,
        in_specs=placed,
        out_specs=(
            P("depth", "east", "north"),
            P("depth", "east", "north"),
            P("depth", "east", "north"),
            P("depth", "east", "north"),
        ),
        check_vma=False,
    )
```

```python
import jax
import jax.numpy as jnp
from jax import lax
from jax.experimental import pallas as pl
from jax.experimental.pallas import tpu as pltpu
from jax.sharding import PartitionSpec as P

SECTIONS = 4


SOFTEN = 0.5
HEAT_CARRY = 0.5
SILL_RATE = 0.3
SILL_HEAT = 2.5
WATER_INPUT = 0.2
CARBON_INPUT = 0.1
MELT_SHARPNESS = 4.0
SOLIDUS = 1.0
DEPRESSION = 0.5
MELT_RATE = 0.5
LATENT = 0.3

ROWS = 8
CHUNKS = 2
LANES = 128
f32 = jnp.float32


def ring_perms(axis):
    count = lax.axis_size(axis)
    forward = [(i, (i + 1) % count) for i in range(count)]
    backward = [((i + 1) % count, i) for i in range(count)]
    return forward, backward


def iotas():
    sub = lax.broadcasted_iota(jnp.int32, (ROWS, LANES), 0)
    lane = lax.broadcasted_iota(jnp.int32, (ROWS, LANES), 1)
    return sub, lane


class EdgeAcc:
    def __init__(self, count, y_first, y_last):
        zero = jnp.zeros((ROWS, LANES), f32)
        self.xf = [zero] * count
        self.xl = [zero] * count
        self.yf = list(y_first)
        self.yl = list(y_last)

    def add_x(self, planes, b):
        at_b = lax.broadcasted_iota(jnp.int32, (ROWS, LANES), 0) == b
        for f, v in enumerate(planes):
            self.xf[f] = jnp.where(at_b, pltpu.roll(v, b, 0), self.xf[f])
            self.xl[f] = jnp.where(at_b, pltpu.roll(v, (b + 1) % ROWS, 0), self.xl[f])

    def add_y(self, planes, d, lane):
        at_d = lane == d
        for f, v in enumerate(planes):
            self.yf[f] = jnp.where(at_d, pltpu.roll(v, d % LANES, 1), self.yf[f])
            self.yl[f] = jnp.where(at_d, pltpu.roll(v, (d + 1) % LANES, 1), self.yl[f])


def x_minus(v, lo_tile, b, sub):
    return jnp.where(sub == 0, pltpu.roll(lo_tile, (ROWS - b) % ROWS, 0), pltpu.roll(v, 1, 0))


def x_plus(v, hi_tile, b, sub):
    return jnp.where(
        sub == ROWS - 1, pltpu.roll(hi_tile, (ROWS - 1 - b) % ROWS, 0), pltpu.roll(v, ROWS - 1, 0)
    )


def y_minus(v, lo_cols, d, lane):
    return jnp.where(lane == 0, pltpu.roll(lo_cols, (LANES - d) % LANES, 1), pltpu.roll(v, 1, 1))


def y_plus(v, hi_cols, d, lane):
    return jnp.where(
        lane == LANES - 1,
        pltpu.roll(hi_cols, (LANES - 1 - d) % LANES, 1),
        pltpu.roll(v, LANES - 1, 1),
    )


def prep_kernel(tab_ref, layer_ref, h_ref, w_ref, c_ref, m_ref,
                ho_ref, wo_ref, cbo_ref, mo_ref, co_ref, xf_ref, xl_ref, y_ref):
    groups = layer_ref.shape[0] // ROWS
    layers_count = tab_ref.shape[1]
    sub, lane = iotas()
    zero = jnp.zeros((ROWS, LANES), f32)

    def group(a, carry):
        y_f, y_l = carry
        acc = EdgeAcc(5, y_f, y_l)
        for b in range(ROWS):
            d = a * ROWS + b
            layer = layer_ref[d]
            vals = [zero] * 5
            for l in range(layers_count):
                hit = layer == l
                vals = [jnp.where(hit, tab_ref[k, l], vals[k]) for k in range(5)]
            for k in range(5):
                co_ref[k, d] = vals[k]
            heat, water, carbon = h_ref[d], w_ref[d], c_ref[d]
            ho_ref[d] = heat
            wo_ref[d] = water
            cbo_ref[d] = carbon
            mo_ref[d] = m_ref[d]
            acc.add_x([heat, water, carbon, vals[0], vals[2]], b)
            acc.add_y([heat, water, carbon, vals[1], vals[3]], d, lane)
        for f in range(5):
            xf_ref[f, a] = acc.xf[f]
            xl_ref[f, a] = acc.xl[f]
        return (tuple(acc.yf), tuple(acc.yl))

    y_f, y_l = lax.fori_loop(0, groups, group, ((zero,) * 5, (zero,) * 5))
    for f in range(5):
        y_ref[0, f] = y_f[f]
        y_ref[1, f] = y_l[f]


def make_section_kernel(chunk, first, cgroups):
    def kernel(h_ref, w_ref, c_ref, m_ref, sill_ref, co_ref, xflo_ref, xfhi_ref, yflo_ref, yfhi_ref,
               *rest):
        if first:
            ho_ref, wo_ref, cbo_ref, mo_ref, xf_ref, xl_ref, y_ref = rest
            xslo_ref, xshi_ref, yslo_ref, yshi_ref = xflo_ref, xfhi_ref, yflo_ref, yfhi_ref
        else:
            xslo_ref, xshi_ref, yslo_ref, yshi_ref = rest[:4]
            ho_ref, wo_ref, cbo_ref, mo_ref, xf_ref, xl_ref, y_ref = rest[4:]
        sub, lane = iotas()
        zero = jnp.zeros((ROWS, LANES), f32)
        step = pl.program_id(0)

        @pl.when(step == 0)
        def _():
            for f in range(3):
                y_ref[0, f] = zero
                y_ref[1, f] = zero

        sylo = [yslo_ref[1, f] for f in range(3)]
        syhi = [yshi_ref[0, f] for f in range(3)]
        cylo = [yflo_ref[1, f] for f in (3, 4)]
        cyhi = [yfhi_ref[0, f] for f in (3, 4)]

        if True:
            a = 0
            acc = EdgeAcc(3, [y_ref[0, f] for f in range(3)], [y_ref[1, f] for f in range(3)])
            sxlo = [xslo_ref[f, a] for f in range(3)]
            sxhi = [xshi_ref[f, a] for f in range(3)]
            cxlo = [xflo_ref[f, a] for f in (3, 4)]
            cxhi = [xfhi_ref[f, a] for f in (3, 4)]
            for b in range(ROWS):
                i = b
                d = (chunk * cgroups + step) * ROWS + b
                heat = h_ref[i]
                water = w_ref[i]
                carbon = c_ref[i]
                melt = m_ref[i]
                sill = sill_ref[i].astype(f32)
                cx = co_ref[0, i]
                cy = co_ref[1, i]
                vx = co_ref[2, i]
                vy = co_ref[3, i]
                mobile = [heat, water, carbon]
                q_xm = [x_minus(mobile[f], sxlo[f], b, sub) for f in range(3)]
                q_xp = [x_plus(mobile[f], sxhi[f], b, sub) for f in range(3)]
                q_ym = [y_minus(mobile[f], sylo[f], d, lane) for f in range(3)]
                q_yp = [y_plus(mobile[f], syhi[f], d, lane) for f in range(3)]
                cx_m = x_minus(cx, cxlo[0], b, sub)
                cx_p = x_plus(cx, cxhi[0], b, sub)
                vx_m = x_minus(vx, cxlo[1], b, sub)
                vx_p = x_plus(vx, cxhi[1], b, sub)
                cy_m = y_minus(cy, cylo[0], d, lane)
                cy_p = y_plus(cy, cyhi[0], d, lane)
                vy_m = y_minus(vy, cylo[1], d, lane)
                vy_p = y_plus(vy, cyhi[1], d, lane)
                soft = jnp.exp(-SOFTEN * heat)
                kx = cx * soft
                ky = cy * soft
                kx_m = cx_m * jnp.exp(-SOFTEN * q_xm[0])
                kx_p = cx_p * jnp.exp(-SOFTEN * q_xp[0])
                ky_m = cy_m * jnp.exp(-SOFTEN * q_ym[0])
                ky_p = cy_p * jnp.exp(-SOFTEN * q_yp[0])
                flux_x_lo = 0.5 * (kx_m + kx) * (heat - q_xm[0])
                flux_x_hi = 0.5 * (kx + kx_p) * (q_xp[0] - heat)
                flux_y_lo = 0.5 * (ky_m + ky) * (heat - q_ym[0])
                flux_y_hi = 0.5 * (ky + ky_p) * (q_yp[0] - heat)
                diffused = flux_x_hi - flux_x_lo + flux_y_hi - flux_y_lo
                fvx_m = 0.5 * (vx_m + vx)
                fvx_p = 0.5 * (vx + vx_p)
                fvy_m = 0.5 * (vy_m + vy)
                fvy_p = 0.5 * (vy + vy_p)
                inflow = []
                for f in range(3):
                    lo_x = jnp.maximum(fvx_m, 0.0) * q_xm[f] + jnp.minimum(fvx_m, 0.0) * mobile[f]
                    hi_x = jnp.maximum(fvx_p, 0.0) * mobile[f] + jnp.minimum(fvx_p, 0.0) * q_xp[f]
                    lo_y = jnp.maximum(fvy_m, 0.0) * q_ym[f] + jnp.minimum(fvy_m, 0.0) * mobile[f]
                    hi_y = jnp.maximum(fvy_p, 0.0) * mobile[f] + jnp.minimum(fvy_p, 0.0) * q_yp[f]
                    inflow.append(lo_x - hi_x + lo_y - hi_y)
                heat_one = heat + diffused + HEAT_CARRY * inflow[0]
                water_two = water + inflow[1] + sill * WATER_INPUT
                carbon_two = carbon + inflow[2] + sill * CARBON_INPUT
                heat_two = heat_one + sill * SILL_RATE * (SILL_HEAT - heat_one)
                z = MELT_SHARPNESS * (heat_two - SOLIDUS + DEPRESSION * water_two)
                target = 1.0 / (1.0 + jnp.exp(-z))
                melt_two = melt + MELT_RATE * (target - melt)
                heat_three = heat_two - LATENT * (melt_two - melt)
                ho_ref[i] = heat_three
                wo_ref[i] = water_two
                cbo_ref[i] = carbon_two
                mo_ref[i] = melt_two
                acc.add_x([heat_three, water_two, carbon_two], b)
                acc.add_y([heat_three, water_two, carbon_two], d, lane)
            for f in range(3):
                xf_ref[f, a] = acc.xf[f]
                xl_ref[f, a] = acc.xl[f]
                y_ref[0, f] = acc.yf[f]
                y_ref[1, f] = acc.yl[f]

    return kernel


def sweep_kernel(r_ref, cz_ref, y_ref, a_ref, b_ref, red_ref, c_s, g_s, vy_s, va_s):
    n = r_ref.shape[0]
    zero = jnp.zeros(r_ref.shape[1:], f32)
    one = jnp.ones(r_ref.shape[1:], f32)

    def conduct(i, carry):
        c_s[i] = cz_ref[0, i] * jnp.exp(-SOFTEN * r_ref[i])
        return carry

    lax.fori_loop(0, n, conduct, 0)

    def forward(i, carry):
        g_prev, vy_prev, va_prev = carry
        up = 0.5 * (c_s[i - 1] + c_s[i])
        down = 0.5 * (c_s[i] + c_s[i + 1])
        inv = 1.0 / (1.0 + up + down - up * g_prev)
        g = down * inv
        vy = (r_ref[i] + up * vy_prev) * inv
        va = (up * va_prev) * inv
        g_s[i] = g
        vy_s[i] = vy
        va_s[i] = va
        return g, vy, va

    lax.fori_loop(1, n - 1, forward, (zero, zero, one))

    def backward(k, carry):
        i = n - 2 - k
        y_next, a_next, b_next = carry
        g = g_s[i]
        y = vy_s[i] + g * y_next
        a = va_s[i] + g * a_next
        b = g * b_next
        y_ref[i] = y
        a_ref[i] = a
        b_ref[i] = b
        return y, a, b

    lax.fori_loop(0, n - 2, backward, (zero, zero, one))
    y_ref[0] = zero
    a_ref[0] = one
    b_ref[0] = zero
    y_ref[n - 1] = zero
    a_ref[n - 1] = zero
    b_ref[n - 1] = one
    up_first = 0.5 * (c_s[0] + c_s[1])
    up_last = 0.5 * (c_s[n - 2] + c_s[n - 1])
    red_ref[0] = 1.0 + up_first * (1.0 - a_ref[1])
    red_ref[1] = up_first * b_ref[1]
    red_ref[2] = r_ref[0] + up_first * y_ref[1]
    red_ref[3] = 1.0 + up_last * (1.0 - b_ref[n - 2])
    red_ref[4] = up_last * a_ref[n - 2]
    red_ref[5] = r_ref[n - 1] + up_last * y_ref[n - 2]
    red_ref[6] = c_s[0]
    red_ref[7] = c_s[n - 1]


def reduced_solve(red_all):
    count = red_all.shape[0]
    lower, diag, upper, side = [], [], [], []
    for j in range(count):
        p0, q0, s0, p1, q1, s1, c_first, c_last = [red_all[j, k] for k in range(8)]
        if j == 0:
            face = c_first
            lower.append(jnp.zeros_like(face))
        else:
            face = 0.5 * (red_all[j - 1, 7] + c_first)
            lower.append(face)
        diag.append(p0 + face)
        upper.append(q0)
        side.append(s0)
        if j + 1 < count:
            below = 0.5 * (c_last + red_all[j + 1, 6])
        else:
            below = jnp.zeros_like(c_last)
        lower.append(q1)
        diag.append(p1 + below)
        upper.append(below)
        side.append(s1)
    size = len(diag)
    ratios, values = [], []
    g_prev = jnp.zeros_like(diag[0])
    v_prev = jnp.zeros_like(diag[0])
    for k in range(size):
        inv = 1.0 / (diag[k] - lower[k] * g_prev)
        g_prev = upper[k] * inv
        v_prev = (side[k] + lower[k] * v_prev) * inv
        ratios.append(g_prev)
        values.append(v_prev)
    solved = [None] * size
    following = jnp.zeros_like(diag[0])
    for k in reversed(range(size)):
        following = values[k] + ratios[k] * following
        solved[k] = following
    return jnp.stack(solved)


def sds(shape):
    return jax.ShapeDtypeStruct(shape, f32)


def exchange(xf, xl, ys):
    east_fwd, east_bwd = ring_perms("east")
    north_fwd, north_bwd = ring_perms("north")
    xlo = lax.ppermute(xl, "east", east_fwd)
    xhi = lax.ppermute(xf, "east", east_bwd)
    ylo = lax.ppermute(ys, "north", north_fwd)
    if lax.axis_size("north") == 2:
        yhi = ylo
    else:
        yhi = lax.ppermute(ys, "north", north_bwd)
    return xlo, xhi, ylo, yhi


def full_spec(shape):
    zeros = (0,) * len(shape)
    return pl.BlockSpec(shape, lambda i: zeros)


def local(
    thermal_field,
    liquid_fraction,
    steam_content_grid,
    carbonic_gas_grid,
    stratum_number_grid,
    injection_flags,
    lateral_transmissivity,
    vertical_transmissivity,
    stratum_advection_offsets,
):
    shape = thermal_field.shape
    n = shape[0]
    groups = n // ROWS
    assert shape[1:] == (ROWS, LANES) and n % ROWS == 0 and n <= LANES
    chunks = CHUNKS if groups % CHUNKS == 0 else 1
    depth = n // chunks
    cgroups = depth // ROWS
    table = jnp.concatenate(
        [lateral_transmissivity, stratum_advection_offsets, vertical_transmissivity[None]], 0
    )
    smem_spec = pl.BlockSpec(memory_space=pltpu.SMEM)
    vspec = pl.BlockSpec(memory_space=pltpu.MemorySpace.VMEM)
    heat, water, carbon, melt, co, xf0, xl0, y0 = pl.pallas_call(
        prep_kernel,
        out_shape=(sds(shape), sds(shape), sds(shape), sds(shape), sds((5,) + shape),
                   sds((5, groups, ROWS, LANES)), sds((5, groups, ROWS, LANES)),
                   sds((2, 5, ROWS, LANES))),
        in_specs=[smem_spec, vspec, vspec, vspec, vspec, vspec],
    )(table, stratum_number_grid, thermal_field, steam_content_grid, carbonic_gas_grid,
      liquid_fraction)
    xflo, xfhi, yflo, yfhi = exchange(xf0, xl0, y0)

    def block_spec(k):
        return pl.BlockSpec((depth, ROWS, LANES), lambda i: (k, 0, 0))

    halos = [None] * chunks
    for section_no in range(SECTIONS):
        first = section_no == 0
        for k in range(chunks):
            def at(shift_fields, k=k, base=True):
                return lambda g: (0,) * shift_fields + ((k * cgroups + g) if base else g, 0, 0)

            plane = pl.BlockSpec((ROWS, ROWS, LANES), at(0))
            x5 = pl.BlockSpec((5, 1, ROWS, LANES), at(1))
            y5 = pl.BlockSpec((2, 5, ROWS, LANES), lambda g: (0, 0, 0, 0))
            x3 = pl.BlockSpec((3, 1, ROWS, LANES), at(1, base=False))
            y3 = pl.BlockSpec((2, 3, ROWS, LANES), lambda g: (0, 0, 0, 0))
            in_specs = [plane] * 5 + [
                pl.BlockSpec((4, ROWS, ROWS, LANES), at(1)), x5, x5, y5, y5,
            ]
            args = [heat, water, carbon, melt, injection_flags, co, xflo, xfhi, yflo, yfhi]
            if not first:
                in_specs += [x3, x3, y3, y3]
                args += list(halos[k])
            heat, water, carbon, melt, xf, xl, ys = pl.pallas_call(
                make_section_kernel(k, first, cgroups),
                grid=(cgroups,),
                out_shape=(sds(shape), sds(shape), sds(shape), sds(shape),
                           sds((3, cgroups, ROWS, LANES)), sds((3, cgroups, ROWS, LANES)),
                           sds((2, 3, ROWS, LANES))),
                in_specs=in_specs,
                out_specs=[plane] * 4 + [x3, x3, y3],
                input_output_aliases={0: 0, 1: 1, 2: 2, 3: 3},
            )(*args)
            if section_no + 1 < SECTIONS:
                halos[k] = exchange(xf, xl, ys)

    y, a, b, red = pl.pallas_call(
        sweep_kernel,
        grid=(1,),
        out_shape=(sds(shape), sds(shape), sds(shape), sds((8,) + shape[1:])),
        in_specs=[full_spec(shape), pl.BlockSpec((1,) + shape, lambda i: (4, 0, 0, 0))],
        out_specs=[full_spec(shape)] * 3 + [full_spec((8,) + shape[1:])],
        scratch_shapes=[pltpu.VMEM(shape, f32)] * 4,
    )(heat, co)
    count = lax.axis_size("depth")
    rank = lax.axis_index("depth")
    received = [red]
    for k in range(1, count):
        received.append(lax.ppermute(red, "depth", [(i, (i + k) % count) for i in range(count)]))
    stacked = jnp.stack(received)
    red_all = jnp.take(stacked, (rank - jnp.arange(count)) % count, axis=0)
    solved = reduced_solve(red_all)
    first = lax.dynamic_index_in_dim(solved, 2 * rank, keepdims=False)
    last = lax.dynamic_index_in_dim(solved, 2 * rank + 1, keepdims=False)
    heat_next = y + a * first[None] + b * last[None]
    return (heat_next, melt, water, carbon)


def solution(mesh):
    placed = (
        P("depth", "east", "north"),
        P("depth", "east", "north"),
        P("depth", "east", "north"),
        P("depth", "east", "north"),
        P("depth", "east", "north"),
        P("depth", "east", "north"),
        P(),
        P(),
        P(),
    )
    return jax.shard_map(
        local,
        mesh=mesh,
        in_specs=placed,
        out_specs=(
            P("depth", "east", "north"),
            P("depth", "east", "north"),
            P("depth", "east", "north"),
            P("depth", "east", "north"),
        ),
        check_vma=False,
    )
```

```python
import jax
import jax.numpy as jnp
from jax import lax
from jax.experimental import pallas as pl
from jax.experimental.pallas import tpu as pltpu
from jax.sharding import PartitionSpec as P

SECTIONS = 4


SOFTEN = 0.5
HEAT_CARRY = 0.5
SILL_RATE = 0.3
SILL_HEAT = 2.5
WATER_INPUT = 0.2
CARBON_INPUT = 0.1
MELT_SHARPNESS = 4.0
SOLIDUS = 1.0
DEPRESSION = 0.5
MELT_RATE = 0.5
LATENT = 0.3

ROWS = 8
CHUNKS = 2
LANES = 128
f32 = jnp.float32


def ring_perms(axis):
    count = lax.axis_size(axis)
    forward = [(i, (i + 1) % count) for i in range(count)]
    backward = [((i + 1) % count, i) for i in range(count)]
    return forward, backward


def iotas():
    sub = lax.broadcasted_iota(jnp.int32, (ROWS, LANES), 0)
    lane = lax.broadcasted_iota(jnp.int32, (ROWS, LANES), 1)
    return sub, lane


class EdgeAcc:
    def __init__(self, count, y_first, y_last):
        zero = jnp.zeros((ROWS, LANES), f32)
        self.xf = [zero] * count
        self.xl = [zero] * count
        self.yf = list(y_first)
        self.yl = list(y_last)

    def add_x(self, planes, b):
        at_b = lax.broadcasted_iota(jnp.int32, (ROWS, LANES), 0) == b
        for f, v in enumerate(planes):
            self.xf[f] = jnp.where(at_b, pltpu.roll(v, b, 0), self.xf[f])
            self.xl[f] = jnp.where(at_b, pltpu.roll(v, (b + 1) % ROWS, 0), self.xl[f])

    def add_y(self, planes, d, lane):
        at_d = lane == d
        for f, v in enumerate(planes):
            self.yf[f] = jnp.where(at_d, pltpu.roll(v, d % LANES, 1), self.yf[f])
            self.yl[f] = jnp.where(at_d, pltpu.roll(v, (d + 1) % LANES, 1), self.yl[f])


def x_minus(v, lo_tile, b, sub):
    return jnp.where(sub == 0, pltpu.roll(lo_tile, (ROWS - b) % ROWS, 0), pltpu.roll(v, 1, 0))


def x_plus(v, hi_tile, b, sub):
    return jnp.where(
        sub == ROWS - 1, pltpu.roll(hi_tile, (ROWS - 1 - b) % ROWS, 0), pltpu.roll(v, ROWS - 1, 0)
    )


def y_minus(v, lo_cols, d, lane):
    return jnp.where(lane == 0, pltpu.roll(lo_cols, (LANES - d) % LANES, 1), pltpu.roll(v, 1, 1))


def y_plus(v, hi_cols, d, lane):
    return jnp.where(
        lane == LANES - 1,
        pltpu.roll(hi_cols, (LANES - 1 - d) % LANES, 1),
        pltpu.roll(v, LANES - 1, 1),
    )


def prep_kernel(lat_ref, vert_ref, adv_ref, layer_ref, h_ref, w_ref, c_ref, m_ref,
                ho_ref, wo_ref, cbo_ref, mo_ref, co_ref, xf_ref, xl_ref, y_ref):
    groups = layer_ref.shape[0] // ROWS
    layers_count = vert_ref.shape[0]
    sub, lane = iotas()
    zero = jnp.zeros((ROWS, LANES), f32)

    def group(a, carry):
        y_f, y_l = carry
        acc = EdgeAcc(5, y_f, y_l)
        for b in range(ROWS):
            d = a * ROWS + b
            layer = layer_ref[d]
            vals = [zero] * 5
            for l in range(layers_count):
                hit = layer == l
                entries = (lat_ref[0, l], lat_ref[1, l], adv_ref[0, l], adv_ref[1, l], vert_ref[l])
                vals = [jnp.where(hit, entries[k], vals[k]) for k in range(5)]
            for k in range(5):
                co_ref[k, d] = vals[k]
            heat, water, carbon = h_ref[d], w_ref[d], c_ref[d]
            ho_ref[d] = heat
            wo_ref[d] = water
            cbo_ref[d] = carbon
            mo_ref[d] = m_ref[d]
            acc.add_x([heat, water, carbon, vals[0], vals[2]], b)
            acc.add_y([heat, water, carbon, vals[1], vals[3]], d, lane)
        for f in range(5):
            xf_ref[f, a] = acc.xf[f]
            xl_ref[f, a] = acc.xl[f]
        return (tuple(acc.yf), tuple(acc.yl))

    y_f, y_l = lax.fori_loop(0, groups, group, ((zero,) * 5, (zero,) * 5))
    for f in range(5):
        y_ref[0, f] = y_f[f]
        y_ref[1, f] = y_l[f]


def make_section_kernel(chunk, first):
    def kernel(h_ref, w_ref, c_ref, m_ref, sill_ref, co_ref, xflo_ref, xfhi_ref, yflo_ref, yfhi_ref,
               *rest):
        if first:
            ho_ref, wo_ref, cbo_ref, mo_ref, xf_ref, xl_ref, y_ref = rest
            xslo_ref, xshi_ref, yslo_ref, yshi_ref = xflo_ref, xfhi_ref, yflo_ref, yfhi_ref
        else:
            xslo_ref, xshi_ref, yslo_ref, yshi_ref = rest[:4]
            ho_ref, wo_ref, cbo_ref, mo_ref, xf_ref, xl_ref, y_ref = rest[4:]
        depth = h_ref.shape[0]
        groups = depth // ROWS
        sub, lane = iotas()
        zero = jnp.zeros((ROWS, LANES), f32)
        sylo = [yslo_ref[1, f] for f in range(3)]
        syhi = [yshi_ref[0, f] for f in range(3)]
        cylo = [yflo_ref[1, f] for f in (3, 4)]
        cyhi = [yfhi_ref[0, f] for f in (3, 4)]

        def group(a, carry):
            y_f, y_l = carry
            acc = EdgeAcc(3, y_f, y_l)
            sxlo = [xslo_ref[f, a] for f in range(3)]
            sxhi = [xshi_ref[f, a] for f in range(3)]
            cxlo = [xflo_ref[f, a] for f in (3, 4)]
            cxhi = [xfhi_ref[f, a] for f in (3, 4)]
            for b in range(ROWS):
                i = a * ROWS + b
                d = chunk * depth + i
                heat = h_ref[i]
                water = w_ref[i]
                carbon = c_ref[i]
                melt = m_ref[i]
                sill = sill_ref[i].astype(f32)
                cx = co_ref[0, i]
                cy = co_ref[1, i]
                vx = co_ref[2, i]
                vy = co_ref[3, i]
                mobile = [heat, water, carbon]
                q_xm = [x_minus(mobile[f], sxlo[f], b, sub) for f in range(3)]
                q_xp = [x_plus(mobile[f], sxhi[f], b, sub) for f in range(3)]
                q_ym = [y_minus(mobile[f], sylo[f], d, lane) for f in range(3)]
                q_yp = [y_plus(mobile[f], syhi[f], d, lane) for f in range(3)]
                cx_m = x_minus(cx, cxlo[0], b, sub)
                cx_p = x_plus(cx, cxhi[0], b, sub)
                vx_m = x_minus(vx, cxlo[1], b, sub)
                vx_p = x_plus(vx, cxhi[1], b, sub)
                cy_m = y_minus(cy, cylo[0], d, lane)
                cy_p = y_plus(cy, cyhi[0], d, lane)
                vy_m = y_minus(vy, cylo[1], d, lane)
                vy_p = y_plus(vy, cyhi[1], d, lane)
                soft = jnp.exp(-SOFTEN * heat)
                kx = cx * soft
                ky = cy * soft
                kx_m = cx_m * jnp.exp(-SOFTEN * q_xm[0])
                kx_p = cx_p * jnp.exp(-SOFTEN * q_xp[0])
                ky_m = cy_m * jnp.exp(-SOFTEN * q_ym[0])
                ky_p = cy_p * jnp.exp(-SOFTEN * q_yp[0])
                flux_x_lo = 0.5 * (kx_m + kx) * (heat - q_xm[0])
                flux_x_hi = 0.5 * (kx + kx_p) * (q_xp[0] - heat)
                flux_y_lo = 0.5 * (ky_m + ky) * (heat - q_ym[0])
                flux_y_hi = 0.5 * (ky + ky_p) * (q_yp[0] - heat)
                diffused = flux_x_hi - flux_x_lo + flux_y_hi - flux_y_lo
                fvx_m = 0.5 * (vx_m + vx)
                fvx_p = 0.5 * (vx + vx_p)
                fvy_m = 0.5 * (vy_m + vy)
                fvy_p = 0.5 * (vy + vy_p)
                inflow = []
                for f in range(3):
                    lo_x = jnp.maximum(fvx_m, 0.0) * q_xm[f] + jnp.minimum(fvx_m, 0.0) * mobile[f]
                    hi_x = jnp.maximum(fvx_p, 0.0) * mobile[f] + jnp.minimum(fvx_p, 0.0) * q_xp[f]
                    lo_y = jnp.maximum(fvy_m, 0.0) * q_ym[f] + jnp.minimum(fvy_m, 0.0) * mobile[f]
                    hi_y = jnp.maximum(fvy_p, 0.0) * mobile[f] + jnp.minimum(fvy_p, 0.0) * q_yp[f]
                    inflow.append(lo_x - hi_x + lo_y - hi_y)
                heat_one = heat + diffused + HEAT_CARRY * inflow[0]
                water_two = water + inflow[1] + sill * WATER_INPUT
                carbon_two = carbon + inflow[2] + sill * CARBON_INPUT
                heat_two = heat_one + sill * SILL_RATE * (SILL_HEAT - heat_one)
                z = MELT_SHARPNESS * (heat_two - SOLIDUS + DEPRESSION * water_two)
                target = 1.0 / (1.0 + jnp.exp(-z))
                melt_two = melt + MELT_RATE * (target - melt)
                heat_three = heat_two - LATENT * (melt_two - melt)
                ho_ref[i] = heat_three
                wo_ref[i] = water_two
                cbo_ref[i] = carbon_two
                mo_ref[i] = melt_two
                acc.add_x([heat_three, water_two, carbon_two], b)
                acc.add_y([heat_three, water_two, carbon_two], d, lane)
            for f in range(3):
                xf_ref[f, a] = acc.xf[f]
                xl_ref[f, a] = acc.xl[f]
            return (tuple(acc.yf), tuple(acc.yl))

        y_f, y_l = lax.fori_loop(0, groups, group, ((zero,) * 3, (zero,) * 3))
        for f in range(3):
            y_ref[0, f] = y_f[f]
            y_ref[1, f] = y_l[f]

    return kernel


def sweep_kernel(r_ref, cz_ref, y_ref, a_ref, b_ref, red_ref, c_s, g_s, vy_s, va_s):
    n = r_ref.shape[0]
    zero = jnp.zeros(r_ref.shape[1:], f32)
    one = jnp.ones(r_ref.shape[1:], f32)

    def conduct(i, carry):
        c_s[i] = cz_ref[0, i] * jnp.exp(-SOFTEN * r_ref[i])
        return carry

    lax.fori_loop(0, n, conduct, 0)

    def forward(i, carry):
        g_prev, vy_prev, va_prev = carry
        up = 0.5 * (c_s[i - 1] + c_s[i])
        down = 0.5 * (c_s[i] + c_s[i + 1])
        inv = 1.0 / (1.0 + up + down - up * g_prev)
        g = down * inv
        vy = (r_ref[i] + up * vy_prev) * inv
        va = (up * va_prev) * inv
        g_s[i] = g
        vy_s[i] = vy
        va_s[i] = va
        return g, vy, va

    lax.fori_loop(1, n - 1, forward, (zero, zero, one))

    def backward(k, carry):
        i = n - 2 - k
        y_next, a_next, b_next = carry
        g = g_s[i]
        y = vy_s[i] + g * y_next
        a = va_s[i] + g * a_next
        b = g * b_next
        y_ref[i] = y
        a_ref[i] = a
        b_ref[i] = b
        return y, a, b

    lax.fori_loop(0, n - 2, backward, (zero, zero, one))
    y_ref[0] = zero
    a_ref[0] = one
    b_ref[0] = zero
    y_ref[n - 1] = zero
    a_ref[n - 1] = zero
    b_ref[n - 1] = one
    up_first = 0.5 * (c_s[0] + c_s[1])
    up_last = 0.5 * (c_s[n - 2] + c_s[n - 1])
    red_ref[0] = 1.0 + up_first * (1.0 - a_ref[1])
    red_ref[1] = up_first * b_ref[1]
    red_ref[2] = r_ref[0] + up_first * y_ref[1]
    red_ref[3] = 1.0 + up_last * (1.0 - b_ref[n - 2])
    red_ref[4] = up_last * a_ref[n - 2]
    red_ref[5] = r_ref[n - 1] + up_last * y_ref[n - 2]
    red_ref[6] = c_s[0]
    red_ref[7] = c_s[n - 1]


def reduced_solve(red_all):
    count = len(red_all)
    lower, diag, upper, side = [], [], [], []
    for j in range(count):
        p0, q0, s0, p1, q1, s1, c_first, c_last = red_all[j]
        if j == 0:
            face = c_first
            lower.append(jnp.zeros_like(face))
        else:
            face = 0.5 * (red_all[j - 1][7] + c_first)
            lower.append(face)
        diag.append(p0 + face)
        upper.append(q0)
        side.append(s0)
        if j + 1 < count:
            below = 0.5 * (c_last + red_all[j + 1][6])
        else:
            below = jnp.zeros_like(c_last)
        lower.append(q1)
        diag.append(p1 + below)
        upper.append(below)
        side.append(s1)
    size = len(diag)
    ratios, values = [], []
    g_prev = jnp.zeros_like(diag[0])
    v_prev = jnp.zeros_like(diag[0])
    for k in range(size):
        inv = 1.0 / (diag[k] - lower[k] * g_prev)
        g_prev = upper[k] * inv
        v_prev = (side[k] + lower[k] * v_prev) * inv
        ratios.append(g_prev)
        values.append(v_prev)
    solved = [None] * size
    following = jnp.zeros_like(diag[0])
    for k in reversed(range(size)):
        following = values[k] + ratios[k] * following
        solved[k] = following
    return solved


def finish_kernel(rank_ref, y_ref, a_ref, b_ref, *rest):
    recv = rest[:-1]
    t_ref = rest[-1]
    count = len(recv)
    rank = rank_ref[0]
    red_all = []
    for j in range(count):
        source = (rank - j + count) % count
        planes = []
        for k in range(8):
            v = recv[count - 1][k]
            for m in reversed(range(count - 1)):
                v = jnp.where(source == m, recv[m][k], v)
            planes.append(v)
        red_all.append(planes)
    solved = reduced_solve(red_all)
    first = solved[2 * (count - 1)]
    last = solved[2 * (count - 1) + 1]
    for j in reversed(range(count - 1)):
        first = jnp.where(rank == j, solved[2 * j], first)
        last = jnp.where(rank == j, solved[2 * j + 1], last)

    def combine(i, carry):
        t_ref[i] = y_ref[i] + a_ref[i] * first + b_ref[i] * last
        return carry

    lax.fori_loop(0, y_ref.shape[0], combine, 0)


def sds(shape):
    return jax.ShapeDtypeStruct(shape, f32)


def exchange(xf, xl, ys):
    east_fwd, east_bwd = ring_perms("east")
    north_fwd, north_bwd = ring_perms("north")
    xlo = lax.ppermute(xl, "east", east_fwd)
    xhi = lax.ppermute(xf, "east", east_bwd)
    ylo = lax.ppermute(ys, "north", north_fwd)
    if lax.axis_size("north") == 2:
        yhi = ylo
    else:
        yhi = lax.ppermute(ys, "north", north_bwd)
    return xlo, xhi, ylo, yhi


def full_spec(shape):
    zeros = (0,) * len(shape)
    return pl.BlockSpec(shape, lambda i: zeros)


def local(
    thermal_field,
    liquid_fraction,
    steam_content_grid,
    carbonic_gas_grid,
    stratum_number_grid,
    injection_flags,
    lateral_transmissivity,
    vertical_transmissivity,
    stratum_advection_offsets,
):
    shape = thermal_field.shape
    n = shape[0]
    groups = n // ROWS
    assert shape[1:] == (ROWS, LANES) and n % ROWS == 0 and n <= LANES
    chunks = CHUNKS if groups % CHUNKS == 0 else 1
    depth = n // chunks
    cgroups = depth // ROWS
    smem_spec = pl.BlockSpec(memory_space=pltpu.SMEM)
    vspec = pl.BlockSpec(memory_space=pltpu.MemorySpace.VMEM)
    heat, water, carbon, melt, co, xf0, xl0, y0 = pl.pallas_call(
        prep_kernel,
        out_shape=(sds(shape), sds(shape), sds(shape), sds(shape), sds((5,) + shape),
                   sds((5, groups, ROWS, LANES)), sds((5, groups, ROWS, LANES)),
                   sds((2, 5, ROWS, LANES))),
        in_specs=[smem_spec] * 3 + [vspec] * 5,
    )(lateral_transmissivity, vertical_transmissivity, stratum_advection_offsets, stratum_number_grid, thermal_field, steam_content_grid, carbonic_gas_grid,
      liquid_fraction)
    xflo, xfhi, yflo, yfhi = exchange(xf0, xl0, y0)

    def block_spec(k):
        return pl.BlockSpec((depth, ROWS, LANES), lambda i: (k, 0, 0))

    halos = [None] * chunks
    for section_no in range(SECTIONS):
        first = section_no == 0
        for k in range(chunks):
            x5 = pl.BlockSpec((5, cgroups, ROWS, LANES), lambda i, k=k: (0, k, 0, 0))
            y5 = full_spec((2, 5, ROWS, LANES))
            in_specs = [block_spec(k)] * 5 + [
                pl.BlockSpec((4, depth, ROWS, LANES), lambda i, k=k: (0, k, 0, 0)),
                x5, x5, y5, y5,
            ]
            args = [heat, water, carbon, melt, injection_flags, co, xflo, xfhi, yflo, yfhi]
            if not first:
                in_specs += [full_spec((3, cgroups, ROWS, LANES))] * 2
                in_specs += [full_spec((2, 3, ROWS, LANES))] * 2
                args += list(halos[k])
            heat, water, carbon, melt, xf, xl, ys = pl.pallas_call(
                make_section_kernel(k, first),
                grid=(1,),
                out_shape=(sds(shape), sds(shape), sds(shape), sds(shape),
                           sds((3, cgroups, ROWS, LANES)), sds((3, cgroups, ROWS, LANES)),
                           sds((2, 3, ROWS, LANES))),
                in_specs=in_specs,
                out_specs=[block_spec(k)] * 4 + [
                    full_spec((3, cgroups, ROWS, LANES)), full_spec((3, cgroups, ROWS, LANES)),
                    full_spec((2, 3, ROWS, LANES)),
                ],
                input_output_aliases={0: 0, 1: 1, 2: 2, 3: 3},
            )(*args)
            if section_no + 1 < SECTIONS:
                halos[k] = exchange(xf, xl, ys)

    y, a, b, red = pl.pallas_call(
        sweep_kernel,
        grid=(1,),
        out_shape=(sds(shape), sds(shape), sds(shape), sds((8,) + shape[1:])),
        in_specs=[full_spec(shape), pl.BlockSpec((1,) + shape, lambda i: (4, 0, 0, 0))],
        out_specs=[full_spec(shape)] * 3 + [full_spec((8,) + shape[1:])],
        scratch_shapes=[pltpu.VMEM(shape, f32)] * 4,
    )(heat, co)
    count = lax.axis_size("depth")
    rank = lax.axis_index("depth")
    received = [red]
    for k in range(1, count):
        received.append(lax.ppermute(red, "depth", [(i, (i + k) % count) for i in range(count)]))
    rank_arr = jnp.full((1,), rank, jnp.int32)
    heat_next = pl.pallas_call(
        finish_kernel,
        out_shape=sds(shape),
        in_specs=[smem_spec] + [vspec] * (3 + count),
    )(rank_arr, y, a, b, *received)
    return (heat_next, melt, water, carbon)


def solution(mesh):
    placed = (
        P("depth", "east", "north"),
        P("depth", "east", "north"),
        P("depth", "east", "north"),
        P("depth", "east", "north"),
        P("depth", "east", "north"),
        P("depth", "east", "north"),
        P(),
        P(),
        P(),
    )
    return jax.shard_map(
        local,
        mesh=mesh,
        in_specs=placed,
        out_specs=(
            P("depth", "east", "north"),
            P("depth", "east", "north"),
            P("depth", "east", "north"),
            P("depth", "east", "north"),
        ),
        check_vma=False,
    )
```

```python
import jax
import jax.numpy as jnp
from jax import lax
from jax.experimental import pallas as pl
from jax.experimental.pallas import tpu as pltpu
from jax.sharding import PartitionSpec as P

SECTIONS = 4


SOFTEN = 0.5
HEAT_CARRY = 0.5
SILL_RATE = 0.3
SILL_HEAT = 2.5
WATER_INPUT = 0.2
CARBON_INPUT = 0.1
MELT_SHARPNESS = 4.0
SOLIDUS = 1.0
DEPRESSION = 0.5
MELT_RATE = 0.5
LATENT = 0.3

ROWS = 8
CHUNKS = 2
LANES = 128
f32 = jnp.float32


def ring_perms(axis):
    count = lax.axis_size(axis)
    forward = [(i, (i + 1) % count) for i in range(count)]
    backward = [((i + 1) % count, i) for i in range(count)]
    return forward, backward


def iotas():
    sub = lax.broadcasted_iota(jnp.int32, (ROWS, LANES), 0)
    lane = lax.broadcasted_iota(jnp.int32, (ROWS, LANES), 1)
    return sub, lane


class EdgeAcc:
    def __init__(self, count, y_first, y_last):
        zero = jnp.zeros((ROWS, LANES), f32)
        self.xf = [zero] * count
        self.xl = [zero] * count
        self.yf = list(y_first)
        self.yl = list(y_last)

    def add_x(self, planes, b):
        at_b = lax.broadcasted_iota(jnp.int32, (ROWS, LANES), 0) == b
        for f, v in enumerate(planes):
            self.xf[f] = jnp.where(at_b, pltpu.roll(v, b, 0), self.xf[f])
            self.xl[f] = jnp.where(at_b, pltpu.roll(v, (b + 1) % ROWS, 0), self.xl[f])

    def add_y(self, planes, d, lane):
        at_d = lane == d
        for f, v in enumerate(planes):
            self.yf[f] = jnp.where(at_d, pltpu.roll(v, d % LANES, 1), self.yf[f])
            self.yl[f] = jnp.where(at_d, pltpu.roll(v, (d + 1) % LANES, 1), self.yl[f])


def x_minus(v, lo_row, b, sub):
    return jnp.where(sub == 0, lo_row, pltpu.roll(v, 1, 0))


def x_plus(v, hi_row, b, sub):
    return jnp.where(sub == ROWS - 1, hi_row, pltpu.roll(v, ROWS - 1, 0))


def y_minus(v, lo_cols, d, lane):
    return jnp.where(lane == 0, pltpu.roll(lo_cols, (LANES - d) % LANES, 1), pltpu.roll(v, 1, 1))


def y_plus(v, hi_cols, d, lane):
    return jnp.where(
        lane == LANES - 1,
        pltpu.roll(hi_cols, (LANES - 1 - d) % LANES, 1),
        pltpu.roll(v, LANES - 1, 1),
    )


def prep_kernel(lat_ref, vert_ref, adv_ref, layer_ref, h_ref, w_ref, c_ref, m_ref,
                ho_ref, wo_ref, cbo_ref, mo_ref, co_ref, xf_ref, xl_ref, y_ref):
    groups = layer_ref.shape[0] // ROWS
    layers_count = vert_ref.shape[0]
    sub, lane = iotas()
    zero = jnp.zeros((ROWS, LANES), f32)

    def group(a, carry):
        y_f, y_l = carry
        acc = EdgeAcc(5, y_f, y_l)
        for b in range(ROWS):
            d = a * ROWS + b
            layer = layer_ref[d]
            vals = [zero] * 5
            for l in range(layers_count):
                hit = layer == l
                entries = (lat_ref[0, l], lat_ref[1, l], adv_ref[0, l], adv_ref[1, l], vert_ref[l])
                vals = [jnp.where(hit, entries[k], vals[k]) for k in range(5)]
            for k in range(5):
                co_ref[k, d] = vals[k]
            heat, water, carbon = h_ref[d], w_ref[d], c_ref[d]
            ho_ref[d] = heat
            wo_ref[d] = water
            cbo_ref[d] = carbon
            mo_ref[d] = m_ref[d]
            acc.add_y([heat, water, carbon, vals[1], vals[3]], d, lane)
        planes = pl.ds(a * ROWS, ROWS)
        sources = ((ho_ref, None), (wo_ref, None), (cbo_ref, None), (co_ref, 0), (co_ref, 2))
        for f, (out, field) in enumerate(sources):
            if field is None:
                xf_ref[f, a] = out[planes, 0, :]
                xl_ref[f, a] = out[planes, ROWS - 1, :]
            else:
                xf_ref[f, a] = out[field, planes, 0, :]
                xl_ref[f, a] = out[field, planes, ROWS - 1, :]
        return (tuple(acc.yf), tuple(acc.yl))

    y_f, y_l = lax.fori_loop(0, groups, group, ((zero,) * 5, (zero,) * 5))
    for f in range(5):
        y_ref[0, f] = y_f[f]
        y_ref[1, f] = y_l[f]


def make_section_kernel(chunk, first):
    def kernel(h_ref, w_ref, c_ref, m_ref, sill_ref, co_ref, xflo_ref, xfhi_ref, yflo_ref, yfhi_ref,
               *rest):
        if first:
            ho_ref, wo_ref, cbo_ref, mo_ref, xf_ref, xl_ref, y_ref = rest
            xslo_ref, xshi_ref, yslo_ref, yshi_ref = xflo_ref, xfhi_ref, yflo_ref, yfhi_ref
        else:
            xslo_ref, xshi_ref, yslo_ref, yshi_ref = rest[:4]
            ho_ref, wo_ref, cbo_ref, mo_ref, xf_ref, xl_ref, y_ref = rest[4:]
        depth = h_ref.shape[0]
        groups = depth // ROWS
        sub, lane = iotas()
        zero = jnp.zeros((ROWS, LANES), f32)
        sylo = [yslo_ref[1, f] for f in range(3)]
        syhi = [yshi_ref[0, f] for f in range(3)]
        cylo = [yflo_ref[1, f] for f in (3, 4)]
        cyhi = [yfhi_ref[0, f] for f in (3, 4)]

        def group(a, carry):
            y_f, y_l = carry
            acc = EdgeAcc(3, y_f, y_l)
            for b in range(ROWS):
                i = a * ROWS + b
                row = pl.ds(b, ROWS, stride=0)
                sxlo = [xslo_ref[f, a, row, :] for f in range(3)]
                sxhi = [xshi_ref[f, a, row, :] for f in range(3)]
                cxlo = [xflo_ref[f, a, row, :] for f in (3, 4)]
                cxhi = [xfhi_ref[f, a, row, :] for f in (3, 4)]
                d = chunk * depth + i
                heat = h_ref[i]
                water = w_ref[i]
                carbon = c_ref[i]
                melt = m_ref[i]
                sill = sill_ref[i].astype(f32)
                cx = co_ref[0, i]
                cy = co_ref[1, i]
                vx = co_ref[2, i]
                vy = co_ref[3, i]
                mobile = [heat, water, carbon]
                q_xm = [x_minus(mobile[f], sxlo[f], b, sub) for f in range(3)]
                q_xp = [x_plus(mobile[f], sxhi[f], b, sub) for f in range(3)]
                q_ym = [y_minus(mobile[f], sylo[f], d, lane) for f in range(3)]
                q_yp = [y_plus(mobile[f], syhi[f], d, lane) for f in range(3)]
                cx_m = x_minus(cx, cxlo[0], b, sub)
                cx_p = x_plus(cx, cxhi[0], b, sub)
                vx_m = x_minus(vx, cxlo[1], b, sub)
                vx_p = x_plus(vx, cxhi[1], b, sub)
                cy_m = y_minus(cy, cylo[0], d, lane)
                cy_p = y_plus(cy, cyhi[0], d, lane)
                vy_m = y_minus(vy, cylo[1], d, lane)
                vy_p = y_plus(vy, cyhi[1], d, lane)
                soft = jnp.exp(-SOFTEN * heat)
                kx = cx * soft
                ky = cy * soft
                kx_m = cx_m * jnp.exp(-SOFTEN * q_xm[0])
                kx_p = cx_p * jnp.exp(-SOFTEN * q_xp[0])
                ky_m = cy_m * jnp.exp(-SOFTEN * q_ym[0])
                ky_p = cy_p * jnp.exp(-SOFTEN * q_yp[0])
                flux_x_lo = 0.5 * (kx_m + kx) * (heat - q_xm[0])
                flux_x_hi = 0.5 * (kx + kx_p) * (q_xp[0] - heat)
                flux_y_lo = 0.5 * (ky_m + ky) * (heat - q_ym[0])
                flux_y_hi = 0.5 * (ky + ky_p) * (q_yp[0] - heat)
                diffused = flux_x_hi - flux_x_lo + flux_y_hi - flux_y_lo
                fvx_m = 0.5 * (vx_m + vx)
                fvx_p = 0.5 * (vx + vx_p)
                fvy_m = 0.5 * (vy_m + vy)
                fvy_p = 0.5 * (vy + vy_p)
                inflow = []
                for f in range(3):
                    lo_x = jnp.maximum(fvx_m, 0.0) * q_xm[f] + jnp.minimum(fvx_m, 0.0) * mobile[f]
                    hi_x = jnp.maximum(fvx_p, 0.0) * mobile[f] + jnp.minimum(fvx_p, 0.0) * q_xp[f]
                    lo_y = jnp.maximum(fvy_m, 0.0) * q_ym[f] + jnp.minimum(fvy_m, 0.0) * mobile[f]
                    hi_y = jnp.maximum(fvy_p, 0.0) * mobile[f] + jnp.minimum(fvy_p, 0.0) * q_yp[f]
                    inflow.append(lo_x - hi_x + lo_y - hi_y)
                heat_one = heat + diffused + HEAT_CARRY * inflow[0]
                water_two = water + inflow[1] + sill * WATER_INPUT
                carbon_two = carbon + inflow[2] + sill * CARBON_INPUT
                heat_two = heat_one + sill * SILL_RATE * (SILL_HEAT - heat_one)
                z = MELT_SHARPNESS * (heat_two - SOLIDUS + DEPRESSION * water_two)
                target = 1.0 / (1.0 + jnp.exp(-z))
                melt_two = melt + MELT_RATE * (target - melt)
                heat_three = heat_two - LATENT * (melt_two - melt)
                ho_ref[i] = heat_three
                wo_ref[i] = water_two
                cbo_ref[i] = carbon_two
                mo_ref[i] = melt_two
                acc.add_y([heat_three, water_two, carbon_two], d, lane)
            planes = pl.ds(a * ROWS, ROWS)
            for f, out in enumerate((ho_ref, wo_ref, cbo_ref)):
                xf_ref[f, a] = out[planes, 0, :]
                xl_ref[f, a] = out[planes, ROWS - 1, :]
            return (tuple(acc.yf), tuple(acc.yl))

        y_f, y_l = lax.fori_loop(0, groups, group, ((zero,) * 3, (zero,) * 3))
        for f in range(3):
            y_ref[0, f] = y_f[f]
            y_ref[1, f] = y_l[f]

    return kernel


def sweep_kernel(r_ref, cz_ref, y_ref, a_ref, b_ref, red_ref, c_s, g_s, vy_s, va_s):
    n = r_ref.shape[0]
    zero = jnp.zeros(r_ref.shape[1:], f32)
    one = jnp.ones(r_ref.shape[1:], f32)

    def conduct(i, carry):
        c_s[i] = cz_ref[0, i] * jnp.exp(-SOFTEN * r_ref[i])
        return carry

    lax.fori_loop(0, n, conduct, 0)

    def forward(i, carry):
        g_prev, vy_prev, va_prev = carry
        up = 0.5 * (c_s[i - 1] + c_s[i])
        down = 0.5 * (c_s[i] + c_s[i + 1])
        inv = 1.0 / (1.0 + up + down - up * g_prev)
        g = down * inv
        vy = (r_ref[i] + up * vy_prev) * inv
        va = (up * va_prev) * inv
        g_s[i] = g
        vy_s[i] = vy
        va_s[i] = va
        return g, vy, va

    lax.fori_loop(1, n - 1, forward, (zero, zero, one))

    def backward(k, carry):
        i = n - 2 - k
        y_next, a_next, b_next = carry
        g = g_s[i]
        y = vy_s[i] + g * y_next
        a = va_s[i] + g * a_next
        b = g * b_next
        y_ref[i] = y
        a_ref[i] = a
        b_ref[i] = b
        return y, a, b

    lax.fori_loop(0, n - 2, backward, (zero, zero, one))
    y_ref[0] = zero
    a_ref[0] = one
    b_ref[0] = zero
    y_ref[n - 1] = zero
    a_ref[n - 1] = zero
    b_ref[n - 1] = one
    up_first = 0.5 * (c_s[0] + c_s[1])
    up_last = 0.5 * (c_s[n - 2] + c_s[n - 1])
    red_ref[0] = 1.0 + up_first * (1.0 - a_ref[1])
    red_ref[1] = up_first * b_ref[1]
    red_ref[2] = r_ref[0] + up_first * y_ref[1]
    red_ref[3] = 1.0 + up_last * (1.0 - b_ref[n - 2])
    red_ref[4] = up_last * a_ref[n - 2]
    red_ref[5] = r_ref[n - 1] + up_last * y_ref[n - 2]
    red_ref[6] = c_s[0]
    red_ref[7] = c_s[n - 1]


def reduced_solve(red_all):
    count = len(red_all)
    lower, diag, upper, side = [], [], [], []
    for j in range(count):
        p0, q0, s0, p1, q1, s1, c_first, c_last = red_all[j]
        if j == 0:
            face = c_first
            lower.append(jnp.zeros_like(face))
        else:
            face = 0.5 * (red_all[j - 1][7] + c_first)
            lower.append(face)
        diag.append(p0 + face)
        upper.append(q0)
        side.append(s0)
        if j + 1 < count:
            below = 0.5 * (c_last + red_all[j + 1][6])
        else:
            below = jnp.zeros_like(c_last)
        lower.append(q1)
        diag.append(p1 + below)
        upper.append(below)
        side.append(s1)
    size = len(diag)
    ratios, values = [], []
    g_prev = jnp.zeros_like(diag[0])
    v_prev = jnp.zeros_like(diag[0])
    for k in range(size):
        inv = 1.0 / (diag[k] - lower[k] * g_prev)
        g_prev = upper[k] * inv
        v_prev = (side[k] + lower[k] * v_prev) * inv
        ratios.append(g_prev)
        values.append(v_prev)
    solved = [None] * size
    following = jnp.zeros_like(diag[0])
    for k in reversed(range(size)):
        following = values[k] + ratios[k] * following
        solved[k] = following
    return solved


def finish_kernel(rank_ref, y_ref, a_ref, b_ref, *rest):
    recv = rest[:-1]
    t_ref = rest[-1]
    count = len(recv)
    rank = rank_ref[0]
    red_all = []
    for j in range(count):
        source = (rank - j + count) % count
        planes = []
        for k in range(8):
            v = recv[count - 1][k]
            for m in reversed(range(count - 1)):
                v = jnp.where(source == m, recv[m][k], v)
            planes.append(v)
        red_all.append(planes)
    solved = reduced_solve(red_all)
    first = solved[2 * (count - 1)]
    last = solved[2 * (count - 1) + 1]
    for j in reversed(range(count - 1)):
        first = jnp.where(rank == j, solved[2 * j], first)
        last = jnp.where(rank == j, solved[2 * j + 1], last)

    def combine(i, carry):
        t_ref[i] = y_ref[i] + a_ref[i] * first + b_ref[i] * last
        return carry

    lax.fori_loop(0, y_ref.shape[0], combine, 0)


def sds(shape):
    return jax.ShapeDtypeStruct(shape, f32)


def exchange(xf, xl, ys):
    east_fwd, east_bwd = ring_perms("east")
    north_fwd, north_bwd = ring_perms("north")
    xlo = lax.ppermute(xl, "east", east_fwd)
    xhi = lax.ppermute(xf, "east", east_bwd)
    ylo = lax.ppermute(ys, "north", north_fwd)
    if lax.axis_size("north") == 2:
        yhi = ylo
    else:
        yhi = lax.ppermute(ys, "north", north_bwd)
    return xlo, xhi, ylo, yhi


def full_spec(shape):
    zeros = (0,) * len(shape)
    return pl.BlockSpec(shape, lambda i: zeros)


def local(
    thermal_field,
    liquid_fraction,
    steam_content_grid,
    carbonic_gas_grid,
    stratum_number_grid,
    injection_flags,
    lateral_transmissivity,
    vertical_transmissivity,
    stratum_advection_offsets,
):
    shape = thermal_field.shape
    n = shape[0]
    groups = n // ROWS
    assert shape[1:] == (ROWS, LANES) and n % ROWS == 0 and n <= LANES
    chunks = CHUNKS if groups % CHUNKS == 0 else 1
    depth = n // chunks
    cgroups = depth // ROWS
    smem_spec = pl.BlockSpec(memory_space=pltpu.SMEM)
    vspec = pl.BlockSpec(memory_space=pltpu.MemorySpace.VMEM)
    heat, water, carbon, melt, co, xf0, xl0, y0 = pl.pallas_call(
        prep_kernel,
        out_shape=(sds(shape), sds(shape), sds(shape), sds(shape), sds((5,) + shape),
                   sds((5, groups, ROWS, LANES)), sds((5, groups, ROWS, LANES)),
                   sds((2, 5, ROWS, LANES))),
        in_specs=[smem_spec] * 3 + [vspec] * 5,
    )(lateral_transmissivity, vertical_transmissivity, stratum_advection_offsets, stratum_number_grid, thermal_field, steam_content_grid, carbonic_gas_grid,
      liquid_fraction)
    xflo, xfhi, yflo, yfhi = exchange(xf0, xl0, y0)

    def block_spec(k):
        return pl.BlockSpec((depth, ROWS, LANES), lambda i: (k, 0, 0))

    halos = [None] * chunks
    for section_no in range(SECTIONS):
        first = section_no == 0
        for k in range(chunks):
            x5 = pl.BlockSpec((5, cgroups, ROWS, LANES), lambda i, k=k: (0, k, 0, 0))
            y5 = full_spec((2, 5, ROWS, LANES))
            in_specs = [block_spec(k)] * 5 + [
                pl.BlockSpec((4, depth, ROWS, LANES), lambda i, k=k: (0, k, 0, 0)),
                x5, x5, y5, y5,
            ]
            args = [heat, water, carbon, melt, injection_flags, co, xflo, xfhi, yflo, yfhi]
            if not first:
                in_specs += [full_spec((3, cgroups, ROWS, LANES))] * 2
                in_specs += [full_spec((2, 3, ROWS, LANES))] * 2
                args += list(halos[k])
            heat, water, carbon, melt, xf, xl, ys = pl.pallas_call(
                make_section_kernel(k, first),
                grid=(1,),
                out_shape=(sds(shape), sds(shape), sds(shape), sds(shape),
                           sds((3, cgroups, ROWS, LANES)), sds((3, cgroups, ROWS, LANES)),
                           sds((2, 3, ROWS, LANES))),
                in_specs=in_specs,
                out_specs=[block_spec(k)] * 4 + [
                    full_spec((3, cgroups, ROWS, LANES)), full_spec((3, cgroups, ROWS, LANES)),
                    full_spec((2, 3, ROWS, LANES)),
                ],
                input_output_aliases={0: 0, 1: 1, 2: 2, 3: 3},
            )(*args)
            if section_no + 1 < SECTIONS:
                halos[k] = exchange(xf, xl, ys)

    y, a, b, red = pl.pallas_call(
        sweep_kernel,
        grid=(1,),
        out_shape=(sds(shape), sds(shape), sds(shape), sds((8,) + shape[1:])),
        in_specs=[full_spec(shape), pl.BlockSpec((1,) + shape, lambda i: (4, 0, 0, 0))],
        out_specs=[full_spec(shape)] * 3 + [full_spec((8,) + shape[1:])],
        scratch_shapes=[pltpu.VMEM(shape, f32)] * 4,
    )(heat, co)
    count = lax.axis_size("depth")
    rank = lax.axis_index("depth")
    received = [red]
    for k in range(1, count):
        received.append(lax.ppermute(red, "depth", [(i, (i + k) % count) for i in range(count)]))
    rank_arr = jnp.full((1,), rank, jnp.int32)
    heat_next = pl.pallas_call(
        finish_kernel,
        out_shape=sds(shape),
        in_specs=[smem_spec] + [vspec] * (3 + count),
    )(rank_arr, y, a, b, *received)
    return (heat_next, melt, water, carbon)


def solution(mesh):
    placed = (
        P("depth", "east", "north"),
        P("depth", "east", "north"),
        P("depth", "east", "north"),
        P("depth", "east", "north"),
        P("depth", "east", "north"),
        P("depth", "east", "north"),
        P(),
        P(),
        P(),
    )
    return jax.shard_map(
        local,
        mesh=mesh,
        in_specs=placed,
        out_specs=(
            P("depth", "east", "north"),
            P("depth", "east", "north"),
            P("depth", "east", "north"),
            P("depth", "east", "north"),
        ),
        check_vma=False,
    )
```

```python
import jax
import jax.numpy as jnp
from jax import lax
from jax.experimental import pallas as pl
from jax.experimental.pallas import tpu as pltpu
from jax.sharding import PartitionSpec as P

SECTIONS = 4


SOFTEN = 0.5
HEAT_CARRY = 0.5
SILL_RATE = 0.3
SILL_HEAT = 2.5
WATER_INPUT = 0.2
CARBON_INPUT = 0.1
MELT_SHARPNESS = 4.0
SOLIDUS = 1.0
DEPRESSION = 0.5
MELT_RATE = 0.5
LATENT = 0.3

ROWS = 8
CHUNKS = 2
LANES = 128
f32 = jnp.float32


def ring_perms(axis):
    count = lax.axis_size(axis)
    forward = [(i, (i + 1) % count) for i in range(count)]
    backward = [((i + 1) % count, i) for i in range(count)]
    return forward, backward


def iotas():
    sub = lax.broadcasted_iota(jnp.int32, (ROWS, LANES), 0)
    lane = lax.broadcasted_iota(jnp.int32, (ROWS, LANES), 1)
    return sub, lane


class EdgeAcc:
    def __init__(self, count, y_first, y_last):
        zero = jnp.zeros((ROWS, LANES), f32)
        self.xf = [zero] * count
        self.xl = [zero] * count
        self.yf = list(y_first)
        self.yl = list(y_last)

    def add_x(self, planes, b):
        at_b = lax.broadcasted_iota(jnp.int32, (ROWS, LANES), 0) == b
        for f, v in enumerate(planes):
            self.xf[f] = jnp.where(at_b, pltpu.roll(v, b, 0), self.xf[f])
            self.xl[f] = jnp.where(at_b, pltpu.roll(v, (b + 1) % ROWS, 0), self.xl[f])

    def add_y(self, planes, d, lane):
        at_d = lane == d
        for f, v in enumerate(planes):
            self.yf[f] = jnp.where(at_d, pltpu.roll(v, d % LANES, 1), self.yf[f])
            self.yl[f] = jnp.where(at_d, pltpu.roll(v, (d + 1) % LANES, 1), self.yl[f])


def x_minus(v, lo_row, b, sub):
    return jnp.where(sub == 0, lo_row, pltpu.roll(v, 1, 0))


def x_plus(v, hi_row, b, sub):
    return jnp.where(sub == ROWS - 1, hi_row, pltpu.roll(v, ROWS - 1, 0))


def y_minus(v, lo_cols, d, lane):
    return jnp.where(lane == 0, pltpu.roll(lo_cols, (LANES - d) % LANES, 1), pltpu.roll(v, 1, 1))


def y_plus(v, hi_cols, d, lane):
    return jnp.where(
        lane == LANES - 1,
        pltpu.roll(hi_cols, (LANES - 1 - d) % LANES, 1),
        pltpu.roll(v, LANES - 1, 1),
    )


def lookup_planes(tables, layer, count):
    zero = jnp.zeros(layer.shape, f32)
    vals = [zero] * len(tables)
    for l in range(count):
        hit = layer == l
        vals = [jnp.where(hit, tab(l), vals[k]) for k, tab in enumerate(tables)]
    return vals


def prep_kernel(lat_ref, vert_ref, adv_ref, layer_ref, h_ref, w_ref, c_ref, m_ref,
                ho_ref, wo_ref, cbo_ref, mo_ref, co_ref):
    count = vert_ref.shape[0]
    tables = (
        lambda l: lat_ref[0, l], lambda l: lat_ref[1, l],
        lambda l: adv_ref[0, l], lambda l: adv_ref[1, l], lambda l: vert_ref[l],
    )

    def plane(d, carry):
        vals = lookup_planes(tables, layer_ref[d], count)
        for k in range(5):
            co_ref[k, d] = vals[k]
        ho_ref[d] = h_ref[d]
        wo_ref[d] = w_ref[d]
        cbo_ref[d] = c_ref[d]
        mo_ref[d] = m_ref[d]
        return carry

    lax.fori_loop(0, layer_ref.shape[0], plane, 0)


def make_section_kernel(chunk, first):
    def kernel(lat_ref, adv_ref, h_ref, w_ref, c_ref, m_ref, sill_ref, co_ref,
               xflo_ref, xfhi_ref, yflo_ref, yfhi_ref, *rest):
        if first:
            ho_ref, wo_ref, cbo_ref, mo_ref, xf_ref, xl_ref, y_ref, cx_s = rest
            xslo_ref, xshi_ref, yslo_ref, yshi_ref = xflo_ref, xfhi_ref, yflo_ref, yfhi_ref
        else:
            xslo_ref, xshi_ref, yslo_ref, yshi_ref = rest[:4]
            ho_ref, wo_ref, cbo_ref, mo_ref, xf_ref, xl_ref, y_ref, cx_s = rest[4:]
        depth = h_ref.shape[0]
        groups = depth // ROWS
        count = lat_ref.shape[1]
        sub, lane = iotas()
        zero = jnp.zeros((ROWS, LANES), f32)
        x_tables = (lambda l: lat_ref[0, l], lambda l: adv_ref[0, l])
        y_tables = (lambda l: lat_ref[1, l], lambda l: adv_ref[1, l])
        for a in range(groups):
            lo = lookup_planes(x_tables, xflo_ref[3, a], count)
            hi = lookup_planes(x_tables, xfhi_ref[3, a], count)
            cx_s[0, a] = lo[0]
            cx_s[1, a] = lo[1]
            cx_s[2, a] = hi[0]
            cx_s[3, a] = hi[1]
        sylo = [yslo_ref[1, f] for f in range(3)]
        syhi = [yshi_ref[0, f] for f in range(3)]
        cylo = lookup_planes(y_tables, yflo_ref[1, 3], count)
        cyhi = lookup_planes(y_tables, yfhi_ref[0, 3], count)

        def group(a, carry):
            y_f, y_l = carry
            acc = EdgeAcc(3, y_f, y_l)
            for b in range(ROWS):
                i = a * ROWS + b
                row = pl.ds(b, ROWS, stride=0)
                sxlo = [xslo_ref[f, a, row, :] for f in range(3)]
                sxhi = [xshi_ref[f, a, row, :] for f in range(3)]
                cxlo = [cx_s[f, a, row, :] for f in (0, 1)]
                cxhi = [cx_s[f, a, row, :] for f in (2, 3)]
                d = chunk * depth + i
                heat = h_ref[i]
                water = w_ref[i]
                carbon = c_ref[i]
                melt = m_ref[i]
                sill = sill_ref[i].astype(f32)
                cx = co_ref[0, i]
                cy = co_ref[1, i]
                vx = co_ref[2, i]
                vy = co_ref[3, i]
                mobile = [heat, water, carbon]
                q_xm = [x_minus(mobile[f], sxlo[f], b, sub) for f in range(3)]
                q_xp = [x_plus(mobile[f], sxhi[f], b, sub) for f in range(3)]
                q_ym = [y_minus(mobile[f], sylo[f], d, lane) for f in range(3)]
                q_yp = [y_plus(mobile[f], syhi[f], d, lane) for f in range(3)]
                cx_m = x_minus(cx, cxlo[0], b, sub)
                cx_p = x_plus(cx, cxhi[0], b, sub)
                vx_m = x_minus(vx, cxlo[1], b, sub)
                vx_p = x_plus(vx, cxhi[1], b, sub)
                cy_m = y_minus(cy, cylo[0], d, lane)
                cy_p = y_plus(cy, cyhi[0], d, lane)
                vy_m = y_minus(vy, cylo[1], d, lane)
                vy_p = y_plus(vy, cyhi[1], d, lane)
                soft = jnp.exp(-SOFTEN * heat)
                kx = cx * soft
                ky = cy * soft
                kx_m = cx_m * jnp.exp(-SOFTEN * q_xm[0])
                kx_p = cx_p * jnp.exp(-SOFTEN * q_xp[0])
                ky_m = cy_m * jnp.exp(-SOFTEN * q_ym[0])
                ky_p = cy_p * jnp.exp(-SOFTEN * q_yp[0])
                flux_x_lo = 0.5 * (kx_m + kx) * (heat - q_xm[0])
                flux_x_hi = 0.5 * (kx + kx_p) * (q_xp[0] - heat)
                flux_y_lo = 0.5 * (ky_m + ky) * (heat - q_ym[0])
                flux_y_hi = 0.5 * (ky + ky_p) * (q_yp[0] - heat)
                diffused = flux_x_hi - flux_x_lo + flux_y_hi - flux_y_lo
                fvx_m = 0.5 * (vx_m + vx)
                fvx_p = 0.5 * (vx + vx_p)
                fvy_m = 0.5 * (vy_m + vy)
                fvy_p = 0.5 * (vy + vy_p)
                inflow = []
                for f in range(3):
                    lo_x = jnp.maximum(fvx_m, 0.0) * q_xm[f] + jnp.minimum(fvx_m, 0.0) * mobile[f]
                    hi_x = jnp.maximum(fvx_p, 0.0) * mobile[f] + jnp.minimum(fvx_p, 0.0) * q_xp[f]
                    lo_y = jnp.maximum(fvy_m, 0.0) * q_ym[f] + jnp.minimum(fvy_m, 0.0) * mobile[f]
                    hi_y = jnp.maximum(fvy_p, 0.0) * mobile[f] + jnp.minimum(fvy_p, 0.0) * q_yp[f]
                    inflow.append(lo_x - hi_x + lo_y - hi_y)
                heat_one = heat + diffused + HEAT_CARRY * inflow[0]
                water_two = water + inflow[1] + sill * WATER_INPUT
                carbon_two = carbon + inflow[2] + sill * CARBON_INPUT
                heat_two = heat_one + sill * SILL_RATE * (SILL_HEAT - heat_one)
                z = MELT_SHARPNESS * (heat_two - SOLIDUS + DEPRESSION * water_two)
                target = 1.0 / (1.0 + jnp.exp(-z))
                melt_two = melt + MELT_RATE * (target - melt)
                heat_three = heat_two - LATENT * (melt_two - melt)
                ho_ref[i] = heat_three
                wo_ref[i] = water_two
                cbo_ref[i] = carbon_two
                mo_ref[i] = melt_two
                acc.add_y([heat_three, water_two, carbon_two], d, lane)
            planes = pl.ds(a * ROWS, ROWS)
            for f, out in enumerate((ho_ref, wo_ref, cbo_ref)):
                xf_ref[f, a] = out[planes, 0, :]
                xl_ref[f, a] = out[planes, ROWS - 1, :]
            return (tuple(acc.yf), tuple(acc.yl))

        y_f, y_l = lax.fori_loop(0, groups, group, ((zero,) * 3, (zero,) * 3))
        for f in range(3):
            y_ref[0, f] = y_f[f]
            y_ref[1, f] = y_l[f]

    return kernel


def sweep_kernel(r_ref, cz_ref, y_ref, a_ref, b_ref, red_ref, c_s, g_s, vy_s, va_s):
    n = r_ref.shape[0]
    zero = jnp.zeros(r_ref.shape[1:], f32)
    one = jnp.ones(r_ref.shape[1:], f32)

    def conduct(i, carry):
        c_s[i] = cz_ref[0, i] * jnp.exp(-SOFTEN * r_ref[i])
        return carry

    lax.fori_loop(0, n, conduct, 0)

    def forward(i, carry):
        g_prev, vy_prev, va_prev = carry
        up = 0.5 * (c_s[i - 1] + c_s[i])
        down = 0.5 * (c_s[i] + c_s[i + 1])
        inv = 1.0 / (1.0 + up + down - up * g_prev)
        g = down * inv
        vy = (r_ref[i] + up * vy_prev) * inv
        va = (up * va_prev) * inv
        g_s[i] = g
        vy_s[i] = vy
        va_s[i] = va
        return g, vy, va

    lax.fori_loop(1, n - 1, forward, (zero, zero, one))

    def backward(k, carry):
        i = n - 2 - k
        y_next, a_next, b_next = carry
        g = g_s[i]
        y = vy_s[i] + g * y_next
        a = va_s[i] + g * a_next
        b = g * b_next
        y_ref[i] = y
        a_ref[i] = a
        b_ref[i] = b
        return y, a, b

    lax.fori_loop(0, n - 2, backward, (zero, zero, one))
    y_ref[0] = zero
    a_ref[0] = one
    b_ref[0] = zero
    y_ref[n - 1] = zero
    a_ref[n - 1] = zero
    b_ref[n - 1] = one
    up_first = 0.5 * (c_s[0] + c_s[1])
    up_last = 0.5 * (c_s[n - 2] + c_s[n - 1])
    red_ref[0] = 1.0 + up_first * (1.0 - a_ref[1])
    red_ref[1] = up_first * b_ref[1]
    red_ref[2] = r_ref[0] + up_first * y_ref[1]
    red_ref[3] = 1.0 + up_last * (1.0 - b_ref[n - 2])
    red_ref[4] = up_last * a_ref[n - 2]
    red_ref[5] = r_ref[n - 1] + up_last * y_ref[n - 2]
    red_ref[6] = c_s[0]
    red_ref[7] = c_s[n - 1]


def reduced_solve(red_all):
    count = len(red_all)
    lower, diag, upper, side = [], [], [], []
    for j in range(count):
        p0, q0, s0, p1, q1, s1, c_first, c_last = red_all[j]
        if j == 0:
            face = c_first
            lower.append(jnp.zeros_like(face))
        else:
            face = 0.5 * (red_all[j - 1][7] + c_first)
            lower.append(face)
        diag.append(p0 + face)
        upper.append(q0)
        side.append(s0)
        if j + 1 < count:
            below = 0.5 * (c_last + red_all[j + 1][6])
        else:
            below = jnp.zeros_like(c_last)
        lower.append(q1)
        diag.append(p1 + below)
        upper.append(below)
        side.append(s1)
    size = len(diag)
    ratios, values = [], []
    g_prev = jnp.zeros_like(diag[0])
    v_prev = jnp.zeros_like(diag[0])
    for k in range(size):
        inv = 1.0 / (diag[k] - lower[k] * g_prev)
        g_prev = upper[k] * inv
        v_prev = (side[k] + lower[k] * v_prev) * inv
        ratios.append(g_prev)
        values.append(v_prev)
    solved = [None] * size
    following = jnp.zeros_like(diag[0])
    for k in reversed(range(size)):
        following = values[k] + ratios[k] * following
        solved[k] = following
    return solved


def finish_kernel(rank_ref, y_ref, a_ref, b_ref, *rest):
    recv = rest[:-1]
    t_ref = rest[-1]
    count = len(recv)
    rank = rank_ref[0]
    red_all = []
    for j in range(count):
        source = (rank - j + count) % count
        planes = []
        for k in range(8):
            v = recv[count - 1][k]
            for m in reversed(range(count - 1)):
                v = jnp.where(source == m, recv[m][k], v)
            planes.append(v)
        red_all.append(planes)
    solved = reduced_solve(red_all)
    first = solved[2 * (count - 1)]
    last = solved[2 * (count - 1) + 1]
    for j in reversed(range(count - 1)):
        first = jnp.where(rank == j, solved[2 * j], first)
        last = jnp.where(rank == j, solved[2 * j + 1], last)

    def combine(i, carry):
        t_ref[i] = y_ref[i] + a_ref[i] * first + b_ref[i] * last
        return carry

    lax.fori_loop(0, y_ref.shape[0], combine, 0)


def sds(shape):
    return jax.ShapeDtypeStruct(shape, f32)


def exchange(xf, xl, ys):
    east_fwd, east_bwd = ring_perms("east")
    north_fwd, north_bwd = ring_perms("north")
    xlo = lax.ppermute(xl, "east", east_fwd)
    xhi = lax.ppermute(xf, "east", east_bwd)
    ylo = lax.ppermute(ys, "north", north_fwd)
    if lax.axis_size("north") == 2:
        yhi = ylo
    else:
        yhi = lax.ppermute(ys, "north", north_bwd)
    return xlo, xhi, ylo, yhi


def full_spec(shape):
    zeros = (0,) * len(shape)
    return pl.BlockSpec(shape, lambda i: zeros)


def local(
    thermal_field,
    liquid_fraction,
    steam_content_grid,
    carbonic_gas_grid,
    stratum_number_grid,
    injection_flags,
    lateral_transmissivity,
    vertical_transmissivity,
    stratum_advection_offsets,
):
    shape = thermal_field.shape
    n = shape[0]
    groups = n // ROWS
    assert shape[1:] == (ROWS, LANES) and n % ROWS == 0 and n <= LANES
    chunks = CHUNKS if groups % CHUNKS == 0 else 1
    depth = n // chunks
    cgroups = depth // ROWS
    smem_spec = pl.BlockSpec(memory_space=pltpu.SMEM)
    vspec = pl.BlockSpec(memory_space=pltpu.MemorySpace.VMEM)
    layer_f = stratum_number_grid.astype(f32)
    initial = (thermal_field, steam_content_grid, carbonic_gas_grid, layer_f)
    xf0 = jnp.stack([v[:, 0, :] for v in initial]).reshape(4, groups, ROWS, LANES)
    xl0 = jnp.stack([v[:, ROWS - 1, :] for v in initial]).reshape(4, groups, ROWS, LANES)
    cols = jnp.stack([jnp.stack([v[:, :, 0] for v in initial]),
                      jnp.stack([v[:, :, LANES - 1] for v in initial])])
    y0 = jnp.pad(jnp.swapaxes(cols, 2, 3), ((0, 0), (0, 0), (0, 0), (0, LANES - n)))
    xflo, xfhi, yflo, yfhi = exchange(xf0, xl0, y0)
    heat, water, carbon, melt, co = pl.pallas_call(
        prep_kernel,
        out_shape=(sds(shape), sds(shape), sds(shape), sds(shape), sds((5,) + shape)),
        in_specs=[smem_spec] * 3 + [vspec] * 5,
    )(lateral_transmissivity, vertical_transmissivity, stratum_advection_offsets, stratum_number_grid, thermal_field, steam_content_grid, carbonic_gas_grid,
      liquid_fraction)

    def block_spec(k):
        return pl.BlockSpec((depth, ROWS, LANES), lambda i: (k, 0, 0))

    halos = [None] * chunks
    for section_no in range(SECTIONS):
        first = section_no == 0
        for k in range(chunks):
            x4 = pl.BlockSpec((4, cgroups, ROWS, LANES), lambda i, k=k: (0, k, 0, 0))
            y4 = full_spec((2, 4, ROWS, LANES))
            in_specs = [smem_spec, smem_spec] + [block_spec(k)] * 5 + [
                pl.BlockSpec((4, depth, ROWS, LANES), lambda i, k=k: (0, k, 0, 0)),
                x4, x4, y4, y4,
            ]
            args = [lateral_transmissivity, stratum_advection_offsets,
                    heat, water, carbon, melt, injection_flags, co, xflo, xfhi, yflo, yfhi]
            if not first:
                in_specs += [full_spec((3, cgroups, ROWS, LANES))] * 2
                in_specs += [full_spec((2, 3, ROWS, LANES))] * 2
                args += list(halos[k])
            heat, water, carbon, melt, xf, xl, ys = pl.pallas_call(
                make_section_kernel(k, first),
                grid=(1,),
                out_shape=(sds(shape), sds(shape), sds(shape), sds(shape),
                           sds((3, cgroups, ROWS, LANES)), sds((3, cgroups, ROWS, LANES)),
                           sds((2, 3, ROWS, LANES))),
                in_specs=in_specs,
                out_specs=[block_spec(k)] * 4 + [
                    full_spec((3, cgroups, ROWS, LANES)), full_spec((3, cgroups, ROWS, LANES)),
                    full_spec((2, 3, ROWS, LANES)),
                ],
                input_output_aliases={2: 0, 3: 1, 4: 2, 5: 3},
                scratch_shapes=[pltpu.VMEM((4, cgroups, ROWS, LANES), f32)],
            )(*args)
            if section_no + 1 < SECTIONS:
                halos[k] = exchange(xf, xl, ys)

    y, a, b, red = pl.pallas_call(
        sweep_kernel,
        grid=(1,),
        out_shape=(sds(shape), sds(shape), sds(shape), sds((8,) + shape[1:])),
        in_specs=[full_spec(shape), pl.BlockSpec((1,) + shape, lambda i: (4, 0, 0, 0))],
        out_specs=[full_spec(shape)] * 3 + [full_spec((8,) + shape[1:])],
        scratch_shapes=[pltpu.VMEM(shape, f32)] * 4,
    )(heat, co)
    count = lax.axis_size("depth")
    rank = lax.axis_index("depth")
    received = [red]
    for k in range(1, count):
        received.append(lax.ppermute(red, "depth", [(i, (i + k) % count) for i in range(count)]))
    rank_arr = jnp.full((1,), rank, jnp.int32)
    heat_next = pl.pallas_call(
        finish_kernel,
        out_shape=sds(shape),
        in_specs=[smem_spec] + [vspec] * (3 + count),
    )(rank_arr, y, a, b, *received)
    return (heat_next, melt, water, carbon)


def solution(mesh):
    placed = (
        P("depth", "east", "north"),
        P("depth", "east", "north"),
        P("depth", "east", "north"),
        P("depth", "east", "north"),
        P("depth", "east", "north"),
        P("depth", "east", "north"),
        P(),
        P(),
        P(),
    )
    return jax.shard_map(
        local,
        mesh=mesh,
        in_specs=placed,
        out_specs=(
            P("depth", "east", "north"),
            P("depth", "east", "north"),
            P("depth", "east", "north"),
            P("depth", "east", "north"),
        ),
        check_vma=False,
    )
```

```python
import jax
import jax.numpy as jnp
from jax import lax
from jax.experimental import pallas as pl
from jax.experimental.pallas import tpu as pltpu
from jax.sharding import PartitionSpec as P

SECTIONS = 4


SOFTEN = 0.5
HEAT_CARRY = 0.5
SILL_RATE = 0.3
SILL_HEAT = 2.5
WATER_INPUT = 0.2
CARBON_INPUT = 0.1
MELT_SHARPNESS = 4.0
SOLIDUS = 1.0
DEPRESSION = 0.5
MELT_RATE = 0.5
LATENT = 0.3

ROWS = 8
CHUNKS = 2
LANES = 128
f32 = jnp.float32


def ring_perms(axis):
    count = lax.axis_size(axis)
    forward = [(i, (i + 1) % count) for i in range(count)]
    backward = [((i + 1) % count, i) for i in range(count)]
    return forward, backward


def iotas():
    sub = lax.broadcasted_iota(jnp.int32, (ROWS, LANES), 0)
    lane = lax.broadcasted_iota(jnp.int32, (ROWS, LANES), 1)
    return sub, lane


class EdgeAcc:
    def __init__(self, count, y_first, y_last):
        zero = jnp.zeros((ROWS, LANES), f32)
        self.xf = [zero] * count
        self.xl = [zero] * count
        self.yf = list(y_first)
        self.yl = list(y_last)

    def add_x(self, planes, b):
        at_b = lax.broadcasted_iota(jnp.int32, (ROWS, LANES), 0) == b
        for f, v in enumerate(planes):
            self.xf[f] = jnp.where(at_b, pltpu.roll(v, b, 0), self.xf[f])
            self.xl[f] = jnp.where(at_b, pltpu.roll(v, (b + 1) % ROWS, 0), self.xl[f])

    def add_y(self, planes, d, lane):
        at_d = lane == d
        for f, v in enumerate(planes):
            self.yf[f] = jnp.where(at_d, pltpu.roll(v, d % LANES, 1), self.yf[f])
            self.yl[f] = jnp.where(at_d, pltpu.roll(v, (d + 1) % LANES, 1), self.yl[f])


def x_minus(v, lo_row, b, sub):
    return jnp.where(sub == 0, lo_row, pltpu.roll(v, 1, 0))


def x_plus(v, hi_row, b, sub):
    return jnp.where(sub == ROWS - 1, hi_row, pltpu.roll(v, ROWS - 1, 0))


def y_minus(v, lo_cols, d, lane):
    return jnp.where(lane == 0, pltpu.roll(lo_cols, (LANES - d) % LANES, 1), pltpu.roll(v, 1, 1))


def y_plus(v, hi_cols, d, lane):
    return jnp.where(
        lane == LANES - 1,
        pltpu.roll(hi_cols, (LANES - 1 - d) % LANES, 1),
        pltpu.roll(v, LANES - 1, 1),
    )


def prep_kernel(lat_ref, vert_ref, adv_ref, layer_ref, h_ref, w_ref, c_ref, m_ref,
                ho_ref, wo_ref, cbo_ref, mo_ref, co_ref, xf_ref, xl_ref, y_ref):
    groups = layer_ref.shape[0] // ROWS
    layers_count = vert_ref.shape[0]
    sub, lane = iotas()
    zero = jnp.zeros((ROWS, LANES), f32)

    def group(a, carry):
        y_f, y_l = carry
        acc = EdgeAcc(5, y_f, y_l)
        for b in range(ROWS):
            d = a * ROWS + b
            layer = layer_ref[d]
            vals = [zero] * 5
            for l in range(layers_count):
                hit = layer == l
                entries = (lat_ref[0, l], lat_ref[1, l], adv_ref[0, l], adv_ref[1, l], vert_ref[l])
                vals = [jnp.where(hit, entries[k], vals[k]) for k in range(5)]
            for k in range(5):
                co_ref[k, d] = vals[k]
            heat, water, carbon = h_ref[d], w_ref[d], c_ref[d]
            ho_ref[d] = heat
            wo_ref[d] = water
            cbo_ref[d] = carbon
            mo_ref[d] = m_ref[d]
            acc.add_y([heat, water, carbon, vals[1], vals[3]], d, lane)
        planes = pl.ds(a * ROWS, ROWS)
        sources = ((ho_ref, None), (wo_ref, None), (cbo_ref, None), (co_ref, 0), (co_ref, 2))
        for f, (out, field) in enumerate(sources):
            if field is None:
                xf_ref[f, a] = out[planes, 0, :]
                xl_ref[f, a] = out[planes, ROWS - 1, :]
            else:
                xf_ref[f, a] = out[field, planes, 0, :]
                xl_ref[f, a] = out[field, planes, ROWS - 1, :]
        return (tuple(acc.yf), tuple(acc.yl))

    y_f, y_l = lax.fori_loop(0, groups, group, ((zero,) * 5, (zero,) * 5))
    for f in range(5):
        y_ref[0, f] = y_f[f]
        y_ref[1, f] = y_l[f]


def make_section_kernel(chunk, first):
    def kernel(h_ref, w_ref, c_ref, m_ref, sill_ref, co_ref, *rest):
        if first:
            xflo_ref, xfhi_ref, yflo_ref, yfhi_ref = rest[:4]
            ho_ref, wo_ref, cbo_ref, mo_ref, xf_ref, xl_ref, y_ref, nb_ref = rest[4:]
            xslo_ref, xshi_ref, yslo_ref, yshi_ref = xflo_ref, xfhi_ref, yflo_ref, yfhi_ref
            cylo = [yflo_ref[1, f] for f in (3, 4)]
            cyhi = [yfhi_ref[0, f] for f in (3, 4)]
        else:
            nb_ref, xslo_ref, xshi_ref, yslo_ref, yshi_ref = rest[:5]
            ho_ref, wo_ref, cbo_ref, mo_ref, xf_ref, xl_ref, y_ref = rest[5:]
        depth = h_ref.shape[0]
        groups = depth // ROWS
        sub, lane = iotas()
        zero = jnp.zeros((ROWS, LANES), f32)
        sylo = [yslo_ref[1, f] for f in range(3)]
        syhi = [yshi_ref[0, f] for f in range(3)]

        def group(a, carry):
            y_f, y_l = carry
            acc = EdgeAcc(3, y_f, y_l)
            for b in range(ROWS):
                i = a * ROWS + b
                row = pl.ds(b, ROWS, stride=0)
                sxlo = [xslo_ref[f, a, row, :] for f in range(3)]
                sxhi = [xshi_ref[f, a, row, :] for f in range(3)]
                d = chunk * depth + i
                heat = h_ref[i]
                water = w_ref[i]
                carbon = c_ref[i]
                melt = m_ref[i]
                sill = sill_ref[i].astype(f32)
                cx = co_ref[0, i]
                cy = co_ref[1, i]
                mobile = [heat, water, carbon]
                q_xm = [x_minus(mobile[f], sxlo[f], b, sub) for f in range(3)]
                q_xp = [x_plus(mobile[f], sxhi[f], b, sub) for f in range(3)]
                q_ym = [y_minus(mobile[f], sylo[f], d, lane) for f in range(3)]
                q_yp = [y_plus(mobile[f], syhi[f], d, lane) for f in range(3)]
                if first:
                    cxlo = [xflo_ref[f, a, row, :] for f in (3, 4)]
                    cxhi = [xfhi_ref[f, a, row, :] for f in (3, 4)]
                    vx = co_ref[2, i]
                    vy = co_ref[3, i]
                    cx_m = x_minus(cx, cxlo[0], b, sub)
                    cx_p = x_plus(cx, cxhi[0], b, sub)
                    vx_m = x_minus(vx, cxlo[1], b, sub)
                    vx_p = x_plus(vx, cxhi[1], b, sub)
                    cy_m = y_minus(cy, cylo[0], d, lane)
                    cy_p = y_plus(cy, cyhi[0], d, lane)
                    vy_m = y_minus(vy, cylo[1], d, lane)
                    vy_p = y_plus(vy, cyhi[1], d, lane)
                    fvx_m = 0.5 * (vx_m + vx)
                    fvx_p = 0.5 * (vx + vx_p)
                    fvy_m = 0.5 * (vy_m + vy)
                    fvy_p = 0.5 * (vy + vy_p)
                    near = (cx_m, cx_p, cy_m, cy_p, fvx_m, fvx_p, fvy_m, fvy_p)
                    for f, v in enumerate(near):
                        nb_ref[f, i] = v
                else:
                    cx_m, cx_p, cy_m, cy_p, fvx_m, fvx_p, fvy_m, fvy_p = [
                        nb_ref[f, i] for f in range(8)
                    ]
                soft = jnp.exp(-SOFTEN * heat)
                kx = cx * soft
                ky = cy * soft
                kx_m = cx_m * jnp.exp(-SOFTEN * q_xm[0])
                kx_p = cx_p * jnp.exp(-SOFTEN * q_xp[0])
                ky_m = cy_m * jnp.exp(-SOFTEN * q_ym[0])
                ky_p = cy_p * jnp.exp(-SOFTEN * q_yp[0])
                flux_x_lo = 0.5 * (kx_m + kx) * (heat - q_xm[0])
                flux_x_hi = 0.5 * (kx + kx_p) * (q_xp[0] - heat)
                flux_y_lo = 0.5 * (ky_m + ky) * (heat - q_ym[0])
                flux_y_hi = 0.5 * (ky + ky_p) * (q_yp[0] - heat)
                diffused = flux_x_hi - flux_x_lo + flux_y_hi - flux_y_lo
                inflow = []
                for f in range(3):
                    lo_x = jnp.maximum(fvx_m, 0.0) * q_xm[f] + jnp.minimum(fvx_m, 0.0) * mobile[f]
                    hi_x = jnp.maximum(fvx_p, 0.0) * mobile[f] + jnp.minimum(fvx_p, 0.0) * q_xp[f]
                    lo_y = jnp.maximum(fvy_m, 0.0) * q_ym[f] + jnp.minimum(fvy_m, 0.0) * mobile[f]
                    hi_y = jnp.maximum(fvy_p, 0.0) * mobile[f] + jnp.minimum(fvy_p, 0.0) * q_yp[f]
                    inflow.append(lo_x - hi_x + lo_y - hi_y)
                heat_one = heat + diffused + HEAT_CARRY * inflow[0]
                water_two = water + inflow[1] + sill * WATER_INPUT
                carbon_two = carbon + inflow[2] + sill * CARBON_INPUT
                heat_two = heat_one + sill * SILL_RATE * (SILL_HEAT - heat_one)
                z = MELT_SHARPNESS * (heat_two - SOLIDUS + DEPRESSION * water_two)
                target = 1.0 / (1.0 + jnp.exp(-z))
                melt_two = melt + MELT_RATE * (target - melt)
                heat_three = heat_two - LATENT * (melt_two - melt)
                ho_ref[i] = heat_three
                wo_ref[i] = water_two
                cbo_ref[i] = carbon_two
                mo_ref[i] = melt_two
                acc.add_y([heat_three, water_two, carbon_two], d, lane)
            planes = pl.ds(a * ROWS, ROWS)
            for f, out in enumerate((ho_ref, wo_ref, cbo_ref)):
                xf_ref[f, a] = out[planes, 0, :]
                xl_ref[f, a] = out[planes, ROWS - 1, :]
            return (tuple(acc.yf), tuple(acc.yl))

        y_f, y_l = lax.fori_loop(0, groups, group, ((zero,) * 3, (zero,) * 3))
        for f in range(3):
            y_ref[0, f] = y_f[f]
            y_ref[1, f] = y_l[f]

    return kernel


def sweep_kernel(r_ref, cz_ref, y_ref, a_ref, b_ref, red_ref, c_s, g_s, vy_s, va_s):
    n = r_ref.shape[0]
    zero = jnp.zeros(r_ref.shape[1:], f32)
    one = jnp.ones(r_ref.shape[1:], f32)

    def conduct(i, carry):
        c_s[i] = cz_ref[0, i] * jnp.exp(-SOFTEN * r_ref[i])
        return carry

    lax.fori_loop(0, n, conduct, 0)

    def forward(i, carry):
        g_prev, vy_prev, va_prev = carry
        up = 0.5 * (c_s[i - 1] + c_s[i])
        down = 0.5 * (c_s[i] + c_s[i + 1])
        inv = 1.0 / (1.0 + up + down - up * g_prev)
        g = down * inv
        vy = (r_ref[i] + up * vy_prev) * inv
        va = (up * va_prev) * inv
        g_s[i] = g
        vy_s[i] = vy
        va_s[i] = va
        return g, vy, va

    lax.fori_loop(1, n - 1, forward, (zero, zero, one))

    def backward(k, carry):
        i = n - 2 - k
        y_next, a_next, b_next = carry
        g = g_s[i]
        y = vy_s[i] + g * y_next
        a = va_s[i] + g * a_next
        b = g * b_next
        y_ref[i] = y
        a_ref[i] = a
        b_ref[i] = b
        return y, a, b

    lax.fori_loop(0, n - 2, backward, (zero, zero, one))
    y_ref[0] = zero
    a_ref[0] = one
    b_ref[0] = zero
    y_ref[n - 1] = zero
    a_ref[n - 1] = zero
    b_ref[n - 1] = one
    up_first = 0.5 * (c_s[0] + c_s[1])
    up_last = 0.5 * (c_s[n - 2] + c_s[n - 1])
    red_ref[0] = 1.0 + up_first * (1.0 - a_ref[1])
    red_ref[1] = up_first * b_ref[1]
    red_ref[2] = r_ref[0] + up_first * y_ref[1]
    red_ref[3] = 1.0 + up_last * (1.0 - b_ref[n - 2])
    red_ref[4] = up_last * a_ref[n - 2]
    red_ref[5] = r_ref[n - 1] + up_last * y_ref[n - 2]
    red_ref[6] = c_s[0]
    red_ref[7] = c_s[n - 1]


def reduced_solve(red_all):
    count = len(red_all)
    lower, diag, upper, side = [], [], [], []
    for j in range(count):
        p0, q0, s0, p1, q1, s1, c_first, c_last = red_all[j]
        if j == 0:
            face = c_first
            lower.append(jnp.zeros_like(face))
        else:
            face = 0.5 * (red_all[j - 1][7] + c_first)
            lower.append(face)
        diag.append(p0 + face)
        upper.append(q0)
        side.append(s0)
        if j + 1 < count:
            below = 0.5 * (c_last + red_all[j + 1][6])
        else:
            below = jnp.zeros_like(c_last)
        lower.append(q1)
        diag.append(p1 + below)
        upper.append(below)
        side.append(s1)
    size = len(diag)
    ratios, values = [], []
    g_prev = jnp.zeros_like(diag[0])
    v_prev = jnp.zeros_like(diag[0])
    for k in range(size):
        inv = 1.0 / (diag[k] - lower[k] * g_prev)
        g_prev = upper[k] * inv
        v_prev = (side[k] + lower[k] * v_prev) * inv
        ratios.append(g_prev)
        values.append(v_prev)
    solved = [None] * size
    following = jnp.zeros_like(diag[0])
    for k in reversed(range(size)):
        following = values[k] + ratios[k] * following
        solved[k] = following
    return solved


def finish_kernel(rank_ref, y_ref, a_ref, b_ref, *rest):
    recv = rest[:-1]
    t_ref = rest[-1]
    count = len(recv)
    rank = rank_ref[0]
    red_all = []
    for j in range(count):
        source = (rank - j + count) % count
        planes = []
        for k in range(8):
            v = recv[count - 1][k]
            for m in reversed(range(count - 1)):
                v = jnp.where(source == m, recv[m][k], v)
            planes.append(v)
        red_all.append(planes)
    solved = reduced_solve(red_all)
    first = solved[2 * (count - 1)]
    last = solved[2 * (count - 1) + 1]
    for j in reversed(range(count - 1)):
        first = jnp.where(rank == j, solved[2 * j], first)
        last = jnp.where(rank == j, solved[2 * j + 1], last)

    def combine(i, carry):
        t_ref[i] = y_ref[i] + a_ref[i] * first + b_ref[i] * last
        return carry

    lax.fori_loop(0, y_ref.shape[0], combine, 0)


def sds(shape):
    return jax.ShapeDtypeStruct(shape, f32)


def exchange(xf, xl, ys):
    east_fwd, east_bwd = ring_perms("east")
    north_fwd, north_bwd = ring_perms("north")
    xlo = lax.ppermute(xl, "east", east_fwd)
    xhi = lax.ppermute(xf, "east", east_bwd)
    ylo = lax.ppermute(ys, "north", north_fwd)
    if lax.axis_size("north") == 2:
        yhi = ylo
    else:
        yhi = lax.ppermute(ys, "north", north_bwd)
    return xlo, xhi, ylo, yhi


def full_spec(shape):
    zeros = (0,) * len(shape)
    return pl.BlockSpec(shape, lambda i: zeros)


def local(
    thermal_field,
    liquid_fraction,
    steam_content_grid,
    carbonic_gas_grid,
    stratum_number_grid,
    injection_flags,
    lateral_transmissivity,
    vertical_transmissivity,
    stratum_advection_offsets,
):
    shape = thermal_field.shape
    n = shape[0]
    groups = n // ROWS
    assert shape[1:] == (ROWS, LANES) and n % ROWS == 0 and n <= LANES
    chunks = CHUNKS if groups % CHUNKS == 0 else 1
    depth = n // chunks
    cgroups = depth // ROWS
    smem_spec = pl.BlockSpec(memory_space=pltpu.SMEM)
    vspec = pl.BlockSpec(memory_space=pltpu.MemorySpace.VMEM)
    heat, water, carbon, melt, co, xf0, xl0, y0 = pl.pallas_call(
        prep_kernel,
        out_shape=(sds(shape), sds(shape), sds(shape), sds(shape), sds((5,) + shape),
                   sds((5, groups, ROWS, LANES)), sds((5, groups, ROWS, LANES)),
                   sds((2, 5, ROWS, LANES))),
        in_specs=[smem_spec] * 3 + [vspec] * 5,
    )(lateral_transmissivity, vertical_transmissivity, stratum_advection_offsets, stratum_number_grid, thermal_field, steam_content_grid, carbonic_gas_grid,
      liquid_fraction)
    xflo, xfhi, yflo, yfhi = exchange(xf0, xl0, y0)

    def block_spec(k):
        return pl.BlockSpec((depth, ROWS, LANES), lambda i: (k, 0, 0))

    halos = [None] * chunks
    nears = [None] * chunks
    x3 = full_spec((3, cgroups, ROWS, LANES))
    y3 = full_spec((2, 3, ROWS, LANES))
    near_spec = full_spec((8, depth, ROWS, LANES))
    for section_no in range(SECTIONS):
        first = section_no == 0
        for k in range(chunks):
            args = [heat, water, carbon, melt, injection_flags, co]
            in_specs = [block_spec(k)] * 5
            out_shape = [sds(shape)] * 4 + [sds((3, cgroups, ROWS, LANES))] * 2
            out_shape += [sds((2, 3, ROWS, LANES))]
            out_specs = [block_spec(k)] * 4 + [x3, x3, y3]
            if first:
                x5 = pl.BlockSpec((5, cgroups, ROWS, LANES), lambda i, k=k: (0, k, 0, 0))
                y5 = full_spec((2, 5, ROWS, LANES))
                in_specs += [pl.BlockSpec((4, depth, ROWS, LANES), lambda i, k=k: (0, k, 0, 0)),
                             x5, x5, y5, y5]
                args += [xflo, xfhi, yflo, yfhi]
                out_shape += [sds((8, depth, ROWS, LANES))]
                out_specs += [near_spec]
            else:
                in_specs += [pl.BlockSpec((2, depth, ROWS, LANES), lambda i, k=k: (0, k, 0, 0)),
                             near_spec, x3, x3, y3, y3]
                args += [nears[k]] + list(halos[k])
            outs = pl.pallas_call(
                make_section_kernel(k, first),
                grid=(1,),
                out_shape=tuple(out_shape),
                in_specs=in_specs,
                out_specs=out_specs,
                input_output_aliases={0: 0, 1: 1, 2: 2, 3: 3},
            )(*args)
            heat, water, carbon, melt, xf, xl, ys = outs[:7]
            if first:
                nears[k] = outs[7]
            if section_no + 1 < SECTIONS:
                halos[k] = exchange(xf, xl, ys)

    y, a, b, red = pl.pallas_call(
        sweep_kernel,
        grid=(1,),
        out_shape=(sds(shape), sds(shape), sds(shape), sds((8,) + shape[1:])),
        in_specs=[full_spec(shape), pl.BlockSpec((1,) + shape, lambda i: (4, 0, 0, 0))],
        out_specs=[full_spec(shape)] * 3 + [full_spec((8,) + shape[1:])],
        scratch_shapes=[pltpu.VMEM(shape, f32)] * 4,
    )(heat, co)
    count = lax.axis_size("depth")
    rank = lax.axis_index("depth")
    received = [red]
    for k in range(1, count):
        received.append(lax.ppermute(red, "depth", [(i, (i + k) % count) for i in range(count)]))
    rank_arr = jnp.full((1,), rank, jnp.int32)
    heat_next = pl.pallas_call(
        finish_kernel,
        out_shape=sds(shape),
        in_specs=[smem_spec] + [vspec] * (3 + count),
    )(rank_arr, y, a, b, *received)
    return (heat_next, melt, water, carbon)


def solution(mesh):
    placed = (
        P("depth", "east", "north"),
        P("depth", "east", "north"),
        P("depth", "east", "north"),
        P("depth", "east", "north"),
        P("depth", "east", "north"),
        P("depth", "east", "north"),
        P(),
        P(),
        P(),
    )
    return jax.shard_map(
        local,
        mesh=mesh,
        in_specs=placed,
        out_specs=(
            P("depth", "east", "north"),
            P("depth", "east", "north"),
            P("depth", "east", "north"),
            P("depth", "east", "north"),
        ),
        check_vma=False,
    )
```

```python
import jax
import jax.numpy as jnp
from jax import lax
from jax.experimental import pallas as pl
from jax.experimental.pallas import tpu as pltpu
from jax.sharding import PartitionSpec as P

SECTIONS = 4


SOFTEN = 0.5
HEAT_CARRY = 0.5
SILL_RATE = 0.3
SILL_HEAT = 2.5
WATER_INPUT = 0.2
CARBON_INPUT = 0.1
MELT_SHARPNESS = 4.0
SOLIDUS = 1.0
DEPRESSION = 0.5
MELT_RATE = 0.5
LATENT = 0.3

ROWS = 8
CHUNKS = 2
LANES = 128
f32 = jnp.float32


def ring_perms(axis):
    count = lax.axis_size(axis)
    forward = [(i, (i + 1) % count) for i in range(count)]
    backward = [((i + 1) % count, i) for i in range(count)]
    return forward, backward


def iotas():
    sub = lax.broadcasted_iota(jnp.int32, (ROWS, LANES), 0)
    lane = lax.broadcasted_iota(jnp.int32, (ROWS, LANES), 1)
    return sub, lane


class EdgeAcc:
    def __init__(self, count, y_first, y_last):
        zero = jnp.zeros((ROWS, LANES), f32)
        self.xf = [zero] * count
        self.xl = [zero] * count
        self.yf = list(y_first)
        self.yl = list(y_last)

    def add_x(self, planes, b):
        at_b = lax.broadcasted_iota(jnp.int32, (ROWS, LANES), 0) == b
        for f, v in enumerate(planes):
            self.xf[f] = jnp.where(at_b, pltpu.roll(v, b, 0), self.xf[f])
            self.xl[f] = jnp.where(at_b, pltpu.roll(v, (b + 1) % ROWS, 0), self.xl[f])

    def add_y(self, planes, d, lane):
        at_d = lane == d
        for f, v in enumerate(planes):
            self.yf[f] = jnp.where(at_d, pltpu.roll(v, d % LANES, 1), self.yf[f])
            self.yl[f] = jnp.where(at_d, pltpu.roll(v, (d + 1) % LANES, 1), self.yl[f])


def x_minus(v, lo_row, b, sub):
    return jnp.where(sub == 0, lo_row, pltpu.roll(v, 1, 0))


def x_plus(v, hi_row, b, sub):
    return jnp.where(sub == ROWS - 1, hi_row, pltpu.roll(v, ROWS - 1, 0))


def y_minus(v, lo_cols, d, lane):
    return jnp.where(lane == 0, pltpu.roll(lo_cols, (LANES - d) % LANES, 1), pltpu.roll(v, 1, 1))


def y_plus(v, hi_cols, d, lane):
    return jnp.where(
        lane == LANES - 1,
        pltpu.roll(hi_cols, (LANES - 1 - d) % LANES, 1),
        pltpu.roll(v, LANES - 1, 1),
    )


def prep_kernel(lat_ref, vert_ref, adv_ref, layer_ref, h_ref, w_ref, c_ref, m_ref,
                ho_ref, wo_ref, cbo_ref, mo_ref, co_ref, xf_ref, xl_ref, y_ref):
    groups = layer_ref.shape[0] // ROWS
    layers_count = vert_ref.shape[0]
    sub, lane = iotas()
    zero = jnp.zeros((ROWS, LANES), f32)

    def group(a, carry):
        y_f, y_l = carry
        acc = EdgeAcc(5, y_f, y_l)
        for b in range(ROWS):
            d = a * ROWS + b
            layer = layer_ref[d]
            vals = [zero] * 5
            for l in range(layers_count):
                hit = layer == l
                entries = (lat_ref[0, l], lat_ref[1, l], adv_ref[0, l], adv_ref[1, l], vert_ref[l])
                vals = [jnp.where(hit, entries[k], vals[k]) for k in range(5)]
            vals[0] = 0.5 * vals[0]
            vals[1] = 0.5 * vals[1]
            for k in range(5):
                co_ref[k, d] = vals[k]
            heat, water, carbon = h_ref[d], w_ref[d], c_ref[d]
            ho_ref[d] = heat
            wo_ref[d] = water
            cbo_ref[d] = carbon
            mo_ref[d] = m_ref[d]
            acc.add_y([heat, water, carbon, vals[1], vals[3]], d, lane)
        planes = pl.ds(a * ROWS, ROWS)
        sources = ((ho_ref, None), (wo_ref, None), (cbo_ref, None), (co_ref, 0), (co_ref, 2))
        for f, (out, field) in enumerate(sources):
            if field is None:
                xf_ref[f, a] = out[planes, 0, :]
                xl_ref[f, a] = out[planes, ROWS - 1, :]
            else:
                xf_ref[f, a] = out[field, planes, 0, :]
                xl_ref[f, a] = out[field, planes, ROWS - 1, :]
        return (tuple(acc.yf), tuple(acc.yl))

    y_f, y_l = lax.fori_loop(0, groups, group, ((zero,) * 5, (zero,) * 5))
    for f in range(5):
        y_ref[0, f] = y_f[f]
        y_ref[1, f] = y_l[f]


def make_section_kernel(chunk, first):
    def kernel(h_ref, w_ref, c_ref, m_ref, sill_ref, co_ref, *rest):
        if first:
            xflo_ref, xfhi_ref, yflo_ref, yfhi_ref = rest[:4]
            ho_ref, wo_ref, cbo_ref, mo_ref, xf_ref, xl_ref, y_ref, nb_ref = rest[4:]
            xslo_ref, xshi_ref, yslo_ref, yshi_ref = xflo_ref, xfhi_ref, yflo_ref, yfhi_ref
            cylo = [yflo_ref[1, f] for f in (3, 4)]
            cyhi = [yfhi_ref[0, f] for f in (3, 4)]
        else:
            nb_ref, xslo_ref, xshi_ref, yslo_ref, yshi_ref = rest[:5]
            ho_ref, wo_ref, cbo_ref, mo_ref, xf_ref, xl_ref, y_ref = rest[5:]
        depth = h_ref.shape[0]
        groups = depth // ROWS
        sub, lane = iotas()
        zero = jnp.zeros((ROWS, LANES), f32)
        sylo = [yslo_ref[1, f] for f in range(3)]
        syhi = [yshi_ref[0, f] for f in range(3)]

        def group(a, carry):
            y_f, y_l = carry
            acc = EdgeAcc(3, y_f, y_l)
            for b in range(ROWS):
                i = a * ROWS + b
                row = pl.ds(b, ROWS, stride=0)
                sxlo = [xslo_ref[f, a, row, :] for f in range(3)]
                sxhi = [xshi_ref[f, a, row, :] for f in range(3)]
                d = chunk * depth + i
                heat = h_ref[i]
                water = w_ref[i]
                carbon = c_ref[i]
                melt = m_ref[i]
                sill = sill_ref[i].astype(f32)
                cx = co_ref[0, i]
                cy = co_ref[1, i]
                mobile = [heat, water, carbon]
                q_xm = [x_minus(mobile[f], sxlo[f], b, sub) for f in range(3)]
                q_xp = [x_plus(mobile[f], sxhi[f], b, sub) for f in range(3)]
                q_ym = [y_minus(mobile[f], sylo[f], d, lane) for f in range(3)]
                q_yp = [y_plus(mobile[f], syhi[f], d, lane) for f in range(3)]
                if first:
                    cxlo = [xflo_ref[f, a, row, :] for f in (3, 4)]
                    cxhi = [xfhi_ref[f, a, row, :] for f in (3, 4)]
                    vx = co_ref[2, i]
                    vy = co_ref[3, i]
                    cx_m = x_minus(cx, cxlo[0], b, sub)
                    cx_p = x_plus(cx, cxhi[0], b, sub)
                    vx_m = x_minus(vx, cxlo[1], b, sub)
                    vx_p = x_plus(vx, cxhi[1], b, sub)
                    cy_m = y_minus(cy, cylo[0], d, lane)
                    cy_p = y_plus(cy, cyhi[0], d, lane)
                    vy_m = y_minus(vy, cylo[1], d, lane)
                    vy_p = y_plus(vy, cyhi[1], d, lane)
                    fvx_m = 0.5 * (vx_m + vx)
                    fvx_p = 0.5 * (vx + vx_p)
                    fvy_m = 0.5 * (vy_m + vy)
                    fvy_p = 0.5 * (vy + vy_p)
                    near = (cx_m, cx_p, cy_m, cy_p, fvx_m, fvx_p, fvy_m, fvy_p)
                    for f, v in enumerate(near):
                        nb_ref[f, i] = v
                else:
                    cx_m, cx_p, cy_m, cy_p, fvx_m, fvx_p, fvy_m, fvy_p = [
                        nb_ref[f, i] for f in range(8)
                    ]
                soft = jnp.exp(-SOFTEN * heat)
                kx = cx * soft
                ky = cy * soft
                kx_m = cx_m * jnp.exp(-SOFTEN * q_xm[0])
                kx_p = cx_p * jnp.exp(-SOFTEN * q_xp[0])
                ky_m = cy_m * jnp.exp(-SOFTEN * q_ym[0])
                ky_p = cy_p * jnp.exp(-SOFTEN * q_yp[0])
                flux_x_lo = (kx_m + kx) * (heat - q_xm[0])
                flux_x_hi = (kx + kx_p) * (q_xp[0] - heat)
                flux_y_lo = (ky_m + ky) * (heat - q_ym[0])
                flux_y_hi = (ky + ky_p) * (q_yp[0] - heat)
                diffused = flux_x_hi - flux_x_lo + flux_y_hi - flux_y_lo
                inflow = []
                for f in range(3):
                    lo_x = jnp.maximum(fvx_m, 0.0) * q_xm[f] + jnp.minimum(fvx_m, 0.0) * mobile[f]
                    hi_x = jnp.maximum(fvx_p, 0.0) * mobile[f] + jnp.minimum(fvx_p, 0.0) * q_xp[f]
                    lo_y = jnp.maximum(fvy_m, 0.0) * q_ym[f] + jnp.minimum(fvy_m, 0.0) * mobile[f]
                    hi_y = jnp.maximum(fvy_p, 0.0) * mobile[f] + jnp.minimum(fvy_p, 0.0) * q_yp[f]
                    inflow.append(lo_x - hi_x + lo_y - hi_y)
                heat_one = heat + diffused + HEAT_CARRY * inflow[0]
                water_two = water + inflow[1] + sill * WATER_INPUT
                carbon_two = carbon + inflow[2] + sill * CARBON_INPUT
                heat_two = heat_one + sill * SILL_RATE * (SILL_HEAT - heat_one)
                z = MELT_SHARPNESS * (heat_two - SOLIDUS + DEPRESSION * water_two)
                target = 1.0 / (1.0 + jnp.exp(-z))
                melt_two = melt + MELT_RATE * (target - melt)
                heat_three = heat_two - LATENT * (melt_two - melt)
                ho_ref[i] = heat_three
                wo_ref[i] = water_two
                cbo_ref[i] = carbon_two
                mo_ref[i] = melt_two
                acc.add_y([heat_three, water_two, carbon_two], d, lane)
            planes = pl.ds(a * ROWS, ROWS)
            for f, out in enumerate((ho_ref, wo_ref, cbo_ref)):
                xf_ref[f, a] = out[planes, 0, :]
                xl_ref[f, a] = out[planes, ROWS - 1, :]
            return (tuple(acc.yf), tuple(acc.yl))

        y_f, y_l = lax.fori_loop(0, groups, group, ((zero,) * 3, (zero,) * 3))
        for f in range(3):
            y_ref[0, f] = y_f[f]
            y_ref[1, f] = y_l[f]

    return kernel


def sweep_kernel(r_ref, cz_ref, y_ref, a_ref, b_ref, red_ref, c_s, g_s, vy_s, va_s):
    n = r_ref.shape[0]
    zero = jnp.zeros(r_ref.shape[1:], f32)
    one = jnp.ones(r_ref.shape[1:], f32)

    def conduct(i, carry):
        c_s[i] = cz_ref[0, i] * jnp.exp(-SOFTEN * r_ref[i])
        return carry

    lax.fori_loop(0, n, conduct, 0)

    def forward(i, carry):
        g_prev, vy_prev, va_prev = carry
        up = 0.5 * (c_s[i - 1] + c_s[i])
        down = 0.5 * (c_s[i] + c_s[i + 1])
        inv = 1.0 / (1.0 + up + down - up * g_prev)
        g = down * inv
        vy = (r_ref[i] + up * vy_prev) * inv
        va = (up * va_prev) * inv
        g_s[i] = g
        vy_s[i] = vy
        va_s[i] = va
        return g, vy, va

    lax.fori_loop(1, n - 1, forward, (zero, zero, one))

    def backward(k, carry):
        i = n - 2 - k
        y_next, a_next, b_next = carry
        g = g_s[i]
        y = vy_s[i] + g * y_next
        a = va_s[i] + g * a_next
        b = g * b_next
        y_ref[i] = y
        a_ref[i] = a
        b_ref[i] = b
        return y, a, b

    lax.fori_loop(0, n - 2, backward, (zero, zero, one))
    y_ref[0] = zero
    a_ref[0] = one
    b_ref[0] = zero
    y_ref[n - 1] = zero
    a_ref[n - 1] = zero
    b_ref[n - 1] = one
    up_first = 0.5 * (c_s[0] + c_s[1])
    up_last = 0.5 * (c_s[n - 2] + c_s[n - 1])
    red_ref[0] = 1.0 + up_first * (1.0 - a_ref[1])
    red_ref[1] = up_first * b_ref[1]
    red_ref[2] = r_ref[0] + up_first * y_ref[1]
    red_ref[3] = 1.0 + up_last * (1.0 - b_ref[n - 2])
    red_ref[4] = up_last * a_ref[n - 2]
    red_ref[5] = r_ref[n - 1] + up_last * y_ref[n - 2]
    red_ref[6] = c_s[0]
    red_ref[7] = c_s[n - 1]


def reduced_solve(red_all):
    count = len(red_all)
    lower, diag, upper, side = [], [], [], []
    for j in range(count):
        p0, q0, s0, p1, q1, s1, c_first, c_last = red_all[j]
        if j == 0:
            face = c_first
            lower.append(jnp.zeros_like(face))
        else:
            face = 0.5 * (red_all[j - 1][7] + c_first)
            lower.append(face)
        diag.append(p0 + face)
        upper.append(q0)
        side.append(s0)
        if j + 1 < count:
            below = 0.5 * (c_last + red_all[j + 1][6])
        else:
            below = jnp.zeros_like(c_last)
        lower.append(q1)
        diag.append(p1 + below)
        upper.append(below)
        side.append(s1)
    size = len(diag)
    ratios, values = [], []
    g_prev = jnp.zeros_like(diag[0])
    v_prev = jnp.zeros_like(diag[0])
    for k in range(size):
        inv = 1.0 / (diag[k] - lower[k] * g_prev)
        g_prev = upper[k] * inv
        v_prev = (side[k] + lower[k] * v_prev) * inv
        ratios.append(g_prev)
        values.append(v_prev)
    solved = [None] * size
    following = jnp.zeros_like(diag[0])
    for k in reversed(range(size)):
        following = values[k] + ratios[k] * following
        solved[k] = following
    return solved


def finish_kernel(rank_ref, y_ref, a_ref, b_ref, *rest):
    recv = rest[:-1]
    t_ref = rest[-1]
    count = len(recv)
    rank = rank_ref[0]
    red_all = []
    for j in range(count):
        source = (rank - j + count) % count
        planes = []
        for k in range(8):
            v = recv[count - 1][k]
            for m in reversed(range(count - 1)):
                v = jnp.where(source == m, recv[m][k], v)
            planes.append(v)
        red_all.append(planes)
    solved = reduced_solve(red_all)
    first = solved[2 * (count - 1)]
    last = solved[2 * (count - 1) + 1]
    for j in reversed(range(count - 1)):
        first = jnp.where(rank == j, solved[2 * j], first)
        last = jnp.where(rank == j, solved[2 * j + 1], last)

    def combine(i, carry):
        t_ref[i] = y_ref[i] + a_ref[i] * first + b_ref[i] * last
        return carry

    lax.fori_loop(0, y_ref.shape[0], combine, 0)


def sds(shape):
    return jax.ShapeDtypeStruct(shape, f32)


def exchange(xf, xl, ys):
    east_fwd, east_bwd = ring_perms("east")
    north_fwd, north_bwd = ring_perms("north")
    xlo = lax.ppermute(xl, "east", east_fwd)
    xhi = lax.ppermute(xf, "east", east_bwd)
    ylo = lax.ppermute(ys, "north", north_fwd)
    if lax.axis_size("north") == 2:
        yhi = ylo
    else:
        yhi = lax.ppermute(ys, "north", north_bwd)
    return xlo, xhi, ylo, yhi


def full_spec(shape):
    zeros = (0,) * len(shape)
    return pl.BlockSpec(shape, lambda i: zeros)


def local(
    thermal_field,
    liquid_fraction,
    steam_content_grid,
    carbonic_gas_grid,
    stratum_number_grid,
    injection_flags,
    lateral_transmissivity,
    vertical_transmissivity,
    stratum_advection_offsets,
):
    shape = thermal_field.shape
    n = shape[0]
    groups = n // ROWS
    assert shape[1:] == (ROWS, LANES) and n % ROWS == 0 and n <= LANES
    chunks = CHUNKS if groups % CHUNKS == 0 else 1
    depth = n // chunks
    cgroups = depth // ROWS
    smem_spec = pl.BlockSpec(memory_space=pltpu.SMEM)
    vspec = pl.BlockSpec(memory_space=pltpu.MemorySpace.VMEM)
    heat, water, carbon, melt, co, xf0, xl0, y0 = pl.pallas_call(
        prep_kernel,
        out_shape=(sds(shape), sds(shape), sds(shape), sds(shape), sds((5,) + shape),
                   sds((5, groups, ROWS, LANES)), sds((5, groups, ROWS, LANES)),
                   sds((2, 5, ROWS, LANES))),
        in_specs=[smem_spec] * 3 + [vspec] * 5,
    )(lateral_transmissivity, vertical_transmissivity, stratum_advection_offsets, stratum_number_grid, thermal_field, steam_content_grid, carbonic_gas_grid,
      liquid_fraction)
    xflo, xfhi, yflo, yfhi = exchange(xf0, xl0, y0)

    def block_spec(k):
        return pl.BlockSpec((depth, ROWS, LANES), lambda i: (k, 0, 0))

    halos = [None] * chunks
    nears = [None] * chunks
    x3 = full_spec((3, cgroups, ROWS, LANES))
    y3 = full_spec((2, 3, ROWS, LANES))
    near_spec = full_spec((8, depth, ROWS, LANES))
    for section_no in range(SECTIONS):
        first = section_no == 0
        for k in range(chunks):
            args = [heat, water, carbon, melt, injection_flags, co]
            in_specs = [block_spec(k)] * 5
            out_shape = [sds(shape)] * 4 + [sds((3, cgroups, ROWS, LANES))] * 2
            out_shape += [sds((2, 3, ROWS, LANES))]
            out_specs = [block_spec(k)] * 4 + [x3, x3, y3]
            if first:
                x5 = pl.BlockSpec((5, cgroups, ROWS, LANES), lambda i, k=k: (0, k, 0, 0))
                y5 = full_spec((2, 5, ROWS, LANES))
                in_specs += [pl.BlockSpec((4, depth, ROWS, LANES), lambda i, k=k: (0, k, 0, 0)),
                             x5, x5, y5, y5]
                args += [xflo, xfhi, yflo, yfhi]
                out_shape += [sds((8, depth, ROWS, LANES))]
                out_specs += [near_spec]
            else:
                in_specs += [pl.BlockSpec((2, depth, ROWS, LANES), lambda i, k=k: (0, k, 0, 0)),
                             near_spec, x3, x3, y3, y3]
                args += [nears[k]] + list(halos[k])
            outs = pl.pallas_call(
                make_section_kernel(k, first),
                grid=(1,),
                out_shape=tuple(out_shape),
                in_specs=in_specs,
                out_specs=out_specs,
                input_output_aliases={0: 0, 1: 1, 2: 2, 3: 3},
            )(*args)
            heat, water, carbon, melt, xf, xl, ys = outs[:7]
            if first:
                nears[k] = outs[7]
            if section_no + 1 < SECTIONS:
                halos[k] = exchange(xf, xl, ys)

    y, a, b, red = pl.pallas_call(
        sweep_kernel,
        grid=(1,),
        out_shape=(sds(shape), sds(shape), sds(shape), sds((8,) + shape[1:])),
        in_specs=[full_spec(shape), pl.BlockSpec((1,) + shape, lambda i: (4, 0, 0, 0))],
        out_specs=[full_spec(shape)] * 3 + [full_spec((8,) + shape[1:])],
        scratch_shapes=[pltpu.VMEM(shape, f32)] * 4,
    )(heat, co)
    count = lax.axis_size("depth")
    rank = lax.axis_index("depth")
    received = [red]
    for k in range(1, count):
        received.append(lax.ppermute(red, "depth", [(i, (i + k) % count) for i in range(count)]))
    rank_arr = jnp.full((1,), rank, jnp.int32)
    heat_next = pl.pallas_call(
        finish_kernel,
        out_shape=sds(shape),
        in_specs=[smem_spec] + [vspec] * (3 + count),
    )(rank_arr, y, a, b, *received)
    return (heat_next, melt, water, carbon)


def solution(mesh):
    placed = (
        P("depth", "east", "north"),
        P("depth", "east", "north"),
        P("depth", "east", "north"),
        P("depth", "east", "north"),
        P("depth", "east", "north"),
        P("depth", "east", "north"),
        P(),
        P(),
        P(),
    )
    return jax.shard_map(
        local,
        mesh=mesh,
        in_specs=placed,
        out_specs=(
            P("depth", "east", "north"),
            P("depth", "east", "north"),
            P("depth", "east", "north"),
            P("depth", "east", "north"),
        ),
        check_vma=False,
    )
```

```python
import jax
import jax.numpy as jnp
from jax import lax
from jax.experimental import pallas as pl
from jax.experimental.pallas import tpu as pltpu
from jax.sharding import PartitionSpec as P

SECTIONS = 4


SOFTEN = 0.5
HEAT_CARRY = 0.5
SILL_RATE = 0.3
SILL_HEAT = 2.5
WATER_INPUT = 0.2
CARBON_INPUT = 0.1
MELT_SHARPNESS = 4.0
SOLIDUS = 1.0
DEPRESSION = 0.5
MELT_RATE = 0.5
LATENT = 0.3

ROWS = 8
CHUNKS = 2
LANES = 128
f32 = jnp.float32


def ring_perms(axis):
    count = lax.axis_size(axis)
    forward = [(i, (i + 1) % count) for i in range(count)]
    backward = [((i + 1) % count, i) for i in range(count)]
    return forward, backward


def iotas():
    sub = lax.broadcasted_iota(jnp.int32, (ROWS, LANES), 0)
    lane = lax.broadcasted_iota(jnp.int32, (ROWS, LANES), 1)
    return sub, lane


class EdgeAcc:
    def __init__(self, count, y_first, y_last):
        zero = jnp.zeros((ROWS, LANES), f32)
        self.xf = [zero] * count
        self.xl = [zero] * count
        self.yf = list(y_first)
        self.yl = list(y_last)

    def add_x(self, planes, b):
        at_b = lax.broadcasted_iota(jnp.int32, (ROWS, LANES), 0) == b
        for f, v in enumerate(planes):
            self.xf[f] = jnp.where(at_b, pltpu.roll(v, b, 0), self.xf[f])
            self.xl[f] = jnp.where(at_b, pltpu.roll(v, (b + 1) % ROWS, 0), self.xl[f])

    def add_y(self, planes, d, lane):
        at_d = lane == d
        for f, v in enumerate(planes):
            self.yf[f] = jnp.where(at_d, pltpu.roll(v, d % LANES, 1), self.yf[f])
            self.yl[f] = jnp.where(at_d, pltpu.roll(v, (d + 1) % LANES, 1), self.yl[f])


def x_minus(v, lo_row, b, sub):
    return jnp.where(sub == 0, lo_row, pltpu.roll(v, 1, 0))


def x_plus(v, hi_row, b, sub):
    return jnp.where(sub == ROWS - 1, hi_row, pltpu.roll(v, ROWS - 1, 0))


def y_minus(v, lo_cols, d, lane):
    return jnp.where(lane == 0, pltpu.roll(lo_cols, (LANES - d) % LANES, 1), pltpu.roll(v, 1, 1))


def y_plus(v, hi_cols, d, lane):
    return jnp.where(
        lane == LANES - 1,
        pltpu.roll(hi_cols, (LANES - 1 - d) % LANES, 1),
        pltpu.roll(v, LANES - 1, 1),
    )


def lookup_tile(layer, entry, count):
    val = jnp.zeros(layer.shape, f32)
    for l in range(count):
        val = jnp.where(layer == l, entry(l), val)
    return val


def edge_kernel(lat_ref, adv_ref, layer_ref, h_ref, w_ref, c_ref, xf_ref, xl_ref, y_ref):
    n = layer_ref.shape[0]
    count = lat_ref.shape[1]
    lane = lax.broadcasted_iota(jnp.int32, (ROWS, LANES), 1)
    half_cx = lambda l: 0.5 * lat_ref[0, l]
    half_cy = lambda l: 0.5 * lat_ref[1, l]
    vx = lambda l: adv_ref[0, l]
    vy = lambda l: adv_ref[1, l]
    for a in range(n // ROWS):
        planes = pl.ds(a * ROWS, ROWS)
        for out_ref, row in ((xf_ref, 0), (xl_ref, ROWS - 1)):
            for f, src_ref in enumerate((h_ref, w_ref, c_ref)):
                out_ref[f, a] = src_ref[planes, row, :]
            layer = layer_ref[planes, row, :]
            out_ref[3, a] = lookup_tile(layer, half_cx, count)
            out_ref[4, a] = lookup_tile(layer, vx, count)
    zero = jnp.zeros((ROWS, LANES), f32)
    izero = jnp.zeros((ROWS, LANES), jnp.int32)

    def plane(d, carry):
        firsts, lasts, lay_f, lay_l = carry
        at_d = lane == d
        firsts = tuple(
            jnp.where(at_d, pltpu.roll(r[d], d, 1), v) for r, v in zip((h_ref, w_ref, c_ref), firsts)
        )
        lasts = tuple(
            jnp.where(at_d, pltpu.roll(r[d], (d + 1) % LANES, 1), v)
            for r, v in zip((h_ref, w_ref, c_ref), lasts)
        )
        layer = layer_ref[d]
        lay_f = jnp.where(at_d, pltpu.roll(layer, d, 1), lay_f)
        lay_l = jnp.where(at_d, pltpu.roll(layer, (d + 1) % LANES, 1), lay_l)
        return firsts, lasts, lay_f, lay_l

    firsts, lasts, lay_f, lay_l = lax.fori_loop(
        0, n, plane, ((zero,) * 3, (zero,) * 3, izero, izero)
    )
    for side, vals, lay in ((0, firsts, lay_f), (1, lasts, lay_l)):
        for f in range(3):
            y_ref[side, f] = vals[f]
        y_ref[side, 3] = lookup_tile(lay, half_cy, count)
        y_ref[side, 4] = lookup_tile(lay, vy, count)


def prep_kernel(lat_ref, vert_ref, adv_ref, layer_ref, h_ref, w_ref, c_ref, m_ref,
                ho_ref, wo_ref, cbo_ref, mo_ref, co_ref):
    layers_count = vert_ref.shape[0]

    def plane(d, carry):
        layer = layer_ref[d]
        zero = jnp.zeros(layer.shape, f32)
        vals = [zero] * 5
        for l in range(layers_count):
            hit = layer == l
            entries = (lat_ref[0, l], lat_ref[1, l], adv_ref[0, l], adv_ref[1, l], vert_ref[l])
            vals = [jnp.where(hit, entries[k], vals[k]) for k in range(5)]
        vals[0] = 0.5 * vals[0]
        vals[1] = 0.5 * vals[1]
        for k in range(5):
            co_ref[k, d] = vals[k]
        ho_ref[d] = h_ref[d]
        wo_ref[d] = w_ref[d]
        cbo_ref[d] = c_ref[d]
        mo_ref[d] = m_ref[d]
        return carry

    lax.fori_loop(0, layer_ref.shape[0], plane, 0)


def make_section_kernel(chunk, first):
    def kernel(h_ref, w_ref, c_ref, m_ref, sill_ref, co_ref, *rest):
        if first:
            xflo_ref, xfhi_ref, yflo_ref, yfhi_ref = rest[:4]
            ho_ref, wo_ref, cbo_ref, mo_ref, xf_ref, xl_ref, y_ref, nb_ref = rest[4:]
            xslo_ref, xshi_ref, yslo_ref, yshi_ref = xflo_ref, xfhi_ref, yflo_ref, yfhi_ref
            cylo = [yflo_ref[1, f] for f in (3, 4)]
            cyhi = [yfhi_ref[0, f] for f in (3, 4)]
        else:
            nb_ref, xslo_ref, xshi_ref, yslo_ref, yshi_ref = rest[:5]
            ho_ref, wo_ref, cbo_ref, mo_ref, xf_ref, xl_ref, y_ref = rest[5:]
        depth = h_ref.shape[0]
        groups = depth // ROWS
        sub, lane = iotas()
        zero = jnp.zeros((ROWS, LANES), f32)
        sylo = [yslo_ref[1, f] for f in range(3)]
        syhi = [yshi_ref[0, f] for f in range(3)]

        def group(a, carry):
            y_f, y_l = carry
            acc = EdgeAcc(3, y_f, y_l)
            for b in range(ROWS):
                i = a * ROWS + b
                row = pl.ds(b, ROWS, stride=0)
                sxlo = [xslo_ref[f, a, row, :] for f in range(3)]
                sxhi = [xshi_ref[f, a, row, :] for f in range(3)]
                d = chunk * depth + i
                heat = h_ref[i]
                water = w_ref[i]
                carbon = c_ref[i]
                melt = m_ref[i]
                sill = sill_ref[i].astype(f32)
                cx = co_ref[0, i]
                cy = co_ref[1, i]
                mobile = [heat, water, carbon]
                q_xm = [x_minus(mobile[f], sxlo[f], b, sub) for f in range(3)]
                q_xp = [x_plus(mobile[f], sxhi[f], b, sub) for f in range(3)]
                q_ym = [y_minus(mobile[f], sylo[f], d, lane) for f in range(3)]
                q_yp = [y_plus(mobile[f], syhi[f], d, lane) for f in range(3)]
                if first:
                    cxlo = [xflo_ref[f, a, row, :] for f in (3, 4)]
                    cxhi = [xfhi_ref[f, a, row, :] for f in (3, 4)]
                    vx = co_ref[2, i]
                    vy = co_ref[3, i]
                    cx_m = x_minus(cx, cxlo[0], b, sub)
                    cx_p = x_plus(cx, cxhi[0], b, sub)
                    vx_m = x_minus(vx, cxlo[1], b, sub)
                    vx_p = x_plus(vx, cxhi[1], b, sub)
                    cy_m = y_minus(cy, cylo[0], d, lane)
                    cy_p = y_plus(cy, cyhi[0], d, lane)
                    vy_m = y_minus(vy, cylo[1], d, lane)
                    vy_p = y_plus(vy, cyhi[1], d, lane)
                    fvx_m = 0.5 * (vx_m + vx)
                    fvx_p = 0.5 * (vx + vx_p)
                    fvy_m = 0.5 * (vy_m + vy)
                    fvy_p = 0.5 * (vy + vy_p)
                    near = (cx_m, cx_p, cy_m, cy_p, fvx_m, fvx_p, fvy_m, fvy_p)
                    for f, v in enumerate(near):
                        nb_ref[f, i] = v
                else:
                    cx_m, cx_p, cy_m, cy_p, fvx_m, fvx_p, fvy_m, fvy_p = [
                        nb_ref[f, i] for f in range(8)
                    ]
                soft = jnp.exp(-SOFTEN * heat)
                kx = cx * soft
                ky = cy * soft
                kx_m = cx_m * jnp.exp(-SOFTEN * q_xm[0])
                kx_p = cx_p * jnp.exp(-SOFTEN * q_xp[0])
                ky_m = cy_m * jnp.exp(-SOFTEN * q_ym[0])
                ky_p = cy_p * jnp.exp(-SOFTEN * q_yp[0])
                flux_x_lo = (kx_m + kx) * (heat - q_xm[0])
                flux_x_hi = (kx + kx_p) * (q_xp[0] - heat)
                flux_y_lo = (ky_m + ky) * (heat - q_ym[0])
                flux_y_hi = (ky + ky_p) * (q_yp[0] - heat)
                diffused = flux_x_hi - flux_x_lo + flux_y_hi - flux_y_lo
                inflow = []
                for f in range(3):
                    lo_x = jnp.maximum(fvx_m, 0.0) * q_xm[f] + jnp.minimum(fvx_m, 0.0) * mobile[f]
                    hi_x = jnp.maximum(fvx_p, 0.0) * mobile[f] + jnp.minimum(fvx_p, 0.0) * q_xp[f]
                    lo_y = jnp.maximum(fvy_m, 0.0) * q_ym[f] + jnp.minimum(fvy_m, 0.0) * mobile[f]
                    hi_y = jnp.maximum(fvy_p, 0.0) * mobile[f] + jnp.minimum(fvy_p, 0.0) * q_yp[f]
                    inflow.append(lo_x - hi_x + lo_y - hi_y)
                heat_one = heat + diffused + HEAT_CARRY * inflow[0]
                water_two = water + inflow[1] + sill * WATER_INPUT
                carbon_two = carbon + inflow[2] + sill * CARBON_INPUT
                heat_two = heat_one + sill * SILL_RATE * (SILL_HEAT - heat_one)
                z = MELT_SHARPNESS * (heat_two - SOLIDUS + DEPRESSION * water_two)
                target = 1.0 / (1.0 + jnp.exp(-z))
                melt_two = melt + MELT_RATE * (target - melt)
                heat_three = heat_two - LATENT * (melt_two - melt)
                ho_ref[i] = heat_three
                wo_ref[i] = water_two
                cbo_ref[i] = carbon_two
                mo_ref[i] = melt_two
                acc.add_y([heat_three, water_two, carbon_two], d, lane)
            planes = pl.ds(a * ROWS, ROWS)
            for f, out in enumerate((ho_ref, wo_ref, cbo_ref)):
                xf_ref[f, a] = out[planes, 0, :]
                xl_ref[f, a] = out[planes, ROWS - 1, :]
            return (tuple(acc.yf), tuple(acc.yl))

        y_f, y_l = lax.fori_loop(0, groups, group, ((zero,) * 3, (zero,) * 3))
        for f in range(3):
            y_ref[0, f] = y_f[f]
            y_ref[1, f] = y_l[f]

    return kernel


def sweep_kernel(r_ref, cz_ref, y_ref, a_ref, b_ref, red_ref, c_s, g_s, vy_s, va_s):
    n = r_ref.shape[0]
    zero = jnp.zeros(r_ref.shape[1:], f32)
    one = jnp.ones(r_ref.shape[1:], f32)

    def conduct(i, carry):
        c_s[i] = cz_ref[0, i] * jnp.exp(-SOFTEN * r_ref[i])
        return carry

    lax.fori_loop(0, n, conduct, 0)

    def forward(i, carry):
        g_prev, vy_prev, va_prev = carry
        up = 0.5 * (c_s[i - 1] + c_s[i])
        down = 0.5 * (c_s[i] + c_s[i + 1])
        inv = 1.0 / (1.0 + up + down - up * g_prev)
        g = down * inv
        vy = (r_ref[i] + up * vy_prev) * inv
        va = (up * va_prev) * inv
        g_s[i] = g
        vy_s[i] = vy
        va_s[i] = va
        return g, vy, va

    lax.fori_loop(1, n - 1, forward, (zero, zero, one))

    def backward(k, carry):
        i = n - 2 - k
        y_next, a_next, b_next = carry
        g = g_s[i]
        y = vy_s[i] + g * y_next
        a = va_s[i] + g * a_next
        b = g * b_next
        y_ref[i] = y
        a_ref[i] = a
        b_ref[i] = b
        return y, a, b

    lax.fori_loop(0, n - 2, backward, (zero, zero, one))
    y_ref[0] = zero
    a_ref[0] = one
    b_ref[0] = zero
    y_ref[n - 1] = zero
    a_ref[n - 1] = zero
    b_ref[n - 1] = one
    up_first = 0.5 * (c_s[0] + c_s[1])
    up_last = 0.5 * (c_s[n - 2] + c_s[n - 1])
    red_ref[0] = 1.0 + up_first * (1.0 - a_ref[1])
    red_ref[1] = up_first * b_ref[1]
    red_ref[2] = r_ref[0] + up_first * y_ref[1]
    red_ref[3] = 1.0 + up_last * (1.0 - b_ref[n - 2])
    red_ref[4] = up_last * a_ref[n - 2]
    red_ref[5] = r_ref[n - 1] + up_last * y_ref[n - 2]
    red_ref[6] = c_s[0]
    red_ref[7] = c_s[n - 1]


def reduced_solve(red_all):
    count = len(red_all)
    lower, diag, upper, side = [], [], [], []
    for j in range(count):
        p0, q0, s0, p1, q1, s1, c_first, c_last = red_all[j]
        if j == 0:
            face = c_first
            lower.append(jnp.zeros_like(face))
        else:
            face = 0.5 * (red_all[j - 1][7] + c_first)
            lower.append(face)
        diag.append(p0 + face)
        upper.append(q0)
        side.append(s0)
        if j + 1 < count:
            below = 0.5 * (c_last + red_all[j + 1][6])
        else:
            below = jnp.zeros_like(c_last)
        lower.append(q1)
        diag.append(p1 + below)
        upper.append(below)
        side.append(s1)
    size = len(diag)
    ratios, values = [], []
    g_prev = jnp.zeros_like(diag[0])
    v_prev = jnp.zeros_like(diag[0])
    for k in range(size):
        inv = 1.0 / (diag[k] - lower[k] * g_prev)
        g_prev = upper[k] * inv
        v_prev = (side[k] + lower[k] * v_prev) * inv
        ratios.append(g_prev)
        values.append(v_prev)
    solved = [None] * size
    following = jnp.zeros_like(diag[0])
    for k in reversed(range(size)):
        following = values[k] + ratios[k] * following
        solved[k] = following
    return solved


def finish_kernel(rank_ref, y_ref, a_ref, b_ref, *rest):
    recv = rest[:-1]
    t_ref = rest[-1]
    count = len(recv)
    rank = rank_ref[0]
    red_all = []
    for j in range(count):
        source = (rank - j + count) % count
        planes = []
        for k in range(8):
            v = recv[count - 1][k]
            for m in reversed(range(count - 1)):
                v = jnp.where(source == m, recv[m][k], v)
            planes.append(v)
        red_all.append(planes)
    solved = reduced_solve(red_all)
    first = solved[2 * (count - 1)]
    last = solved[2 * (count - 1) + 1]
    for j in reversed(range(count - 1)):
        first = jnp.where(rank == j, solved[2 * j], first)
        last = jnp.where(rank == j, solved[2 * j + 1], last)

    def combine(i, carry):
        t_ref[i] = y_ref[i] + a_ref[i] * first + b_ref[i] * last
        return carry

    lax.fori_loop(0, y_ref.shape[0], combine, 0)


def sds(shape):
    return jax.ShapeDtypeStruct(shape, f32)


def exchange(xf, xl, ys):
    east_fwd, east_bwd = ring_perms("east")
    north_fwd, north_bwd = ring_perms("north")
    xlo = lax.ppermute(xl, "east", east_fwd)
    xhi = lax.ppermute(xf, "east", east_bwd)
    ylo = lax.ppermute(ys, "north", north_fwd)
    if lax.axis_size("north") == 2:
        yhi = ylo
    else:
        yhi = lax.ppermute(ys, "north", north_bwd)
    return xlo, xhi, ylo, yhi


def full_spec(shape):
    zeros = (0,) * len(shape)
    return pl.BlockSpec(shape, lambda i: zeros)


def local(
    thermal_field,
    liquid_fraction,
    steam_content_grid,
    carbonic_gas_grid,
    stratum_number_grid,
    injection_flags,
    lateral_transmissivity,
    vertical_transmissivity,
    stratum_advection_offsets,
):
    shape = thermal_field.shape
    n = shape[0]
    groups = n // ROWS
    assert shape[1:] == (ROWS, LANES) and n % ROWS == 0 and n <= LANES
    chunks = CHUNKS if groups % CHUNKS == 0 else 1
    depth = n // chunks
    cgroups = depth // ROWS
    smem_spec = pl.BlockSpec(memory_space=pltpu.SMEM)
    vspec = pl.BlockSpec(memory_space=pltpu.MemorySpace.VMEM)
    xf0, xl0, y0 = pl.pallas_call(
        edge_kernel,
        out_shape=(sds((5, groups, ROWS, LANES)), sds((5, groups, ROWS, LANES)),
                   sds((2, 5, ROWS, LANES))),
        in_specs=[smem_spec] * 2 + [vspec] * 4,
    )(lateral_transmissivity, stratum_advection_offsets, stratum_number_grid,
      thermal_field, steam_content_grid, carbonic_gas_grid)
    xflo, xfhi, yflo, yfhi = exchange(xf0, xl0, y0)
    heat, water, carbon, melt, co = pl.pallas_call(
        prep_kernel,
        out_shape=(sds(shape), sds(shape), sds(shape), sds(shape), sds((5,) + shape)),
        in_specs=[smem_spec] * 3 + [vspec] * 5,
    )(lateral_transmissivity, vertical_transmissivity, stratum_advection_offsets,
      stratum_number_grid, thermal_field, steam_content_grid, carbonic_gas_grid, liquid_fraction)

    def block_spec(k):
        return pl.BlockSpec((depth, ROWS, LANES), lambda i: (k, 0, 0))

    halos = [None] * chunks
    nears = [None] * chunks
    x3 = full_spec((3, cgroups, ROWS, LANES))
    y3 = full_spec((2, 3, ROWS, LANES))
    near_spec = full_spec((8, depth, ROWS, LANES))
    for section_no in range(SECTIONS):
        first = section_no == 0
        for k in range(chunks):
            args = [heat, water, carbon, melt, injection_flags, co]
            in_specs = [block_spec(k)] * 5
            out_shape = [sds(shape)] * 4 + [sds((3, cgroups, ROWS, LANES))] * 2
            out_shape += [sds((2, 3, ROWS, LANES))]
            out_specs = [block_spec(k)] * 4 + [x3, x3, y3]
            if first:
                x5 = pl.BlockSpec((5, cgroups, ROWS, LANES), lambda i, k=k: (0, k, 0, 0))
                y5 = full_spec((2, 5, ROWS, LANES))
                in_specs += [pl.BlockSpec((4, depth, ROWS, LANES), lambda i, k=k: (0, k, 0, 0)),
                             x5, x5, y5, y5]
                args += [xflo, xfhi, yflo, yfhi]
                out_shape += [sds((8, depth, ROWS, LANES))]
                out_specs += [near_spec]
            else:
                in_specs += [pl.BlockSpec((2, depth, ROWS, LANES), lambda i, k=k: (0, k, 0, 0)),
                             near_spec, x3, x3, y3, y3]
                args += [nears[k]] + list(halos[k])
            outs = pl.pallas_call(
                make_section_kernel(k, first),
                grid=(1,),
                out_shape=tuple(out_shape),
                in_specs=in_specs,
                out_specs=out_specs,
                input_output_aliases={0: 0, 1: 1, 2: 2, 3: 3},
            )(*args)
            heat, water, carbon, melt, xf, xl, ys = outs[:7]
            if first:
                nears[k] = outs[7]
            if section_no + 1 < SECTIONS:
                halos[k] = exchange(xf, xl, ys)

    y, a, b, red = pl.pallas_call(
        sweep_kernel,
        grid=(1,),
        out_shape=(sds(shape), sds(shape), sds(shape), sds((8,) + shape[1:])),
        in_specs=[full_spec(shape), pl.BlockSpec((1,) + shape, lambda i: (4, 0, 0, 0))],
        out_specs=[full_spec(shape)] * 3 + [full_spec((8,) + shape[1:])],
        scratch_shapes=[pltpu.VMEM(shape, f32)] * 4,
    )(heat, co)
    count = lax.axis_size("depth")
    rank = lax.axis_index("depth")
    received = [red]
    for k in range(1, count):
        received.append(lax.ppermute(red, "depth", [(i, (i + k) % count) for i in range(count)]))
    rank_arr = jnp.full((1,), rank, jnp.int32)
    heat_next = pl.pallas_call(
        finish_kernel,
        out_shape=sds(shape),
        in_specs=[smem_spec] + [vspec] * (3 + count),
    )(rank_arr, y, a, b, *received)
    return (heat_next, melt, water, carbon)


def solution(mesh):
    placed = (
        P("depth", "east", "north"),
        P("depth", "east", "north"),
        P("depth", "east", "north"),
        P("depth", "east", "north"),
        P("depth", "east", "north"),
        P("depth", "east", "north"),
        P(),
        P(),
        P(),
    )
    return jax.shard_map(
        local,
        mesh=mesh,
        in_specs=placed,
        out_specs=(
            P("depth", "east", "north"),
            P("depth", "east", "north"),
            P("depth", "east", "north"),
            P("depth", "east", "north"),
        ),
        check_vma=False,
    )
```

```python
import jax
import jax.numpy as jnp
from jax import lax
from jax.experimental import pallas as pl
from jax.experimental.pallas import tpu as pltpu
from jax.sharding import PartitionSpec as P

SECTIONS = 4


SOFTEN = 0.5
HEAT_CARRY = 0.5
SILL_RATE = 0.3
SILL_HEAT = 2.5
WATER_INPUT = 0.2
CARBON_INPUT = 0.1
MELT_SHARPNESS = 4.0
SOLIDUS = 1.0
DEPRESSION = 0.5
MELT_RATE = 0.5
LATENT = 0.3

ROWS = 8
CHUNKS = 2
LANES = 128
f32 = jnp.float32


def ring_perms(axis):
    count = lax.axis_size(axis)
    forward = [(i, (i + 1) % count) for i in range(count)]
    backward = [((i + 1) % count, i) for i in range(count)]
    return forward, backward


def iotas():
    sub = lax.broadcasted_iota(jnp.int32, (ROWS, LANES), 0)
    lane = lax.broadcasted_iota(jnp.int32, (ROWS, LANES), 1)
    return sub, lane


class EdgeAcc:
    def __init__(self, count, y_first, y_last):
        zero = jnp.zeros((ROWS, LANES), f32)
        self.xf = [zero] * count
        self.xl = [zero] * count
        self.yf = list(y_first)
        self.yl = list(y_last)

    def add_x(self, planes, b):
        at_b = lax.broadcasted_iota(jnp.int32, (ROWS, LANES), 0) == b
        for f, v in enumerate(planes):
            self.xf[f] = jnp.where(at_b, pltpu.roll(v, b, 0), self.xf[f])
            self.xl[f] = jnp.where(at_b, pltpu.roll(v, (b + 1) % ROWS, 0), self.xl[f])

    def add_y(self, planes, d, lane):
        at_d = lane == d
        for f, v in enumerate(planes):
            self.yf[f] = jnp.where(at_d, pltpu.roll(v, d % LANES, 1), self.yf[f])
            self.yl[f] = jnp.where(at_d, pltpu.roll(v, (d + 1) % LANES, 1), self.yl[f])


def x_minus(v, lo_row, b, sub):
    return jnp.where(sub == 0, lo_row, pltpu.roll(v, 1, 0))


def x_plus(v, hi_row, b, sub):
    return jnp.where(sub == ROWS - 1, hi_row, pltpu.roll(v, ROWS - 1, 0))


def y_minus(v, lo_cols, d, lane):
    return jnp.where(lane == 0, pltpu.roll(lo_cols, (LANES - d) % LANES, 1), pltpu.roll(v, 1, 1))


def y_plus(v, hi_cols, d, lane):
    return jnp.where(
        lane == LANES - 1,
        pltpu.roll(hi_cols, (LANES - 1 - d) % LANES, 1),
        pltpu.roll(v, LANES - 1, 1),
    )


def lookup_tile(layer, entry, count):
    val = jnp.zeros(layer.shape, f32)
    for l in range(count):
        val = jnp.where(layer == l, entry(l), val)
    return val


def edge_kernel(lat_ref, adv_ref, layer_ref, h_ref, w_ref, c_ref, xf_ref, xl_ref, y_ref):
    n = layer_ref.shape[0]
    count = lat_ref.shape[1]
    lane = lax.broadcasted_iota(jnp.int32, (ROWS, LANES), 1)
    half_cx = lambda l: 0.5 * lat_ref[0, l]
    half_cy = lambda l: 0.5 * lat_ref[1, l]
    vx = lambda l: adv_ref[0, l]
    vy = lambda l: adv_ref[1, l]
    for a in range(n // ROWS):
        planes = pl.ds(a * ROWS, ROWS)
        for out_ref, row in ((xf_ref, 0), (xl_ref, ROWS - 1)):
            for f, src_ref in enumerate((h_ref, w_ref, c_ref)):
                out_ref[f, a] = src_ref[planes, row, :]
            layer = layer_ref[planes, row, :]
            out_ref[3, a] = lookup_tile(layer, half_cx, count)
            out_ref[4, a] = lookup_tile(layer, vx, count)
    zero = jnp.zeros((ROWS, LANES), f32)
    izero = jnp.zeros((ROWS, LANES), jnp.int32)

    def group(a, carry):
        firsts, lasts, lay_f, lay_l = carry
        for b in range(ROWS):
            d = a * ROWS + b
            at_d = lane == d
            srcs = (h_ref[d], w_ref[d], c_ref[d])
            firsts = tuple(
                jnp.where(at_d, pltpu.roll(v, d, 1), acc) for v, acc in zip(srcs, firsts)
            )
            lasts = tuple(
                jnp.where(at_d, pltpu.roll(v, (d + 1) % LANES, 1), acc)
                for v, acc in zip(srcs, lasts)
            )
            layer = layer_ref[d]
            lay_f = jnp.where(at_d, pltpu.roll(layer, d, 1), lay_f)
            lay_l = jnp.where(at_d, pltpu.roll(layer, (d + 1) % LANES, 1), lay_l)
        return firsts, lasts, lay_f, lay_l

    firsts, lasts, lay_f, lay_l = lax.fori_loop(
        0, n // ROWS, group, ((zero,) * 3, (zero,) * 3, izero, izero)
    )
    for side, vals, lay in ((0, firsts, lay_f), (1, lasts, lay_l)):
        for f in range(3):
            y_ref[side, f] = vals[f]
        y_ref[side, 3] = lookup_tile(lay, half_cy, count)
        y_ref[side, 4] = lookup_tile(lay, vy, count)


def prep_kernel(lat_ref, vert_ref, adv_ref, layer_ref, h_ref, w_ref, c_ref, m_ref,
                ho_ref, wo_ref, cbo_ref, mo_ref, co_ref):
    layers_count = vert_ref.shape[0]

    def plane(d, carry):
        layer = layer_ref[d]
        zero = jnp.zeros(layer.shape, f32)
        vals = [zero] * 5
        for l in range(layers_count):
            hit = layer == l
            entries = (lat_ref[0, l], lat_ref[1, l], adv_ref[0, l], adv_ref[1, l], vert_ref[l])
            vals = [jnp.where(hit, entries[k], vals[k]) for k in range(5)]
        vals[0] = 0.5 * vals[0]
        vals[1] = 0.5 * vals[1]
        for k in range(5):
            co_ref[k, d] = vals[k]
        ho_ref[d] = h_ref[d]
        wo_ref[d] = w_ref[d]
        cbo_ref[d] = c_ref[d]
        mo_ref[d] = m_ref[d]
        return carry

    lax.fori_loop(0, layer_ref.shape[0], plane, 0)


def make_section_kernel(chunk, first):
    def kernel(h_ref, w_ref, c_ref, m_ref, sill_ref, co_ref, *rest):
        if first:
            xflo_ref, xfhi_ref, yflo_ref, yfhi_ref = rest[:4]
            ho_ref, wo_ref, cbo_ref, mo_ref, xf_ref, xl_ref, y_ref, nb_ref = rest[4:]
            xslo_ref, xshi_ref, yslo_ref, yshi_ref = xflo_ref, xfhi_ref, yflo_ref, yfhi_ref
            cylo = [yflo_ref[1, f] for f in (3, 4)]
            cyhi = [yfhi_ref[0, f] for f in (3, 4)]
        else:
            nb_ref, xslo_ref, xshi_ref, yslo_ref, yshi_ref = rest[:5]
            ho_ref, wo_ref, cbo_ref, mo_ref, xf_ref, xl_ref, y_ref = rest[5:]
        depth = h_ref.shape[0]
        groups = depth // ROWS
        sub, lane = iotas()
        zero = jnp.zeros((ROWS, LANES), f32)
        sylo = [yslo_ref[1, f] for f in range(3)]
        syhi = [yshi_ref[0, f] for f in range(3)]

        def group(a, carry):
            y_f, y_l = carry
            acc = EdgeAcc(3, y_f, y_l)
            for b in range(ROWS):
                i = a * ROWS + b
                row = pl.ds(b, ROWS, stride=0)
                sxlo = [xslo_ref[f, a, row, :] for f in range(3)]
                sxhi = [xshi_ref[f, a, row, :] for f in range(3)]
                d = chunk * depth + i
                heat = h_ref[i]
                water = w_ref[i]
                carbon = c_ref[i]
                melt = m_ref[i]
                sill = sill_ref[i].astype(f32)
                cx = co_ref[0, i]
                cy = co_ref[1, i]
                mobile = [heat, water, carbon]
                q_xm = [x_minus(mobile[f], sxlo[f], b, sub) for f in range(3)]
                q_xp = [x_plus(mobile[f], sxhi[f], b, sub) for f in range(3)]
                q_ym = [y_minus(mobile[f], sylo[f], d, lane) for f in range(3)]
                q_yp = [y_plus(mobile[f], syhi[f], d, lane) for f in range(3)]
                if first:
                    cxlo = [xflo_ref[f, a, row, :] for f in (3, 4)]
                    cxhi = [xfhi_ref[f, a, row, :] for f in (3, 4)]
                    vx = co_ref[2, i]
                    vy = co_ref[3, i]
                    cx_m = x_minus(cx, cxlo[0], b, sub)
                    cx_p = x_plus(cx, cxhi[0], b, sub)
                    vx_m = x_minus(vx, cxlo[1], b, sub)
                    vx_p = x_plus(vx, cxhi[1], b, sub)
                    cy_m = y_minus(cy, cylo[0], d, lane)
                    cy_p = y_plus(cy, cyhi[0], d, lane)
                    vy_m = y_minus(vy, cylo[1], d, lane)
                    vy_p = y_plus(vy, cyhi[1], d, lane)
                    fvx_m = 0.5 * (vx_m + vx)
                    fvx_p = 0.5 * (vx + vx_p)
                    fvy_m = 0.5 * (vy_m + vy)
                    fvy_p = 0.5 * (vy + vy_p)
                    near = (cx_m, cx_p, cy_m, cy_p, fvx_m, fvx_p, fvy_m, fvy_p)
                    for f, v in enumerate(near):
                        nb_ref[f, i] = v
                else:
                    cx_m, cx_p, cy_m, cy_p, fvx_m, fvx_p, fvy_m, fvy_p = [
                        nb_ref[f, i] for f in range(8)
                    ]
                soft = jnp.exp(-SOFTEN * heat)
                kx = cx * soft
                ky = cy * soft
                kx_m = cx_m * jnp.exp(-SOFTEN * q_xm[0])
                kx_p = cx_p * jnp.exp(-SOFTEN * q_xp[0])
                ky_m = cy_m * jnp.exp(-SOFTEN * q_ym[0])
                ky_p = cy_p * jnp.exp(-SOFTEN * q_yp[0])
                flux_x_lo = (kx_m + kx) * (heat - q_xm[0])
                flux_x_hi = (kx + kx_p) * (q_xp[0] - heat)
                flux_y_lo = (ky_m + ky) * (heat - q_ym[0])
                flux_y_hi = (ky + ky_p) * (q_yp[0] - heat)
                diffused = flux_x_hi - flux_x_lo + flux_y_hi - flux_y_lo
                inflow = []
                for f in range(3):
                    lo_x = jnp.maximum(fvx_m, 0.0) * q_xm[f] + jnp.minimum(fvx_m, 0.0) * mobile[f]
                    hi_x = jnp.maximum(fvx_p, 0.0) * mobile[f] + jnp.minimum(fvx_p, 0.0) * q_xp[f]
                    lo_y = jnp.maximum(fvy_m, 0.0) * q_ym[f] + jnp.minimum(fvy_m, 0.0) * mobile[f]
                    hi_y = jnp.maximum(fvy_p, 0.0) * mobile[f] + jnp.minimum(fvy_p, 0.0) * q_yp[f]
                    inflow.append(lo_x - hi_x + lo_y - hi_y)
                heat_one = heat + diffused + HEAT_CARRY * inflow[0]
                water_two = water + inflow[1] + sill * WATER_INPUT
                carbon_two = carbon + inflow[2] + sill * CARBON_INPUT
                heat_two = heat_one + sill * SILL_RATE * (SILL_HEAT - heat_one)
                z = MELT_SHARPNESS * (heat_two - SOLIDUS + DEPRESSION * water_two)
                target = 1.0 / (1.0 + jnp.exp(-z))
                melt_two = melt + MELT_RATE * (target - melt)
                heat_three = heat_two - LATENT * (melt_two - melt)
                ho_ref[i] = heat_three
                wo_ref[i] = water_two
                cbo_ref[i] = carbon_two
                mo_ref[i] = melt_two
                acc.add_y([heat_three, water_two, carbon_two], d, lane)
            planes = pl.ds(a * ROWS, ROWS)
            for f, out in enumerate((ho_ref, wo_ref, cbo_ref)):
                xf_ref[f, a] = out[planes, 0, :]
                xl_ref[f, a] = out[planes, ROWS - 1, :]
            return (tuple(acc.yf), tuple(acc.yl))

        y_f, y_l = lax.fori_loop(0, groups, group, ((zero,) * 3, (zero,) * 3))
        for f in range(3):
            y_ref[0, f] = y_f[f]
            y_ref[1, f] = y_l[f]

    return kernel


def sweep_kernel(r_ref, cz_ref, y_ref, a_ref, b_ref, red_ref, c_s, g_s, vy_s, va_s):
    n = r_ref.shape[0]
    zero = jnp.zeros(r_ref.shape[1:], f32)
    one = jnp.ones(r_ref.shape[1:], f32)

    def conduct(i, carry):
        c_s[i] = cz_ref[0, i] * jnp.exp(-SOFTEN * r_ref[i])
        return carry

    lax.fori_loop(0, n, conduct, 0)

    def forward(i, carry):
        g_prev, vy_prev, va_prev = carry
        up = 0.5 * (c_s[i - 1] + c_s[i])
        down = 0.5 * (c_s[i] + c_s[i + 1])
        inv = 1.0 / (1.0 + up + down - up * g_prev)
        g = down * inv
        vy = (r_ref[i] + up * vy_prev) * inv
        va = (up * va_prev) * inv
        g_s[i] = g
        vy_s[i] = vy
        va_s[i] = va
        return g, vy, va

    lax.fori_loop(1, n - 1, forward, (zero, zero, one))

    def backward(k, carry):
        i = n - 2 - k
        y_next, a_next, b_next = carry
        g = g_s[i]
        y = vy_s[i] + g * y_next
        a = va_s[i] + g * a_next
        b = g * b_next
        y_ref[i] = y
        a_ref[i] = a
        b_ref[i] = b
        return y, a, b

    lax.fori_loop(0, n - 2, backward, (zero, zero, one))
    y_ref[0] = zero
    a_ref[0] = one
    b_ref[0] = zero
    y_ref[n - 1] = zero
    a_ref[n - 1] = zero
    b_ref[n - 1] = one
    up_first = 0.5 * (c_s[0] + c_s[1])
    up_last = 0.5 * (c_s[n - 2] + c_s[n - 1])
    red_ref[0] = 1.0 + up_first * (1.0 - a_ref[1])
    red_ref[1] = up_first * b_ref[1]
    red_ref[2] = r_ref[0] + up_first * y_ref[1]
    red_ref[3] = 1.0 + up_last * (1.0 - b_ref[n - 2])
    red_ref[4] = up_last * a_ref[n - 2]
    red_ref[5] = r_ref[n - 1] + up_last * y_ref[n - 2]
    red_ref[6] = c_s[0]
    red_ref[7] = c_s[n - 1]


def reduced_solve(red_all):
    count = len(red_all)
    lower, diag, upper, side = [], [], [], []
    for j in range(count):
        p0, q0, s0, p1, q1, s1, c_first, c_last = red_all[j]
        if j == 0:
            face = c_first
            lower.append(jnp.zeros_like(face))
        else:
            face = 0.5 * (red_all[j - 1][7] + c_first)
            lower.append(face)
        diag.append(p0 + face)
        upper.append(q0)
        side.append(s0)
        if j + 1 < count:
            below = 0.5 * (c_last + red_all[j + 1][6])
        else:
            below = jnp.zeros_like(c_last)
        lower.append(q1)
        diag.append(p1 + below)
        upper.append(below)
        side.append(s1)
    size = len(diag)
    ratios, values = [], []
    g_prev = jnp.zeros_like(diag[0])
    v_prev = jnp.zeros_like(diag[0])
    for k in range(size):
        inv = 1.0 / (diag[k] - lower[k] * g_prev)
        g_prev = upper[k] * inv
        v_prev = (side[k] + lower[k] * v_prev) * inv
        ratios.append(g_prev)
        values.append(v_prev)
    solved = [None] * size
    following = jnp.zeros_like(diag[0])
    for k in reversed(range(size)):
        following = values[k] + ratios[k] * following
        solved[k] = following
    return solved


def finish_kernel(rank_ref, y_ref, a_ref, b_ref, *rest):
    recv = rest[:-1]
    t_ref = rest[-1]
    count = len(recv)
    rank = rank_ref[0]
    red_all = []
    for j in range(count):
        source = (rank - j + count) % count
        planes = []
        for k in range(8):
            v = recv[count - 1][k]
            for m in reversed(range(count - 1)):
                v = jnp.where(source == m, recv[m][k], v)
            planes.append(v)
        red_all.append(planes)
    solved = reduced_solve(red_all)
    first = solved[2 * (count - 1)]
    last = solved[2 * (count - 1) + 1]
    for j in reversed(range(count - 1)):
        first = jnp.where(rank == j, solved[2 * j], first)
        last = jnp.where(rank == j, solved[2 * j + 1], last)

    def combine(i, carry):
        t_ref[i] = y_ref[i] + a_ref[i] * first + b_ref[i] * last
        return carry

    lax.fori_loop(0, y_ref.shape[0], combine, 0)


def sds(shape):
    return jax.ShapeDtypeStruct(shape, f32)


def exchange(xf, xl, ys):
    east_fwd, east_bwd = ring_perms("east")
    north_fwd, north_bwd = ring_perms("north")
    xlo = lax.ppermute(xl, "east", east_fwd)
    xhi = lax.ppermute(xf, "east", east_bwd)
    ylo = lax.ppermute(ys, "north", north_fwd)
    if lax.axis_size("north") == 2:
        yhi = ylo
    else:
        yhi = lax.ppermute(ys, "north", north_bwd)
    return xlo, xhi, ylo, yhi


def full_spec(shape):
    zeros = (0,) * len(shape)
    return pl.BlockSpec(shape, lambda i: zeros)


def local(
    thermal_field,
    liquid_fraction,
    steam_content_grid,
    carbonic_gas_grid,
    stratum_number_grid,
    injection_flags,
    lateral_transmissivity,
    vertical_transmissivity,
    stratum_advection_offsets,
):
    shape = thermal_field.shape
    n = shape[0]
    groups = n // ROWS
    assert shape[1:] == (ROWS, LANES) and n % ROWS == 0 and n <= LANES
    chunks = CHUNKS if groups % CHUNKS == 0 else 1
    depth = n // chunks
    cgroups = depth // ROWS
    smem_spec = pl.BlockSpec(memory_space=pltpu.SMEM)
    vspec = pl.BlockSpec(memory_space=pltpu.MemorySpace.VMEM)
    xf0, xl0, y0 = pl.pallas_call(
        edge_kernel,
        out_shape=(sds((5, groups, ROWS, LANES)), sds((5, groups, ROWS, LANES)),
                   sds((2, 5, ROWS, LANES))),
        in_specs=[smem_spec] * 2 + [vspec] * 4,
    )(lateral_transmissivity, stratum_advection_offsets, stratum_number_grid,
      thermal_field, steam_content_grid, carbonic_gas_grid)
    xflo, xfhi, yflo, yfhi = exchange(xf0, xl0, y0)
    heat, water, carbon, melt, co = pl.pallas_call(
        prep_kernel,
        out_shape=(sds(shape), sds(shape), sds(shape), sds(shape), sds((5,) + shape)),
        in_specs=[smem_spec] * 3 + [vspec] * 5,
    )(lateral_transmissivity, vertical_transmissivity, stratum_advection_offsets,
      stratum_number_grid, thermal_field, steam_content_grid, carbonic_gas_grid, liquid_fraction)

    def block_spec(k):
        return pl.BlockSpec((depth, ROWS, LANES), lambda i: (k, 0, 0))

    halos = [None] * chunks
    nears = [None] * chunks
    x3 = full_spec((3, cgroups, ROWS, LANES))
    y3 = full_spec((2, 3, ROWS, LANES))
    near_spec = full_spec((8, depth, ROWS, LANES))
    for section_no in range(SECTIONS):
        first = section_no == 0
        for k in range(chunks):
            args = [heat, water, carbon, melt, injection_flags, co]
            in_specs = [block_spec(k)] * 5
            out_shape = [sds(shape)] * 4 + [sds((3, cgroups, ROWS, LANES))] * 2
            out_shape += [sds((2, 3, ROWS, LANES))]
            out_specs = [block_spec(k)] * 4 + [x3, x3, y3]
            if first:
                x5 = pl.BlockSpec((5, cgroups, ROWS, LANES), lambda i, k=k: (0, k, 0, 0))
                y5 = full_spec((2, 5, ROWS, LANES))
                in_specs += [pl.BlockSpec((4, depth, ROWS, LANES), lambda i, k=k: (0, k, 0, 0)),
                             x5, x5, y5, y5]
                args += [xflo, xfhi, yflo, yfhi]
                out_shape += [sds((8, depth, ROWS, LANES))]
                out_specs += [near_spec]
            else:
                in_specs += [pl.BlockSpec((2, depth, ROWS, LANES), lambda i, k=k: (0, k, 0, 0)),
                             near_spec, x3, x3, y3, y3]
                args += [nears[k]] + list(halos[k])
            outs = pl.pallas_call(
                make_section_kernel(k, first),
                grid=(1,),
                out_shape=tuple(out_shape),
                in_specs=in_specs,
                out_specs=out_specs,
                input_output_aliases={0: 0, 1: 1, 2: 2, 3: 3},
            )(*args)
            heat, water, carbon, melt, xf, xl, ys = outs[:7]
            if first:
                nears[k] = outs[7]
            if section_no + 1 < SECTIONS:
                halos[k] = exchange(xf, xl, ys)

    y, a, b, red = pl.pallas_call(
        sweep_kernel,
        grid=(1,),
        out_shape=(sds(shape), sds(shape), sds(shape), sds((8,) + shape[1:])),
        in_specs=[full_spec(shape), pl.BlockSpec((1,) + shape, lambda i: (4, 0, 0, 0))],
        out_specs=[full_spec(shape)] * 3 + [full_spec((8,) + shape[1:])],
        scratch_shapes=[pltpu.VMEM(shape, f32)] * 4,
    )(heat, co)
    count = lax.axis_size("depth")
    rank = lax.axis_index("depth")
    received = [red]
    for k in range(1, count):
        received.append(lax.ppermute(red, "depth", [(i, (i + k) % count) for i in range(count)]))
    rank_arr = jnp.full((1,), rank, jnp.int32)
    heat_next = pl.pallas_call(
        finish_kernel,
        out_shape=sds(shape),
        in_specs=[smem_spec] + [vspec] * (3 + count),
    )(rank_arr, y, a, b, *received)
    return (heat_next, melt, water, carbon)


def solution(mesh):
    placed = (
        P("depth", "east", "north"),
        P("depth", "east", "north"),
        P("depth", "east", "north"),
        P("depth", "east", "north"),
        P("depth", "east", "north"),
        P("depth", "east", "north"),
        P(),
        P(),
        P(),
    )
    return jax.shard_map(
        local,
        mesh=mesh,
        in_specs=placed,
        out_specs=(
            P("depth", "east", "north"),
            P("depth", "east", "north"),
            P("depth", "east", "north"),
            P("depth", "east", "north"),
        ),
        check_vma=False,
    )
```

```python
import jax
import jax.numpy as jnp
from jax import lax
from jax.experimental import pallas as pl
from jax.experimental.pallas import tpu as pltpu
from jax.sharding import PartitionSpec as P

SECTIONS = 4


SOFTEN = 0.5
HEAT_CARRY = 0.5
SILL_RATE = 0.3
SILL_HEAT = 2.5
WATER_INPUT = 0.2
CARBON_INPUT = 0.1
MELT_SHARPNESS = 4.0
SOLIDUS = 1.0
DEPRESSION = 0.5
MELT_RATE = 0.5
LATENT = 0.3

ROWS = 8
CHUNKS = 4
LANES = 128
f32 = jnp.float32


def ring_perms(axis):
    count = lax.axis_size(axis)
    forward = [(i, (i + 1) % count) for i in range(count)]
    backward = [((i + 1) % count, i) for i in range(count)]
    return forward, backward


def iotas():
    sub = lax.broadcasted_iota(jnp.int32, (ROWS, LANES), 0)
    lane = lax.broadcasted_iota(jnp.int32, (ROWS, LANES), 1)
    return sub, lane


class EdgeAcc:
    def __init__(self, count, y_first, y_last):
        zero = jnp.zeros((ROWS, LANES), f32)
        self.xf = [zero] * count
        self.xl = [zero] * count
        self.yf = list(y_first)
        self.yl = list(y_last)

    def add_x(self, planes, b):
        at_b = lax.broadcasted_iota(jnp.int32, (ROWS, LANES), 0) == b
        for f, v in enumerate(planes):
            self.xf[f] = jnp.where(at_b, pltpu.roll(v, b, 0), self.xf[f])
            self.xl[f] = jnp.where(at_b, pltpu.roll(v, (b + 1) % ROWS, 0), self.xl[f])

    def add_y(self, planes, d, lane):
        at_d = lane == d
        for f, v in enumerate(planes):
            self.yf[f] = jnp.where(at_d, pltpu.roll(v, d % LANES, 1), self.yf[f])
            self.yl[f] = jnp.where(at_d, pltpu.roll(v, (d + 1) % LANES, 1), self.yl[f])


def x_minus(v, lo_row, b, sub):
    return jnp.where(sub == 0, lo_row, pltpu.roll(v, 1, 0))


def x_plus(v, hi_row, b, sub):
    return jnp.where(sub == ROWS - 1, hi_row, pltpu.roll(v, ROWS - 1, 0))


def y_minus(v, lo_cols, d, lane):
    return jnp.where(lane == 0, pltpu.roll(lo_cols, (LANES - d) % LANES, 1), pltpu.roll(v, 1, 1))


def y_plus(v, hi_cols, d, lane):
    return jnp.where(
        lane == LANES - 1,
        pltpu.roll(hi_cols, (LANES - 1 - d) % LANES, 1),
        pltpu.roll(v, LANES - 1, 1),
    )


def prep_kernel(lat_ref, vert_ref, adv_ref, layer_ref, h_ref, w_ref, c_ref, m_ref,
                ho_ref, wo_ref, cbo_ref, mo_ref, co_ref, xf_ref, xl_ref, y_ref):
    groups = layer_ref.shape[0] // ROWS
    layers_count = vert_ref.shape[0]
    sub, lane = iotas()
    zero = jnp.zeros((ROWS, LANES), f32)

    def group(a, carry):
        y_f, y_l = carry
        acc = EdgeAcc(5, y_f, y_l)
        for b in range(ROWS):
            d = a * ROWS + b
            layer = layer_ref[d]
            vals = [zero] * 5
            for l in range(layers_count):
                hit = layer == l
                entries = (lat_ref[0, l], lat_ref[1, l], adv_ref[0, l], adv_ref[1, l], vert_ref[l])
                vals = [jnp.where(hit, entries[k], vals[k]) for k in range(5)]
            for k in range(5):
                co_ref[k, d] = vals[k]
            heat, water, carbon = h_ref[d], w_ref[d], c_ref[d]
            ho_ref[d] = heat
            wo_ref[d] = water
            cbo_ref[d] = carbon
            mo_ref[d] = m_ref[d]
            acc.add_y([heat, water, carbon, vals[1], vals[3]], d, lane)
        planes = pl.ds(a * ROWS, ROWS)
        sources = ((ho_ref, None), (wo_ref, None), (cbo_ref, None), (co_ref, 0), (co_ref, 2))
        for f, (out, field) in enumerate(sources):
            if field is None:
                xf_ref[f, a] = out[planes, 0, :]
                xl_ref[f, a] = out[planes, ROWS - 1, :]
            else:
                xf_ref[f, a] = out[field, planes, 0, :]
                xl_ref[f, a] = out[field, planes, ROWS - 1, :]
        return (tuple(acc.yf), tuple(acc.yl))

    y_f, y_l = lax.fori_loop(0, groups, group, ((zero,) * 5, (zero,) * 5))
    for f in range(5):
        y_ref[0, f] = y_f[f]
        y_ref[1, f] = y_l[f]


def make_section_kernel(chunk, first):
    def kernel(h_ref, w_ref, c_ref, m_ref, sill_ref, co_ref, *rest):
        if first:
            xflo_ref, xfhi_ref, yflo_ref, yfhi_ref = rest[:4]
            ho_ref, wo_ref, cbo_ref, mo_ref, xf_ref, xl_ref, y_ref, nb_ref = rest[4:]
            xslo_ref, xshi_ref, yslo_ref, yshi_ref = xflo_ref, xfhi_ref, yflo_ref, yfhi_ref
            cylo = [yflo_ref[1, f] for f in (3, 4)]
            cyhi = [yfhi_ref[0, f] for f in (3, 4)]
        else:
            nb_ref, xslo_ref, xshi_ref, yslo_ref, yshi_ref = rest[:5]
            ho_ref, wo_ref, cbo_ref, mo_ref, xf_ref, xl_ref, y_ref = rest[5:]
        depth = h_ref.shape[0]
        groups = depth // ROWS
        sub, lane = iotas()
        zero = jnp.zeros((ROWS, LANES), f32)
        sylo = [yslo_ref[1, f] for f in range(3)]
        syhi = [yshi_ref[0, f] for f in range(3)]

        def group(a, carry):
            y_f, y_l = carry
            acc = EdgeAcc(3, y_f, y_l)
            for b in range(ROWS):
                i = a * ROWS + b
                row = pl.ds(b, ROWS, stride=0)
                sxlo = [xslo_ref[f, a, row, :] for f in range(3)]
                sxhi = [xshi_ref[f, a, row, :] for f in range(3)]
                d = chunk * depth + i
                heat = h_ref[i]
                water = w_ref[i]
                carbon = c_ref[i]
                melt = m_ref[i]
                sill = sill_ref[i].astype(f32)
                cx = co_ref[0, i]
                cy = co_ref[1, i]
                mobile = [heat, water, carbon]
                q_xm = [x_minus(mobile[f], sxlo[f], b, sub) for f in range(3)]
                q_xp = [x_plus(mobile[f], sxhi[f], b, sub) for f in range(3)]
                q_ym = [y_minus(mobile[f], sylo[f], d, lane) for f in range(3)]
                q_yp = [y_plus(mobile[f], syhi[f], d, lane) for f in range(3)]
                if first:
                    cxlo = [xflo_ref[f, a, row, :] for f in (3, 4)]
                    cxhi = [xfhi_ref[f, a, row, :] for f in (3, 4)]
                    vx = co_ref[2, i]
                    vy = co_ref[3, i]
                    cx_m = x_minus(cx, cxlo[0], b, sub)
                    cx_p = x_plus(cx, cxhi[0], b, sub)
                    vx_m = x_minus(vx, cxlo[1], b, sub)
                    vx_p = x_plus(vx, cxhi[1], b, sub)
                    cy_m = y_minus(cy, cylo[0], d, lane)
                    cy_p = y_plus(cy, cyhi[0], d, lane)
                    vy_m = y_minus(vy, cylo[1], d, lane)
                    vy_p = y_plus(vy, cyhi[1], d, lane)
                    fvx_m = 0.5 * (vx_m + vx)
                    fvx_p = 0.5 * (vx + vx_p)
                    fvy_m = 0.5 * (vy_m + vy)
                    fvy_p = 0.5 * (vy + vy_p)
                    near = (cx_m, cx_p, cy_m, cy_p, fvx_m, fvx_p, fvy_m, fvy_p)
                    for f, v in enumerate(near):
                        nb_ref[f, i] = v
                else:
                    cx_m, cx_p, cy_m, cy_p, fvx_m, fvx_p, fvy_m, fvy_p = [
                        nb_ref[f, i] for f in range(8)
                    ]
                soft = jnp.exp(-SOFTEN * heat)
                kx = cx * soft
                ky = cy * soft
                kx_m = cx_m * jnp.exp(-SOFTEN * q_xm[0])
                kx_p = cx_p * jnp.exp(-SOFTEN * q_xp[0])
                ky_m = cy_m * jnp.exp(-SOFTEN * q_ym[0])
                ky_p = cy_p * jnp.exp(-SOFTEN * q_yp[0])
                flux_x_lo = 0.5 * (kx_m + kx) * (heat - q_xm[0])
                flux_x_hi = 0.5 * (kx + kx_p) * (q_xp[0] - heat)
                flux_y_lo = 0.5 * (ky_m + ky) * (heat - q_ym[0])
                flux_y_hi = 0.5 * (ky + ky_p) * (q_yp[0] - heat)
                diffused = flux_x_hi - flux_x_lo + flux_y_hi - flux_y_lo
                inflow = []
                for f in range(3):
                    lo_x = jnp.maximum(fvx_m, 0.0) * q_xm[f] + jnp.minimum(fvx_m, 0.0) * mobile[f]
                    hi_x = jnp.maximum(fvx_p, 0.0) * mobile[f] + jnp.minimum(fvx_p, 0.0) * q_xp[f]
                    lo_y = jnp.maximum(fvy_m, 0.0) * q_ym[f] + jnp.minimum(fvy_m, 0.0) * mobile[f]
                    hi_y = jnp.maximum(fvy_p, 0.0) * mobile[f] + jnp.minimum(fvy_p, 0.0) * q_yp[f]
                    inflow.append(lo_x - hi_x + lo_y - hi_y)
                heat_one = heat + diffused + HEAT_CARRY * inflow[0]
                water_two = water + inflow[1] + sill * WATER_INPUT
                carbon_two = carbon + inflow[2] + sill * CARBON_INPUT
                heat_two = heat_one + sill * SILL_RATE * (SILL_HEAT - heat_one)
                z = MELT_SHARPNESS * (heat_two - SOLIDUS + DEPRESSION * water_two)
                target = 1.0 / (1.0 + jnp.exp(-z))
                melt_two = melt + MELT_RATE * (target - melt)
                heat_three = heat_two - LATENT * (melt_two - melt)
                ho_ref[i] = heat_three
                wo_ref[i] = water_two
                cbo_ref[i] = carbon_two
                mo_ref[i] = melt_two
                acc.add_y([heat_three, water_two, carbon_two], d, lane)
            planes = pl.ds(a * ROWS, ROWS)
            for f, out in enumerate((ho_ref, wo_ref, cbo_ref)):
                xf_ref[f, a] = out[planes, 0, :]
                xl_ref[f, a] = out[planes, ROWS - 1, :]
            return (tuple(acc.yf), tuple(acc.yl))

        y_f, y_l = lax.fori_loop(0, groups, group, ((zero,) * 3, (zero,) * 3))
        for f in range(3):
            y_ref[0, f] = y_f[f]
            y_ref[1, f] = y_l[f]

    return kernel


def sweep_kernel(r_ref, cz_ref, y_ref, a_ref, b_ref, red_ref, c_s, g_s, vy_s, va_s):
    n = r_ref.shape[0]
    zero = jnp.zeros(r_ref.shape[1:], f32)
    one = jnp.ones(r_ref.shape[1:], f32)

    def conduct(i, carry):
        c_s[i] = cz_ref[0, i] * jnp.exp(-SOFTEN * r_ref[i])
        return carry

    lax.fori_loop(0, n, conduct, 0)

    def forward(i, carry):
        g_prev, vy_prev, va_prev = carry
        up = 0.5 * (c_s[i - 1] + c_s[i])
        down = 0.5 * (c_s[i] + c_s[i + 1])
        inv = 1.0 / (1.0 + up + down - up * g_prev)
        g = down * inv
        vy = (r_ref[i] + up * vy_prev) * inv
        va = (up * va_prev) * inv
        g_s[i] = g
        vy_s[i] = vy
        va_s[i] = va
        return g, vy, va

    lax.fori_loop(1, n - 1, forward, (zero, zero, one))

    def backward(k, carry):
        i = n - 2 - k
        y_next, a_next, b_next = carry
        g = g_s[i]
        y = vy_s[i] + g * y_next
        a = va_s[i] + g * a_next
        b = g * b_next
        y_ref[i] = y
        a_ref[i] = a
        b_ref[i] = b
        return y, a, b

    lax.fori_loop(0, n - 2, backward, (zero, zero, one))
    y_ref[0] = zero
    a_ref[0] = one
    b_ref[0] = zero
    y_ref[n - 1] = zero
    a_ref[n - 1] = zero
    b_ref[n - 1] = one
    up_first = 0.5 * (c_s[0] + c_s[1])
    up_last = 0.5 * (c_s[n - 2] + c_s[n - 1])
    red_ref[0] = 1.0 + up_first * (1.0 - a_ref[1])
    red_ref[1] = up_first * b_ref[1]
    red_ref[2] = r_ref[0] + up_first * y_ref[1]
    red_ref[3] = 1.0 + up_last * (1.0 - b_ref[n - 2])
    red_ref[4] = up_last * a_ref[n - 2]
    red_ref[5] = r_ref[n - 1] + up_last * y_ref[n - 2]
    red_ref[6] = c_s[0]
    red_ref[7] = c_s[n - 1]


def reduced_solve(red_all):
    count = len(red_all)
    lower, diag, upper, side = [], [], [], []
    for j in range(count):
        p0, q0, s0, p1, q1, s1, c_first, c_last = red_all[j]
        if j == 0:
            face = c_first
            lower.append(jnp.zeros_like(face))
        else:
            face = 0.5 * (red_all[j - 1][7] + c_first)
            lower.append(face)
        diag.append(p0 + face)
        upper.append(q0)
        side.append(s0)
        if j + 1 < count:
            below = 0.5 * (c_last + red_all[j + 1][6])
        else:
            below = jnp.zeros_like(c_last)
        lower.append(q1)
        diag.append(p1 + below)
        upper.append(below)
        side.append(s1)
    size = len(diag)
    ratios, values = [], []
    g_prev = jnp.zeros_like(diag[0])
    v_prev = jnp.zeros_like(diag[0])
    for k in range(size):
        inv = 1.0 / (diag[k] - lower[k] * g_prev)
        g_prev = upper[k] * inv
        v_prev = (side[k] + lower[k] * v_prev) * inv
        ratios.append(g_prev)
        values.append(v_prev)
    solved = [None] * size
    following = jnp.zeros_like(diag[0])
    for k in reversed(range(size)):
        following = values[k] + ratios[k] * following
        solved[k] = following
    return solved


def finish_kernel(rank_ref, y_ref, a_ref, b_ref, *rest):
    recv = rest[:-1]
    t_ref = rest[-1]
    count = len(recv)
    rank = rank_ref[0]
    red_all = []
    for j in range(count):
        source = (rank - j + count) % count
        planes = []
        for k in range(8):
            v = recv[count - 1][k]
            for m in reversed(range(count - 1)):
                v = jnp.where(source == m, recv[m][k], v)
            planes.append(v)
        red_all.append(planes)
    solved = reduced_solve(red_all)
    first = solved[2 * (count - 1)]
    last = solved[2 * (count - 1) + 1]
    for j in reversed(range(count - 1)):
        first = jnp.where(rank == j, solved[2 * j], first)
        last = jnp.where(rank == j, solved[2 * j + 1], last)

    def combine(i, carry):
        t_ref[i] = y_ref[i] + a_ref[i] * first + b_ref[i] * last
        return carry

    lax.fori_loop(0, y_ref.shape[0], combine, 0)


def sds(shape):
    return jax.ShapeDtypeStruct(shape, f32)


def exchange(xf, xl, ys):
    east_fwd, east_bwd = ring_perms("east")
    north_fwd, north_bwd = ring_perms("north")
    xlo = lax.ppermute(xl, "east", east_fwd)
    xhi = lax.ppermute(xf, "east", east_bwd)
    ylo = lax.ppermute(ys, "north", north_fwd)
    if lax.axis_size("north") == 2:
        yhi = ylo
    else:
        yhi = lax.ppermute(ys, "north", north_bwd)
    return xlo, xhi, ylo, yhi


def full_spec(shape):
    zeros = (0,) * len(shape)
    return pl.BlockSpec(shape, lambda i: zeros)


def local(
    thermal_field,
    liquid_fraction,
    steam_content_grid,
    carbonic_gas_grid,
    stratum_number_grid,
    injection_flags,
    lateral_transmissivity,
    vertical_transmissivity,
    stratum_advection_offsets,
):
    shape = thermal_field.shape
    n = shape[0]
    groups = n // ROWS
    assert shape[1:] == (ROWS, LANES) and n % ROWS == 0 and n <= LANES
    chunks = CHUNKS if groups % CHUNKS == 0 else 1
    depth = n // chunks
    cgroups = depth // ROWS
    smem_spec = pl.BlockSpec(memory_space=pltpu.SMEM)
    vspec = pl.BlockSpec(memory_space=pltpu.MemorySpace.VMEM)
    heat, water, carbon, melt, co, xf0, xl0, y0 = pl.pallas_call(
        prep_kernel,
        out_shape=(sds(shape), sds(shape), sds(shape), sds(shape), sds((5,) + shape),
                   sds((5, groups, ROWS, LANES)), sds((5, groups, ROWS, LANES)),
                   sds((2, 5, ROWS, LANES))),
        in_specs=[smem_spec] * 3 + [vspec] * 5,
    )(lateral_transmissivity, vertical_transmissivity, stratum_advection_offsets, stratum_number_grid, thermal_field, steam_content_grid, carbonic_gas_grid,
      liquid_fraction)
    xflo, xfhi, yflo, yfhi = exchange(xf0, xl0, y0)

    def block_spec(k):
        return pl.BlockSpec((depth, ROWS, LANES), lambda i: (k, 0, 0))

    halos = [None] * chunks
    nears = [None] * chunks
    x3 = full_spec((3, cgroups, ROWS, LANES))
    y3 = full_spec((2, 3, ROWS, LANES))
    near_spec = full_spec((8, depth, ROWS, LANES))
    for section_no in range(SECTIONS):
        first = section_no == 0
        for k in range(chunks):
            args = [heat, water, carbon, melt, injection_flags, co]
            in_specs = [block_spec(k)] * 5
            out_shape = [sds(shape)] * 4 + [sds((3, cgroups, ROWS, LANES))] * 2
            out_shape += [sds((2, 3, ROWS, LANES))]
            out_specs = [block_spec(k)] * 4 + [x3, x3, y3]
            if first:
                x5 = pl.BlockSpec((5, cgroups, ROWS, LANES), lambda i, k=k: (0, k, 0, 0))
                y5 = full_spec((2, 5, ROWS, LANES))
                in_specs += [pl.BlockSpec((4, depth, ROWS, LANES), lambda i, k=k: (0, k, 0, 0)),
                             x5, x5, y5, y5]
                args += [xflo, xfhi, yflo, yfhi]
                out_shape += [sds((8, depth, ROWS, LANES))]
                out_specs += [near_spec]
            else:
                in_specs += [pl.BlockSpec((2, depth, ROWS, LANES), lambda i, k=k: (0, k, 0, 0)),
                             near_spec, x3, x3, y3, y3]
                args += [nears[k]] + list(halos[k])
            outs = pl.pallas_call(
                make_section_kernel(k, first),
                grid=(1,),
                out_shape=tuple(out_shape),
                in_specs=in_specs,
                out_specs=out_specs,
                input_output_aliases={0: 0, 1: 1, 2: 2, 3: 3},
            )(*args)
            heat, water, carbon, melt, xf, xl, ys = outs[:7]
            if first:
                nears[k] = outs[7]
            if section_no + 1 < SECTIONS:
                halos[k] = exchange(xf, xl, ys)

    y, a, b, red = pl.pallas_call(
        sweep_kernel,
        grid=(1,),
        out_shape=(sds(shape), sds(shape), sds(shape), sds((8,) + shape[1:])),
        in_specs=[full_spec(shape), pl.BlockSpec((1,) + shape, lambda i: (4, 0, 0, 0))],
        out_specs=[full_spec(shape)] * 3 + [full_spec((8,) + shape[1:])],
        scratch_shapes=[pltpu.VMEM(shape, f32)] * 4,
    )(heat, co)
    count = lax.axis_size("depth")
    rank = lax.axis_index("depth")
    received = [red]
    for k in range(1, count):
        received.append(lax.ppermute(red, "depth", [(i, (i + k) % count) for i in range(count)]))
    rank_arr = jnp.full((1,), rank, jnp.int32)
    heat_next = pl.pallas_call(
        finish_kernel,
        out_shape=sds(shape),
        in_specs=[smem_spec] + [vspec] * (3 + count),
    )(rank_arr, y, a, b, *received)
    return (heat_next, melt, water, carbon)


def solution(mesh):
    placed = (
        P("depth", "east", "north"),
        P("depth", "east", "north"),
        P("depth", "east", "north"),
        P("depth", "east", "north"),
        P("depth", "east", "north"),
        P("depth", "east", "north"),
        P(),
        P(),
        P(),
    )
    return jax.shard_map(
        local,
        mesh=mesh,
        in_specs=placed,
        out_specs=(
            P("depth", "east", "north"),
            P("depth", "east", "north"),
            P("depth", "east", "north"),
            P("depth", "east", "north"),
        ),
        check_vma=False,
    )
```

```python
import jax
import jax.numpy as jnp
from jax import lax
from jax.experimental import pallas as pl
from jax.experimental.pallas import tpu as pltpu
from jax.sharding import PartitionSpec as P

SECTIONS = 4


SOFTEN = 0.5
HEAT_CARRY = 0.5
SILL_RATE = 0.3
SILL_HEAT = 2.5
WATER_INPUT = 0.2
CARBON_INPUT = 0.1
MELT_SHARPNESS = 4.0
SOLIDUS = 1.0
DEPRESSION = 0.5
MELT_RATE = 0.5
LATENT = 0.3

ROWS = 8
CHUNKS = 2
LANES = 128
f32 = jnp.float32


def ring_perms(axis):
    count = lax.axis_size(axis)
    forward = [(i, (i + 1) % count) for i in range(count)]
    backward = [((i + 1) % count, i) for i in range(count)]
    return forward, backward


def iotas():
    sub = lax.broadcasted_iota(jnp.int32, (ROWS, LANES), 0)
    lane = lax.broadcasted_iota(jnp.int32, (ROWS, LANES), 1)
    return sub, lane


class EdgeAcc:
    def __init__(self, count, y_first, y_last):
        zero = jnp.zeros((ROWS, LANES), f32)
        self.xf = [zero] * count
        self.xl = [zero] * count
        self.yf = list(y_first)
        self.yl = list(y_last)

    def add_x(self, planes, b):
        at_b = lax.broadcasted_iota(jnp.int32, (ROWS, LANES), 0) == b
        for f, v in enumerate(planes):
            self.xf[f] = jnp.where(at_b, pltpu.roll(v, b, 0), self.xf[f])
            self.xl[f] = jnp.where(at_b, pltpu.roll(v, (b + 1) % ROWS, 0), self.xl[f])

    def add_y(self, planes, d, lane):
        at_d = lane == d
        for f, v in enumerate(planes):
            self.yf[f] = jnp.where(at_d, pltpu.roll(v, d % LANES, 1), self.yf[f])
            self.yl[f] = jnp.where(at_d, pltpu.roll(v, (d + 1) % LANES, 1), self.yl[f])


def x_minus(v, lo_row, b, sub):
    return jnp.where(sub == 0, lo_row, pltpu.roll(v, 1, 0))


def x_plus(v, hi_row, b, sub):
    return jnp.where(sub == ROWS - 1, hi_row, pltpu.roll(v, ROWS - 1, 0))


def y_minus(v, lo_cols, d, lane):
    return jnp.where(lane == 0, pltpu.roll(lo_cols, (LANES - d) % LANES, 1), pltpu.roll(v, 1, 1))


def y_plus(v, hi_cols, d, lane):
    return jnp.where(
        lane == LANES - 1,
        pltpu.roll(hi_cols, (LANES - 1 - d) % LANES, 1),
        pltpu.roll(v, LANES - 1, 1),
    )


def prep_kernel(lat_ref, vert_ref, adv_ref, layer_ref, h_ref, w_ref, c_ref, m_ref,
                ho_ref, wo_ref, cbo_ref, mo_ref, co_ref, xf_ref, xl_ref, y_ref):
    groups = layer_ref.shape[0] // ROWS
    layers_count = vert_ref.shape[0]
    sub, lane = iotas()
    zero = jnp.zeros((ROWS, LANES), f32)

    def group(a, carry):
        y_f, y_l = carry
        acc = EdgeAcc(5, y_f, y_l)
        for b in range(ROWS):
            d = a * ROWS + b
            layer = layer_ref[d]
            vals = [zero] * 5
            for l in range(layers_count):
                hit = layer == l
                entries = (lat_ref[0, l], lat_ref[1, l], adv_ref[0, l], adv_ref[1, l], vert_ref[l])
                vals = [jnp.where(hit, entries[k], vals[k]) for k in range(5)]
            for k in range(5):
                co_ref[k, d] = vals[k]
            heat, water, carbon = h_ref[d], w_ref[d], c_ref[d]
            ho_ref[d] = heat
            wo_ref[d] = water
            cbo_ref[d] = carbon
            mo_ref[d] = m_ref[d]
            acc.add_y([heat, water, carbon, vals[1], vals[3]], d, lane)
        planes = pl.ds(a * ROWS, ROWS)
        sources = ((ho_ref, None), (wo_ref, None), (cbo_ref, None), (co_ref, 0), (co_ref, 2))
        for f, (out, field) in enumerate(sources):
            if field is None:
                xf_ref[f, a] = out[planes, 0, :]
                xl_ref[f, a] = out[planes, ROWS - 1, :]
            else:
                xf_ref[f, a] = out[field, planes, 0, :]
                xl_ref[f, a] = out[field, planes, ROWS - 1, :]
        return (tuple(acc.yf), tuple(acc.yl))

    y_f, y_l = lax.fori_loop(0, groups, group, ((zero,) * 5, (zero,) * 5))
    for f in range(5):
        y_ref[0, f] = y_f[f]
        y_ref[1, f] = y_l[f]


def make_section_kernel(chunk, first, last):
    def kernel(h_ref, w_ref, c_ref, m_ref, sill_ref, co_ref, *rest):
        if last:
            rest = rest + (None, None, None)
        if first:
            xflo_ref, xfhi_ref, yflo_ref, yfhi_ref = rest[:4]
            ho_ref, wo_ref, cbo_ref, mo_ref, nb_ref, xf_ref, xl_ref, y_ref = rest[4:]
            xslo_ref, xshi_ref, yslo_ref, yshi_ref = xflo_ref, xfhi_ref, yflo_ref, yfhi_ref
            cylo = [yflo_ref[1, f] for f in (3, 4)]
            cyhi = [yfhi_ref[0, f] for f in (3, 4)]
        else:
            nb_ref, xslo_ref, xshi_ref, yslo_ref, yshi_ref = rest[:5]
            ho_ref, wo_ref, cbo_ref, mo_ref, xf_ref, xl_ref, y_ref = rest[5:]
        depth = h_ref.shape[0]
        groups = depth // ROWS
        sub, lane = iotas()
        zero = jnp.zeros((ROWS, LANES), f32)
        sylo = [yslo_ref[1, f] for f in range(3)]
        syhi = [yshi_ref[0, f] for f in range(3)]

        def group(a, carry):
            y_f, y_l = carry
            acc = EdgeAcc(3, y_f, y_l)
            for b in range(ROWS):
                i = a * ROWS + b
                row = pl.ds(b, ROWS, stride=0)
                sxlo = [xslo_ref[f, a, row, :] for f in range(3)]
                sxhi = [xshi_ref[f, a, row, :] for f in range(3)]
                d = chunk * depth + i
                heat = h_ref[i]
                water = w_ref[i]
                carbon = c_ref[i]
                melt = m_ref[i]
                sill = sill_ref[i].astype(f32)
                cx = co_ref[0, i]
                cy = co_ref[1, i]
                mobile = [heat, water, carbon]
                q_xm = [x_minus(mobile[f], sxlo[f], b, sub) for f in range(3)]
                q_xp = [x_plus(mobile[f], sxhi[f], b, sub) for f in range(3)]
                q_ym = [y_minus(mobile[f], sylo[f], d, lane) for f in range(3)]
                q_yp = [y_plus(mobile[f], syhi[f], d, lane) for f in range(3)]
                if first:
                    cxlo = [xflo_ref[f, a, row, :] for f in (3, 4)]
                    cxhi = [xfhi_ref[f, a, row, :] for f in (3, 4)]
                    vx = co_ref[2, i]
                    vy = co_ref[3, i]
                    cx_m = x_minus(cx, cxlo[0], b, sub)
                    cx_p = x_plus(cx, cxhi[0], b, sub)
                    vx_m = x_minus(vx, cxlo[1], b, sub)
                    vx_p = x_plus(vx, cxhi[1], b, sub)
                    cy_m = y_minus(cy, cylo[0], d, lane)
                    cy_p = y_plus(cy, cyhi[0], d, lane)
                    vy_m = y_minus(vy, cylo[1], d, lane)
                    vy_p = y_plus(vy, cyhi[1], d, lane)
                    fvx_m = 0.5 * (vx_m + vx)
                    fvx_p = 0.5 * (vx + vx_p)
                    fvy_m = 0.5 * (vy_m + vy)
                    fvy_p = 0.5 * (vy + vy_p)
                    near = (cx_m, cx_p, cy_m, cy_p, fvx_m, fvx_p, fvy_m, fvy_p)
                    for f, v in enumerate(near):
                        nb_ref[f, i] = v
                else:
                    cx_m, cx_p, cy_m, cy_p, fvx_m, fvx_p, fvy_m, fvy_p = [
                        nb_ref[f, i] for f in range(8)
                    ]
                soft = jnp.exp(-SOFTEN * heat)
                kx = cx * soft
                ky = cy * soft
                kx_m = cx_m * jnp.exp(-SOFTEN * q_xm[0])
                kx_p = cx_p * jnp.exp(-SOFTEN * q_xp[0])
                ky_m = cy_m * jnp.exp(-SOFTEN * q_ym[0])
                ky_p = cy_p * jnp.exp(-SOFTEN * q_yp[0])
                flux_x_lo = 0.5 * (kx_m + kx) * (heat - q_xm[0])
                flux_x_hi = 0.5 * (kx + kx_p) * (q_xp[0] - heat)
                flux_y_lo = 0.5 * (ky_m + ky) * (heat - q_ym[0])
                flux_y_hi = 0.5 * (ky + ky_p) * (q_yp[0] - heat)
                diffused = flux_x_hi - flux_x_lo + flux_y_hi - flux_y_lo
                inflow = []
                for f in range(3):
                    lo_x = jnp.maximum(fvx_m, 0.0) * q_xm[f] + jnp.minimum(fvx_m, 0.0) * mobile[f]
                    hi_x = jnp.maximum(fvx_p, 0.0) * mobile[f] + jnp.minimum(fvx_p, 0.0) * q_xp[f]
                    lo_y = jnp.maximum(fvy_m, 0.0) * q_ym[f] + jnp.minimum(fvy_m, 0.0) * mobile[f]
                    hi_y = jnp.maximum(fvy_p, 0.0) * mobile[f] + jnp.minimum(fvy_p, 0.0) * q_yp[f]
                    inflow.append(lo_x - hi_x + lo_y - hi_y)
                heat_one = heat + diffused + HEAT_CARRY * inflow[0]
                water_two = water + inflow[1] + sill * WATER_INPUT
                carbon_two = carbon + inflow[2] + sill * CARBON_INPUT
                heat_two = heat_one + sill * SILL_RATE * (SILL_HEAT - heat_one)
                z = MELT_SHARPNESS * (heat_two - SOLIDUS + DEPRESSION * water_two)
                target = 1.0 / (1.0 + jnp.exp(-z))
                melt_two = melt + MELT_RATE * (target - melt)
                heat_three = heat_two - LATENT * (melt_two - melt)
                ho_ref[i] = heat_three
                wo_ref[i] = water_two
                cbo_ref[i] = carbon_two
                mo_ref[i] = melt_two
                if not last:
                    acc.add_y([heat_three, water_two, carbon_two], d, lane)
            if not last:
                planes = pl.ds(a * ROWS, ROWS)
                for f, out in enumerate((ho_ref, wo_ref, cbo_ref)):
                    xf_ref[f, a] = out[planes, 0, :]
                    xl_ref[f, a] = out[planes, ROWS - 1, :]
            return (tuple(acc.yf), tuple(acc.yl))

        y_f, y_l = lax.fori_loop(0, groups, group, ((zero,) * 3, (zero,) * 3))
        if not last:
            for f in range(3):
                y_ref[0, f] = y_f[f]
                y_ref[1, f] = y_l[f]

    return kernel


def sweep_kernel(r_ref, cz_ref, y_ref, a_ref, b_ref, red_ref, c_s, g_s, vy_s, va_s):
    n = r_ref.shape[0]
    zero = jnp.zeros(r_ref.shape[1:], f32)
    one = jnp.ones(r_ref.shape[1:], f32)

    def conduct(i, carry):
        c_s[i] = cz_ref[0, i] * jnp.exp(-SOFTEN * r_ref[i])
        return carry

    lax.fori_loop(0, n, conduct, 0)

    def forward(i, carry):
        g_prev, vy_prev, va_prev = carry
        up = 0.5 * (c_s[i - 1] + c_s[i])
        down = 0.5 * (c_s[i] + c_s[i + 1])
        inv = 1.0 / (1.0 + up + down - up * g_prev)
        g = down * inv
        vy = (r_ref[i] + up * vy_prev) * inv
        va = (up * va_prev) * inv
        g_s[i] = g
        vy_s[i] = vy
        va_s[i] = va
        return g, vy, va

    lax.fori_loop(1, n - 1, forward, (zero, zero, one))

    def backward(k, carry):
        i = n - 2 - k
        y_next, a_next, b_next = carry
        g = g_s[i]
        y = vy_s[i] + g * y_next
        a = va_s[i] + g * a_next
        b = g * b_next
        y_ref[i] = y
        a_ref[i] = a
        b_ref[i] = b
        return y, a, b

    lax.fori_loop(0, n - 2, backward, (zero, zero, one))
    y_ref[0] = zero
    a_ref[0] = one
    b_ref[0] = zero
    y_ref[n - 1] = zero
    a_ref[n - 1] = zero
    b_ref[n - 1] = one
    up_first = 0.5 * (c_s[0] + c_s[1])
    up_last = 0.5 * (c_s[n - 2] + c_s[n - 1])
    red_ref[0] = 1.0 + up_first * (1.0 - a_ref[1])
    red_ref[1] = up_first * b_ref[1]
    red_ref[2] = r_ref[0] + up_first * y_ref[1]
    red_ref[3] = 1.0 + up_last * (1.0 - b_ref[n - 2])
    red_ref[4] = up_last * a_ref[n - 2]
    red_ref[5] = r_ref[n - 1] + up_last * y_ref[n - 2]
    red_ref[6] = c_s[0]
    red_ref[7] = c_s[n - 1]


def reduced_solve(red_all):
    count = len(red_all)
    lower, diag, upper, side = [], [], [], []
    for j in range(count):
        p0, q0, s0, p1, q1, s1, c_first, c_last = red_all[j]
        if j == 0:
            face = c_first
            lower.append(jnp.zeros_like(face))
        else:
            face = 0.5 * (red_all[j - 1][7] + c_first)
            lower.append(face)
        diag.append(p0 + face)
        upper.append(q0)
        side.append(s0)
        if j + 1 < count:
            below = 0.5 * (c_last + red_all[j + 1][6])
        else:
            below = jnp.zeros_like(c_last)
        lower.append(q1)
        diag.append(p1 + below)
        upper.append(below)
        side.append(s1)
    size = len(diag)
    ratios, values = [], []
    g_prev = jnp.zeros_like(diag[0])
    v_prev = jnp.zeros_like(diag[0])
    for k in range(size):
        inv = 1.0 / (diag[k] - lower[k] * g_prev)
        g_prev = upper[k] * inv
        v_prev = (side[k] + lower[k] * v_prev) * inv
        ratios.append(g_prev)
        values.append(v_prev)
    solved = [None] * size
    following = jnp.zeros_like(diag[0])
    for k in reversed(range(size)):
        following = values[k] + ratios[k] * following
        solved[k] = following
    return solved


def finish_kernel(rank_ref, y_ref, a_ref, b_ref, *rest):
    recv = rest[:-1]
    t_ref = rest[-1]
    count = len(recv)
    rank = rank_ref[0]
    red_all = []
    for j in range(count):
        source = (rank - j + count) % count
        planes = []
        for k in range(8):
            v = recv[count - 1][k]
            for m in reversed(range(count - 1)):
                v = jnp.where(source == m, recv[m][k], v)
            planes.append(v)
        red_all.append(planes)
    solved = reduced_solve(red_all)
    first = solved[2 * (count - 1)]
    last = solved[2 * (count - 1) + 1]
    for j in reversed(range(count - 1)):
        first = jnp.where(rank == j, solved[2 * j], first)
        last = jnp.where(rank == j, solved[2 * j + 1], last)

    def combine(i, carry):
        t_ref[i] = y_ref[i] + a_ref[i] * first + b_ref[i] * last
        return carry

    lax.fori_loop(0, y_ref.shape[0], combine, 0)


def sds(shape):
    return jax.ShapeDtypeStruct(shape, f32)


def exchange(xf, xl, ys):
    east_fwd, east_bwd = ring_perms("east")
    north_fwd, north_bwd = ring_perms("north")
    xlo = lax.ppermute(xl, "east", east_fwd)
    xhi = lax.ppermute(xf, "east", east_bwd)
    ylo = lax.ppermute(ys, "north", north_fwd)
    if lax.axis_size("north") == 2:
        yhi = ylo
    else:
        yhi = lax.ppermute(ys, "north", north_bwd)
    return xlo, xhi, ylo, yhi


def full_spec(shape):
    zeros = (0,) * len(shape)
    return pl.BlockSpec(shape, lambda i: zeros)


def local(
    thermal_field,
    liquid_fraction,
    steam_content_grid,
    carbonic_gas_grid,
    stratum_number_grid,
    injection_flags,
    lateral_transmissivity,
    vertical_transmissivity,
    stratum_advection_offsets,
):
    shape = thermal_field.shape
    n = shape[0]
    groups = n // ROWS
    assert shape[1:] == (ROWS, LANES) and n % ROWS == 0 and n <= LANES
    chunks = CHUNKS if groups % CHUNKS == 0 else 1
    depth = n // chunks
    cgroups = depth // ROWS
    smem_spec = pl.BlockSpec(memory_space=pltpu.SMEM)
    vspec = pl.BlockSpec(memory_space=pltpu.MemorySpace.VMEM)
    heat, water, carbon, melt, co, xf0, xl0, y0 = pl.pallas_call(
        prep_kernel,
        out_shape=(sds(shape), sds(shape), sds(shape), sds(shape), sds((5,) + shape),
                   sds((5, groups, ROWS, LANES)), sds((5, groups, ROWS, LANES)),
                   sds((2, 5, ROWS, LANES))),
        in_specs=[smem_spec] * 3 + [vspec] * 5,
    )(lateral_transmissivity, vertical_transmissivity, stratum_advection_offsets, stratum_number_grid, thermal_field, steam_content_grid, carbonic_gas_grid,
      liquid_fraction)
    xflo, xfhi, yflo, yfhi = exchange(xf0, xl0, y0)

    def block_spec(k):
        return pl.BlockSpec((depth, ROWS, LANES), lambda i: (k, 0, 0))

    halos = [None] * chunks
    nears = [None] * chunks
    x3 = full_spec((3, cgroups, ROWS, LANES))
    y3 = full_spec((2, 3, ROWS, LANES))
    near_spec = full_spec((8, depth, ROWS, LANES))
    for section_no in range(SECTIONS):
        first = section_no == 0
        for k in range(chunks):
            last = section_no + 1 == SECTIONS
            args = [heat, water, carbon, melt, injection_flags, co]
            in_specs = [block_spec(k)] * 5
            out_shape = [sds(shape)] * 4
            out_specs = [block_spec(k)] * 4
            if first:
                x5 = pl.BlockSpec((5, cgroups, ROWS, LANES), lambda i, k=k: (0, k, 0, 0))
                y5 = full_spec((2, 5, ROWS, LANES))
                in_specs += [pl.BlockSpec((4, depth, ROWS, LANES), lambda i, k=k: (0, k, 0, 0)),
                             x5, x5, y5, y5]
                args += [xflo, xfhi, yflo, yfhi]
                out_shape += [sds((8, depth, ROWS, LANES))]
                out_specs += [near_spec]
            else:
                in_specs += [pl.BlockSpec((2, depth, ROWS, LANES), lambda i, k=k: (0, k, 0, 0)),
                             near_spec, x3, x3, y3, y3]
                args += [nears[k]] + list(halos[k])
            if not last:
                out_shape += [sds((3, cgroups, ROWS, LANES))] * 2 + [sds((2, 3, ROWS, LANES))]
                out_specs += [x3, x3, y3]
            outs = pl.pallas_call(
                make_section_kernel(k, first, last),
                grid=(1,),
                out_shape=tuple(out_shape),
                in_specs=in_specs,
                out_specs=out_specs,
                input_output_aliases={0: 0, 1: 1, 2: 2, 3: 3},
            )(*args)
            heat, water, carbon, melt = outs[:4]
            rest = list(outs[4:])
            if first:
                nears[k] = rest.pop(0)
            if not last:
                halos[k] = exchange(*rest)

    y, a, b, red = pl.pallas_call(
        sweep_kernel,
        grid=(1,),
        out_shape=(sds(shape), sds(shape), sds(shape), sds((8,) + shape[1:])),
        in_specs=[full_spec(shape), pl.BlockSpec((1,) + shape, lambda i: (4, 0, 0, 0))],
        out_specs=[full_spec(shape)] * 3 + [full_spec((8,) + shape[1:])],
        scratch_shapes=[pltpu.VMEM(shape, f32)] * 4,
    )(heat, co)
    count = lax.axis_size("depth")
    rank = lax.axis_index("depth")
    received = [red]
    for k in range(1, count):
        received.append(lax.ppermute(red, "depth", [(i, (i + k) % count) for i in range(count)]))
    rank_arr = jnp.full((1,), rank, jnp.int32)
    heat_next = pl.pallas_call(
        finish_kernel,
        out_shape=sds(shape),
        in_specs=[smem_spec] + [vspec] * (3 + count),
    )(rank_arr, y, a, b, *received)
    return (heat_next, melt, water, carbon)


def solution(mesh):
    placed = (
        P("depth", "east", "north"),
        P("depth", "east", "north"),
        P("depth", "east", "north"),
        P("depth", "east", "north"),
        P("depth", "east", "north"),
        P("depth", "east", "north"),
        P(),
        P(),
        P(),
    )
    return jax.shard_map(
        local,
        mesh=mesh,
        in_specs=placed,
        out_specs=(
            P("depth", "east", "north"),
            P("depth", "east", "north"),
            P("depth", "east", "north"),
            P("depth", "east", "north"),
        ),
        check_vma=False,
    )
```

```python
import jax
import jax.numpy as jnp
from jax import lax
from jax.experimental import pallas as pl
from jax.experimental.pallas import tpu as pltpu
from jax.sharding import PartitionSpec as P

SECTIONS = 4


SOFTEN = 0.5
HEAT_CARRY = 0.5
SILL_RATE = 0.3
SILL_HEAT = 2.5
WATER_INPUT = 0.2
CARBON_INPUT = 0.1
MELT_SHARPNESS = 4.0
SOLIDUS = 1.0
DEPRESSION = 0.5
MELT_RATE = 0.5
LATENT = 0.3

ROWS = 8
CHUNKS = 2
LANES = 128
f32 = jnp.float32


def ring_perms(axis):
    count = lax.axis_size(axis)
    forward = [(i, (i + 1) % count) for i in range(count)]
    backward = [((i + 1) % count, i) for i in range(count)]
    return forward, backward


def iotas():
    sub = lax.broadcasted_iota(jnp.int32, (ROWS, LANES), 0)
    lane = lax.broadcasted_iota(jnp.int32, (ROWS, LANES), 1)
    return sub, lane


class EdgeAcc:
    def __init__(self, count, y_first, y_last):
        zero = jnp.zeros((ROWS, LANES), f32)
        self.xf = [zero] * count
        self.xl = [zero] * count
        self.yf = list(y_first)
        self.yl = list(y_last)

    def add_x(self, planes, b):
        at_b = lax.broadcasted_iota(jnp.int32, (ROWS, LANES), 0) == b
        for f, v in enumerate(planes):
            self.xf[f] = jnp.where(at_b, pltpu.roll(v, b, 0), self.xf[f])
            self.xl[f] = jnp.where(at_b, pltpu.roll(v, (b + 1) % ROWS, 0), self.xl[f])

    def add_y(self, planes, d, lane):
        at_d = lane == d
        for f, v in enumerate(planes):
            self.yf[f] = jnp.where(at_d, pltpu.roll(v, d % LANES, 1), self.yf[f])
            self.yl[f] = jnp.where(at_d, pltpu.roll(v, (d + 1) % LANES, 1), self.yl[f])


def x_minus(v, lo_row, b, sub):
    return jnp.where(sub == 0, lo_row, pltpu.roll(v, 1, 0))


def x_plus(v, hi_row, b, sub):
    return jnp.where(sub == ROWS - 1, hi_row, pltpu.roll(v, ROWS - 1, 0))


def y_minus(v, lo_cols, d, lane):
    return jnp.where(lane == 0, pltpu.roll(lo_cols, (LANES - d) % LANES, 1), pltpu.roll(v, 1, 1))


def y_plus(v, hi_cols, d, lane):
    return jnp.where(
        lane == LANES - 1,
        pltpu.roll(hi_cols, (LANES - 1 - d) % LANES, 1),
        pltpu.roll(v, LANES - 1, 1),
    )


def prep_kernel(lat_ref, vert_ref, adv_ref, layer_ref, h_ref, w_ref, c_ref, m_ref,
                ho_ref, wo_ref, cbo_ref, mo_ref, co_ref, xf_ref, xl_ref, y_ref):
    groups = layer_ref.shape[0] // ROWS
    layers_count = vert_ref.shape[0]
    sub, lane = iotas()
    zero = jnp.zeros((ROWS, LANES), f32)

    def group(a, carry):
        y_f, y_l = carry
        acc = EdgeAcc(5, y_f, y_l)
        for b in range(ROWS):
            d = a * ROWS + b
            layer = layer_ref[d]
            vals = [zero] * 5
            for l in range(layers_count):
                hit = layer == l
                entries = (lat_ref[0, l], lat_ref[1, l], adv_ref[0, l], adv_ref[1, l], vert_ref[l])
                vals = [jnp.where(hit, entries[k], vals[k]) for k in range(5)]
            for k in range(5):
                co_ref[k, d] = vals[k]
            heat, water, carbon = h_ref[d], w_ref[d], c_ref[d]
            ho_ref[d] = heat
            wo_ref[d] = water
            cbo_ref[d] = carbon
            mo_ref[d] = m_ref[d]
            acc.add_y([heat, water, carbon, vals[1], vals[3]], d, lane)
        planes = pl.ds(a * ROWS, ROWS)
        sources = ((ho_ref, None), (wo_ref, None), (cbo_ref, None), (co_ref, 0), (co_ref, 2))
        for f, (out, field) in enumerate(sources):
            if field is None:
                xf_ref[f, a] = out[planes, 0, :]
                xl_ref[f, a] = out[planes, ROWS - 1, :]
            else:
                xf_ref[f, a] = out[field, planes, 0, :]
                xl_ref[f, a] = out[field, planes, ROWS - 1, :]
        return (tuple(acc.yf), tuple(acc.yl))

    y_f, y_l = lax.fori_loop(0, groups, group, ((zero,) * 5, (zero,) * 5))
    for f in range(5):
        y_ref[0, f] = y_f[f]
        y_ref[1, f] = y_l[f]


def make_section_kernel(chunk, first, last):
    def kernel(h_ref, w_ref, c_ref, m_ref, sill_ref, co_ref, *rest):
        if last:
            rest = rest + (None, None, None)
        if first:
            xflo_ref, xfhi_ref, yflo_ref, yfhi_ref = rest[:4]
            ho_ref, wo_ref, cbo_ref, mo_ref, nb_ref, xf_ref, xl_ref, y_ref = rest[4:]
            xslo_ref, xshi_ref, yslo_ref, yshi_ref = xflo_ref, xfhi_ref, yflo_ref, yfhi_ref
            cylo = [yflo_ref[1, f] for f in (3, 4)]
            cyhi = [yfhi_ref[0, f] for f in (3, 4)]
        else:
            nb_ref, xslo_ref, xshi_ref, yslo_ref, yshi_ref = rest[:5]
            ho_ref, wo_ref, cbo_ref, mo_ref, xf_ref, xl_ref, y_ref = rest[5:]
        depth = h_ref.shape[0]
        groups = depth // ROWS
        sub, lane = iotas()
        zero = jnp.zeros((ROWS, LANES), f32)
        sylo = [yslo_ref[1, f] for f in range(3)]
        syhi = [yshi_ref[0, f] for f in range(3)]

        def group(a, carry):
            y_f, y_l = carry
            acc = EdgeAcc(3, y_f, y_l)
            for b in range(ROWS):
                i = a * ROWS + b
                row = pl.ds(b, ROWS, stride=0)
                sxlo = [xslo_ref[f, a, row, :] for f in range(3)]
                sxhi = [xshi_ref[f, a, row, :] for f in range(3)]
                d = chunk * depth + i
                heat = h_ref[i]
                water = w_ref[i]
                carbon = c_ref[i]
                melt = m_ref[i]
                sill = sill_ref[i].astype(f32)
                cx = co_ref[0, i]
                cy = co_ref[1, i]
                mobile = [heat, water, carbon]
                q_xm = [x_minus(mobile[f], sxlo[f], b, sub) for f in range(3)]
                q_xp = [x_plus(mobile[f], sxhi[f], b, sub) for f in range(3)]
                q_ym = [y_minus(mobile[f], sylo[f], d, lane) for f in range(3)]
                q_yp = [y_plus(mobile[f], syhi[f], d, lane) for f in range(3)]
                if first:
                    cxlo = [xflo_ref[f, a, row, :] for f in (3, 4)]
                    cxhi = [xfhi_ref[f, a, row, :] for f in (3, 4)]
                    vx = co_ref[2, i]
                    vy = co_ref[3, i]
                    cx_m = x_minus(cx, cxlo[0], b, sub)
                    cx_p = x_plus(cx, cxhi[0], b, sub)
                    vx_m = x_minus(vx, cxlo[1], b, sub)
                    vx_p = x_plus(vx, cxhi[1], b, sub)
                    cy_m = y_minus(cy, cylo[0], d, lane)
                    cy_p = y_plus(cy, cyhi[0], d, lane)
                    vy_m = y_minus(vy, cylo[1], d, lane)
                    vy_p = y_plus(vy, cyhi[1], d, lane)
                    fvx_m = 0.5 * (vx_m + vx)
                    fvx_p = 0.5 * (vx + vx_p)
                    fvy_m = 0.5 * (vy_m + vy)
                    fvy_p = 0.5 * (vy + vy_p)
                    near = (cx_m, cx_p, cy_m, cy_p, fvx_m, fvx_p, fvy_m, fvy_p)
                    for f, v in enumerate(near):
                        nb_ref[f, i] = v
                else:
                    cx_m, cx_p, cy_m, cy_p, fvx_m, fvx_p, fvy_m, fvy_p = [
                        nb_ref[f, i] for f in range(8)
                    ]
                soft = jnp.exp(-SOFTEN * heat)
                kx = cx * soft
                ky = cy * soft
                kx_m = cx_m * jnp.exp(-SOFTEN * q_xm[0])
                kx_p = cx_p * jnp.exp(-SOFTEN * q_xp[0])
                ky_m = cy_m * jnp.exp(-SOFTEN * q_ym[0])
                ky_p = cy_p * jnp.exp(-SOFTEN * q_yp[0])
                flux_x_lo = 0.5 * (kx_m + kx) * (heat - q_xm[0])
                flux_x_hi = 0.5 * (kx + kx_p) * (q_xp[0] - heat)
                flux_y_lo = 0.5 * (ky_m + ky) * (heat - q_ym[0])
                flux_y_hi = 0.5 * (ky + ky_p) * (q_yp[0] - heat)
                diffused = flux_x_hi - flux_x_lo + flux_y_hi - flux_y_lo
                inflow = []
                for f in range(3):
                    lo_x = jnp.maximum(fvx_m, 0.0) * q_xm[f] + jnp.minimum(fvx_m, 0.0) * mobile[f]
                    hi_x = jnp.maximum(fvx_p, 0.0) * mobile[f] + jnp.minimum(fvx_p, 0.0) * q_xp[f]
                    lo_y = jnp.maximum(fvy_m, 0.0) * q_ym[f] + jnp.minimum(fvy_m, 0.0) * mobile[f]
                    hi_y = jnp.maximum(fvy_p, 0.0) * mobile[f] + jnp.minimum(fvy_p, 0.0) * q_yp[f]
                    inflow.append(lo_x - hi_x + lo_y - hi_y)
                heat_one = heat + diffused + HEAT_CARRY * inflow[0]
                water_two = water + inflow[1] + sill * WATER_INPUT
                carbon_two = carbon + inflow[2] + sill * CARBON_INPUT
                heat_two = heat_one + sill * SILL_RATE * (SILL_HEAT - heat_one)
                z = MELT_SHARPNESS * (heat_two - SOLIDUS + DEPRESSION * water_two)
                target = 1.0 / (1.0 + jnp.exp(-z))
                melt_two = melt + MELT_RATE * (target - melt)
                heat_three = heat_two - LATENT * (melt_two - melt)
                ho_ref[i] = heat_three
                wo_ref[i] = water_two
                cbo_ref[i] = carbon_two
                mo_ref[i] = melt_two
                if not last:
                    acc.add_y([heat_three, water_two, carbon_two], d, lane)
            if not last:
                planes = pl.ds(a * ROWS, ROWS)
                for f, out in enumerate((ho_ref, wo_ref, cbo_ref)):
                    xf_ref[f, a] = out[planes, 0, :]
                    xl_ref[f, a] = out[planes, ROWS - 1, :]
            return (tuple(acc.yf), tuple(acc.yl))

        y_f, y_l = lax.fori_loop(0, groups, group, ((zero,) * 3, (zero,) * 3))
        if not last:
            for f in range(3):
                y_ref[0, f] = y_f[f]
                y_ref[1, f] = y_l[f]

    return kernel


def sweep_kernel(r_ref, cz_ref, y_ref, a_ref, b_ref, red_ref, c_s, g_s, vy_s, va_s):
    n = r_ref.shape[0]
    zero = jnp.zeros(r_ref.shape[1:], f32)
    one = jnp.ones(r_ref.shape[1:], f32)

    def conduct(i, carry):
        c_s[i] = cz_ref[0, i] * jnp.exp(-SOFTEN * r_ref[i])
        return carry

    lax.fori_loop(0, n, conduct, 0, unroll=8)

    def forward(i, carry):
        g_prev, vy_prev, va_prev = carry
        up = 0.5 * (c_s[i - 1] + c_s[i])
        down = 0.5 * (c_s[i] + c_s[i + 1])
        inv = 1.0 / (1.0 + up + down - up * g_prev)
        g = down * inv
        vy = (r_ref[i] + up * vy_prev) * inv
        va = (up * va_prev) * inv
        g_s[i] = g
        vy_s[i] = vy
        va_s[i] = va
        return g, vy, va

    lax.fori_loop(1, n - 1, forward, (zero, zero, one))

    def backward(k, carry):
        i = n - 2 - k
        y_next, a_next, b_next = carry
        g = g_s[i]
        y = vy_s[i] + g * y_next
        a = va_s[i] + g * a_next
        b = g * b_next
        y_ref[i] = y
        a_ref[i] = a
        b_ref[i] = b
        return y, a, b

    lax.fori_loop(0, n - 2, backward, (zero, zero, one))
    y_ref[0] = zero
    a_ref[0] = one
    b_ref[0] = zero
    y_ref[n - 1] = zero
    a_ref[n - 1] = zero
    b_ref[n - 1] = one
    up_first = 0.5 * (c_s[0] + c_s[1])
    up_last = 0.5 * (c_s[n - 2] + c_s[n - 1])
    red_ref[0] = 1.0 + up_first * (1.0 - a_ref[1])
    red_ref[1] = up_first * b_ref[1]
    red_ref[2] = r_ref[0] + up_first * y_ref[1]
    red_ref[3] = 1.0 + up_last * (1.0 - b_ref[n - 2])
    red_ref[4] = up_last * a_ref[n - 2]
    red_ref[5] = r_ref[n - 1] + up_last * y_ref[n - 2]
    red_ref[6] = c_s[0]
    red_ref[7] = c_s[n - 1]


def reduced_solve(red_all):
    count = len(red_all)
    lower, diag, upper, side = [], [], [], []
    for j in range(count):
        p0, q0, s0, p1, q1, s1, c_first, c_last = red_all[j]
        if j == 0:
            face = c_first
            lower.append(jnp.zeros_like(face))
        else:
            face = 0.5 * (red_all[j - 1][7] + c_first)
            lower.append(face)
        diag.append(p0 + face)
        upper.append(q0)
        side.append(s0)
        if j + 1 < count:
            below = 0.5 * (c_last + red_all[j + 1][6])
        else:
            below = jnp.zeros_like(c_last)
        lower.append(q1)
        diag.append(p1 + below)
        upper.append(below)
        side.append(s1)
    size = len(diag)
    ratios, values = [], []
    g_prev = jnp.zeros_like(diag[0])
    v_prev = jnp.zeros_like(diag[0])
    for k in range(size):
        inv = 1.0 / (diag[k] - lower[k] * g_prev)
        g_prev = upper[k] * inv
        v_prev = (side[k] + lower[k] * v_prev) * inv
        ratios.append(g_prev)
        values.append(v_prev)
    solved = [None] * size
    following = jnp.zeros_like(diag[0])
    for k in reversed(range(size)):
        following = values[k] + ratios[k] * following
        solved[k] = following
    return solved


def finish_kernel(rank_ref, y_ref, a_ref, b_ref, *rest):
    recv = rest[:-1]
    t_ref = rest[-1]
    count = len(recv)
    rank = rank_ref[0]
    red_all = []
    for j in range(count):
        source = (rank - j + count) % count
        planes = []
        for k in range(8):
            v = recv[count - 1][k]
            for m in reversed(range(count - 1)):
                v = jnp.where(source == m, recv[m][k], v)
            planes.append(v)
        red_all.append(planes)
    solved = reduced_solve(red_all)
    first = solved[2 * (count - 1)]
    last = solved[2 * (count - 1) + 1]
    for j in reversed(range(count - 1)):
        first = jnp.where(rank == j, solved[2 * j], first)
        last = jnp.where(rank == j, solved[2 * j + 1], last)

    def combine(i, carry):
        t_ref[i] = y_ref[i] + a_ref[i] * first + b_ref[i] * last
        return carry

    lax.fori_loop(0, y_ref.shape[0], combine, 0, unroll=8)


def sds(shape):
    return jax.ShapeDtypeStruct(shape, f32)


def exchange(xf, xl, ys):
    east_fwd, east_bwd = ring_perms("east")
    north_fwd, north_bwd = ring_perms("north")
    xlo = lax.ppermute(xl, "east", east_fwd)
    xhi = lax.ppermute(xf, "east", east_bwd)
    ylo = lax.ppermute(ys, "north", north_fwd)
    if lax.axis_size("north") == 2:
        yhi = ylo
    else:
        yhi = lax.ppermute(ys, "north", north_bwd)
    return xlo, xhi, ylo, yhi


def full_spec(shape):
    zeros = (0,) * len(shape)
    return pl.BlockSpec(shape, lambda i: zeros)


def local(
    thermal_field,
    liquid_fraction,
    steam_content_grid,
    carbonic_gas_grid,
    stratum_number_grid,
    injection_flags,
    lateral_transmissivity,
    vertical_transmissivity,
    stratum_advection_offsets,
):
    shape = thermal_field.shape
    n = shape[0]
    groups = n // ROWS
    assert shape[1:] == (ROWS, LANES) and n % ROWS == 0 and n <= LANES
    chunks = CHUNKS if groups % CHUNKS == 0 else 1
    depth = n // chunks
    cgroups = depth // ROWS
    smem_spec = pl.BlockSpec(memory_space=pltpu.SMEM)
    vspec = pl.BlockSpec(memory_space=pltpu.MemorySpace.VMEM)
    heat, water, carbon, melt, co, xf0, xl0, y0 = pl.pallas_call(
        prep_kernel,
        out_shape=(sds(shape), sds(shape), sds(shape), sds(shape), sds((5,) + shape),
                   sds((5, groups, ROWS, LANES)), sds((5, groups, ROWS, LANES)),
                   sds((2, 5, ROWS, LANES))),
        in_specs=[smem_spec] * 3 + [vspec] * 5,
    )(lateral_transmissivity, vertical_transmissivity, stratum_advection_offsets, stratum_number_grid, thermal_field, steam_content_grid, carbonic_gas_grid,
      liquid_fraction)
    xflo, xfhi, yflo, yfhi = exchange(xf0, xl0, y0)

    def block_spec(k):
        return pl.BlockSpec((depth, ROWS, LANES), lambda i: (k, 0, 0))

    halos = [None] * chunks
    nears = [None] * chunks
    x3 = full_spec((3, cgroups, ROWS, LANES))
    y3 = full_spec((2, 3, ROWS, LANES))
    near_spec = full_spec((8, depth, ROWS, LANES))
    for section_no in range(SECTIONS):
        first = section_no == 0
        for k in range(chunks):
            last = section_no + 1 == SECTIONS
            args = [heat, water, carbon, melt, injection_flags, co]
            in_specs = [block_spec(k)] * 5
            out_shape = [sds(shape)] * 4
            out_specs = [block_spec(k)] * 4
            if first:
                x5 = pl.BlockSpec((5, cgroups, ROWS, LANES), lambda i, k=k: (0, k, 0, 0))
                y5 = full_spec((2, 5, ROWS, LANES))
                in_specs += [pl.BlockSpec((4, depth, ROWS, LANES), lambda i, k=k: (0, k, 0, 0)),
                             x5, x5, y5, y5]
                args += [xflo, xfhi, yflo, yfhi]
                out_shape += [sds((8, depth, ROWS, LANES))]
                out_specs += [near_spec]
            else:
                in_specs += [pl.BlockSpec((2, depth, ROWS, LANES), lambda i, k=k: (0, k, 0, 0)),
                             near_spec, x3, x3, y3, y3]
                args += [nears[k]] + list(halos[k])
            if not last:
                out_shape += [sds((3, cgroups, ROWS, LANES))] * 2 + [sds((2, 3, ROWS, LANES))]
                out_specs += [x3, x3, y3]
            outs = pl.pallas_call(
                make_section_kernel(k, first, last),
                grid=(1,),
                out_shape=tuple(out_shape),
                in_specs=in_specs,
                out_specs=out_specs,
                input_output_aliases={0: 0, 1: 1, 2: 2, 3: 3},
            )(*args)
            heat, water, carbon, melt = outs[:4]
            rest = list(outs[4:])
            if first:
                nears[k] = rest.pop(0)
            if not last:
                halos[k] = exchange(*rest)

    y, a, b, red = pl.pallas_call(
        sweep_kernel,
        grid=(1,),
        out_shape=(sds(shape), sds(shape), sds(shape), sds((8,) + shape[1:])),
        in_specs=[full_spec(shape), pl.BlockSpec((1,) + shape, lambda i: (4, 0, 0, 0))],
        out_specs=[full_spec(shape)] * 3 + [full_spec((8,) + shape[1:])],
        scratch_shapes=[pltpu.VMEM(shape, f32)] * 4,
    )(heat, co)
    count = lax.axis_size("depth")
    rank = lax.axis_index("depth")
    received = [red]
    for k in range(1, count):
        received.append(lax.ppermute(red, "depth", [(i, (i + k) % count) for i in range(count)]))
    rank_arr = jnp.full((1,), rank, jnp.int32)
    heat_next = pl.pallas_call(
        finish_kernel,
        out_shape=sds(shape),
        in_specs=[smem_spec] + [vspec] * (3 + count),
    )(rank_arr, y, a, b, *received)
    return (heat_next, melt, water, carbon)


def solution(mesh):
    placed = (
        P("depth", "east", "north"),
        P("depth", "east", "north"),
        P("depth", "east", "north"),
        P("depth", "east", "north"),
        P("depth", "east", "north"),
        P("depth", "east", "north"),
        P(),
        P(),
        P(),
    )
    return jax.shard_map(
        local,
        mesh=mesh,
        in_specs=placed,
        out_specs=(
            P("depth", "east", "north"),
            P("depth", "east", "north"),
            P("depth", "east", "north"),
            P("depth", "east", "north"),
        ),
        check_vma=False,
    )
```

```python
import jax
import jax.numpy as jnp
from jax import lax
from jax.experimental import pallas as pl
from jax.experimental.pallas import tpu as pltpu
from jax.sharding import PartitionSpec as P

SECTIONS = 4


SOFTEN = 0.5
HEAT_CARRY = 0.5
SILL_RATE = 0.3
SILL_HEAT = 2.5
WATER_INPUT = 0.2
CARBON_INPUT = 0.1
MELT_SHARPNESS = 4.0
SOLIDUS = 1.0
DEPRESSION = 0.5
MELT_RATE = 0.5
LATENT = 0.3

ROWS = 8
CHUNKS = 2
LANES = 128
f32 = jnp.float32


def ring_perms(axis):
    count = lax.axis_size(axis)
    forward = [(i, (i + 1) % count) for i in range(count)]
    backward = [((i + 1) % count, i) for i in range(count)]
    return forward, backward


def iotas():
    sub = lax.broadcasted_iota(jnp.int32, (ROWS, LANES), 0)
    lane = lax.broadcasted_iota(jnp.int32, (ROWS, LANES), 1)
    return sub, lane


class EdgeAcc:
    def __init__(self, count, y_first, y_last):
        zero = jnp.zeros((ROWS, LANES), f32)
        self.xf = [zero] * count
        self.xl = [zero] * count
        self.yf = list(y_first)
        self.yl = list(y_last)

    def add_x(self, planes, b):
        at_b = lax.broadcasted_iota(jnp.int32, (ROWS, LANES), 0) == b
        for f, v in enumerate(planes):
            self.xf[f] = jnp.where(at_b, pltpu.roll(v, b, 0), self.xf[f])
            self.xl[f] = jnp.where(at_b, pltpu.roll(v, (b + 1) % ROWS, 0), self.xl[f])

    def add_y(self, planes, d, lane):
        at_d = lane == d
        for f, v in enumerate(planes):
            self.yf[f] = jnp.where(at_d, pltpu.roll(v, d % LANES, 1), self.yf[f])
            self.yl[f] = jnp.where(at_d, pltpu.roll(v, (d + 1) % LANES, 1), self.yl[f])


def x_minus(v, lo_row, b, sub):
    return jnp.where(sub == 0, lo_row, pltpu.roll(v, 1, 0))


def x_plus(v, hi_row, b, sub):
    return jnp.where(sub == ROWS - 1, hi_row, pltpu.roll(v, ROWS - 1, 0))


def y_minus(v, lo_cols, d, lane):
    return jnp.where(lane == 0, pltpu.roll(lo_cols, (LANES - d) % LANES, 1), pltpu.roll(v, 1, 1))


def y_plus(v, hi_cols, d, lane):
    return jnp.where(
        lane == LANES - 1,
        pltpu.roll(hi_cols, (LANES - 1 - d) % LANES, 1),
        pltpu.roll(v, LANES - 1, 1),
    )


def prep_kernel(lat_ref, vert_ref, adv_ref, layer_ref, h_ref, w_ref, c_ref, m_ref,
                ho_ref, wo_ref, cbo_ref, mo_ref, co_ref, xf_ref, xl_ref, y_ref):
    groups = layer_ref.shape[0] // ROWS
    layers_count = vert_ref.shape[0]
    sub, lane = iotas()
    zero = jnp.zeros((ROWS, LANES), f32)

    def group(a, carry):
        y_f, y_l = carry
        acc = EdgeAcc(5, y_f, y_l)
        for b in range(ROWS):
            d = a * ROWS + b
            layer = layer_ref[d]
            vals = [zero] * 5
            for l in range(layers_count):
                hit = layer == l
                entries = (lat_ref[0, l], lat_ref[1, l], adv_ref[0, l], adv_ref[1, l], vert_ref[l])
                vals = [jnp.where(hit, entries[k], vals[k]) for k in range(5)]
            for k in range(5):
                co_ref[k, d] = vals[k]
            heat, water, carbon = h_ref[d], w_ref[d], c_ref[d]
            ho_ref[d] = heat
            wo_ref[d] = water
            cbo_ref[d] = carbon
            mo_ref[d] = m_ref[d]
            acc.add_y([heat, water, carbon, vals[1], vals[3]], d, lane)
        planes = pl.ds(a * ROWS, ROWS)
        sources = ((ho_ref, None), (wo_ref, None), (cbo_ref, None), (co_ref, 0), (co_ref, 2))
        for f, (out, field) in enumerate(sources):
            if field is None:
                xf_ref[f, a] = out[planes, 0, :]
                xl_ref[f, a] = out[planes, ROWS - 1, :]
            else:
                xf_ref[f, a] = out[field, planes, 0, :]
                xl_ref[f, a] = out[field, planes, ROWS - 1, :]
        return (tuple(acc.yf), tuple(acc.yl))

    y_f, y_l = lax.fori_loop(0, groups, group, ((zero,) * 5, (zero,) * 5))
    for f in range(5):
        y_ref[0, f] = y_f[f]
        y_ref[1, f] = y_l[f]


def make_section_kernel(chunk, first, last):
    def kernel(h_ref, w_ref, c_ref, m_ref, sill_ref, co_ref, *rest):
        if last:
            rest = rest + (None, None, None)
        if first:
            xflo_ref, xfhi_ref, yflo_ref, yfhi_ref = rest[:4]
            ho_ref, wo_ref, cbo_ref, mo_ref, nb_ref, xf_ref, xl_ref, y_ref = rest[4:]
            xslo_ref, xshi_ref, yslo_ref, yshi_ref = xflo_ref, xfhi_ref, yflo_ref, yfhi_ref
            cylo = [yflo_ref[1, f] for f in (3, 4)]
            cyhi = [yfhi_ref[0, f] for f in (3, 4)]
        else:
            nb_ref, xslo_ref, xshi_ref, yslo_ref, yshi_ref = rest[:5]
            ho_ref, wo_ref, cbo_ref, mo_ref, xf_ref, xl_ref, y_ref = rest[5:]
        depth = h_ref.shape[0]
        groups = depth // ROWS
        sub, lane = iotas()
        zero = jnp.zeros((ROWS, LANES), f32)
        sylo = [yslo_ref[1, f] for f in range(3)]
        syhi = [yshi_ref[0, f] for f in range(3)]

        def group(a, carry):
            y_f, y_l = carry
            acc = EdgeAcc(3, y_f, y_l)
            for b in range(ROWS):
                i = a * ROWS + b
                row = pl.ds(b, ROWS, stride=0)
                sxlo = [xslo_ref[f, a, row, :] for f in range(3)]
                sxhi = [xshi_ref[f, a, row, :] for f in range(3)]
                d = chunk * depth + i
                heat = h_ref[i]
                water = w_ref[i]
                carbon = c_ref[i]
                melt = m_ref[i]
                sill = sill_ref[i].astype(f32)
                cx = co_ref[0, i]
                cy = co_ref[1, i]
                mobile = [heat, water, carbon]
                q_xm = [x_minus(mobile[f], sxlo[f], b, sub) for f in range(3)]
                q_xp = [x_plus(mobile[f], sxhi[f], b, sub) for f in range(3)]
                q_ym = [y_minus(mobile[f], sylo[f], d, lane) for f in range(3)]
                q_yp = [y_plus(mobile[f], syhi[f], d, lane) for f in range(3)]
                if first:
                    cxlo = [xflo_ref[f, a, row, :] for f in (3, 4)]
                    cxhi = [xfhi_ref[f, a, row, :] for f in (3, 4)]
                    vx = co_ref[2, i]
                    vy = co_ref[3, i]
                    cx_m = x_minus(cx, cxlo[0], b, sub)
                    cx_p = x_plus(cx, cxhi[0], b, sub)
                    vx_m = x_minus(vx, cxlo[1], b, sub)
                    vx_p = x_plus(vx, cxhi[1], b, sub)
                    cy_m = y_minus(cy, cylo[0], d, lane)
                    cy_p = y_plus(cy, cyhi[0], d, lane)
                    vy_m = y_minus(vy, cylo[1], d, lane)
                    vy_p = y_plus(vy, cyhi[1], d, lane)
                    fvx_m = 0.5 * (vx_m + vx)
                    fvx_p = 0.5 * (vx + vx_p)
                    fvy_m = 0.5 * (vy_m + vy)
                    fvy_p = 0.5 * (vy + vy_p)
                    near = (cx_m, cx_p, cy_m, cy_p, fvx_m, fvx_p, fvy_m, fvy_p)
                    for f, v in enumerate(near):
                        nb_ref[f, i] = v
                else:
                    cx_m, cx_p, cy_m, cy_p, fvx_m, fvx_p, fvy_m, fvy_p = [
                        nb_ref[f, i] for f in range(8)
                    ]
                soft = jnp.exp(-SOFTEN * heat)
                kx = cx * soft
                ky = cy * soft
                kx_m = cx_m * jnp.exp(-SOFTEN * q_xm[0])
                kx_p = cx_p * jnp.exp(-SOFTEN * q_xp[0])
                ky_m = cy_m * jnp.exp(-SOFTEN * q_ym[0])
                ky_p = cy_p * jnp.exp(-SOFTEN * q_yp[0])
                flux_x_lo = 0.5 * (kx_m + kx) * (heat - q_xm[0])
                flux_x_hi = 0.5 * (kx + kx_p) * (q_xp[0] - heat)
                flux_y_lo = 0.5 * (ky_m + ky) * (heat - q_ym[0])
                flux_y_hi = 0.5 * (ky + ky_p) * (q_yp[0] - heat)
                diffused = flux_x_hi - flux_x_lo + flux_y_hi - flux_y_lo
                inflow = []
                for f in range(3):
                    lo_x = jnp.maximum(fvx_m, 0.0) * q_xm[f] + jnp.minimum(fvx_m, 0.0) * mobile[f]
                    hi_x = jnp.maximum(fvx_p, 0.0) * mobile[f] + jnp.minimum(fvx_p, 0.0) * q_xp[f]
                    lo_y = jnp.maximum(fvy_m, 0.0) * q_ym[f] + jnp.minimum(fvy_m, 0.0) * mobile[f]
                    hi_y = jnp.maximum(fvy_p, 0.0) * mobile[f] + jnp.minimum(fvy_p, 0.0) * q_yp[f]
                    inflow.append(lo_x - hi_x + lo_y - hi_y)
                heat_one = heat + diffused + HEAT_CARRY * inflow[0]
                water_two = water + inflow[1] + sill * WATER_INPUT
                carbon_two = carbon + inflow[2] + sill * CARBON_INPUT
                heat_two = heat_one + sill * SILL_RATE * (SILL_HEAT - heat_one)
                z = MELT_SHARPNESS * (heat_two - SOLIDUS + DEPRESSION * water_two)
                target = 1.0 / (1.0 + jnp.exp(-z))
                melt_two = melt + MELT_RATE * (target - melt)
                heat_three = heat_two - LATENT * (melt_two - melt)
                ho_ref[i] = heat_three
                wo_ref[i] = water_two
                cbo_ref[i] = carbon_two
                mo_ref[i] = melt_two
                if not last:
                    acc.add_y([heat_three, water_two, carbon_two], d, lane)
            if not last:
                planes = pl.ds(a * ROWS, ROWS)
                for f, out in enumerate((ho_ref, wo_ref, cbo_ref)):
                    xf_ref[f, a] = out[planes, 0, :]
                    xl_ref[f, a] = out[planes, ROWS - 1, :]
            return (tuple(acc.yf), tuple(acc.yl))

        y_f, y_l = lax.fori_loop(0, groups, group, ((zero,) * 3, (zero,) * 3))
        if not last:
            for f in range(3):
                y_ref[0, f] = y_f[f]
                y_ref[1, f] = y_l[f]

    return kernel


def sweep_kernel(r_ref, cz_ref, y_ref, a_ref, b_ref, red_ref, c_s, g_s, vy_s, va_s):
    n = r_ref.shape[0]
    zero = jnp.zeros(r_ref.shape[1:], f32)
    one = jnp.ones(r_ref.shape[1:], f32)

    def conduct(i, carry):
        c_s[i] = cz_ref[0, i] * jnp.exp(-SOFTEN * r_ref[i])
        return carry

    lax.fori_loop(0, n, conduct, 0, unroll=8)

    def forward(i, carry):
        g_prev, vy_prev, va_prev = carry
        up = 0.5 * (c_s[i - 1] + c_s[i])
        down = 0.5 * (c_s[i] + c_s[i + 1])
        inv = 1.0 / (1.0 + up + down - up * g_prev)
        g = down * inv
        vy = (r_ref[i] + up * vy_prev) * inv
        va = (up * va_prev) * inv
        g_s[i] = g
        vy_s[i] = vy
        va_s[i] = va
        return g, vy, va

    lax.fori_loop(1, n - 1, forward, (zero, zero, one), unroll=2)

    def backward(k, carry):
        i = n - 2 - k
        y_next, a_next, b_next = carry
        g = g_s[i]
        y = vy_s[i] + g * y_next
        a = va_s[i] + g * a_next
        b = g * b_next
        y_ref[i] = y
        a_ref[i] = a
        b_ref[i] = b
        return y, a, b

    lax.fori_loop(0, n - 2, backward, (zero, zero, one), unroll=2)
    y_ref[0] = zero
    a_ref[0] = one
    b_ref[0] = zero
    y_ref[n - 1] = zero
    a_ref[n - 1] = zero
    b_ref[n - 1] = one
    up_first = 0.5 * (c_s[0] + c_s[1])
    up_last = 0.5 * (c_s[n - 2] + c_s[n - 1])
    red_ref[0] = 1.0 + up_first * (1.0 - a_ref[1])
    red_ref[1] = up_first * b_ref[1]
    red_ref[2] = r_ref[0] + up_first * y_ref[1]
    red_ref[3] = 1.0 + up_last * (1.0 - b_ref[n - 2])
    red_ref[4] = up_last * a_ref[n - 2]
    red_ref[5] = r_ref[n - 1] + up_last * y_ref[n - 2]
    red_ref[6] = c_s[0]
    red_ref[7] = c_s[n - 1]


def reduced_solve(red_all):
    count = len(red_all)
    lower, diag, upper, side = [], [], [], []
    for j in range(count):
        p0, q0, s0, p1, q1, s1, c_first, c_last = red_all[j]
        if j == 0:
            face = c_first
            lower.append(jnp.zeros_like(face))
        else:
            face = 0.5 * (red_all[j - 1][7] + c_first)
            lower.append(face)
        diag.append(p0 + face)
        upper.append(q0)
        side.append(s0)
        if j + 1 < count:
            below = 0.5 * (c_last + red_all[j + 1][6])
        else:
            below = jnp.zeros_like(c_last)
        lower.append(q1)
        diag.append(p1 + below)
        upper.append(below)
        side.append(s1)
    size = len(diag)
    ratios, values = [], []
    g_prev = jnp.zeros_like(diag[0])
    v_prev = jnp.zeros_like(diag[0])
    for k in range(size):
        inv = 1.0 / (diag[k] - lower[k] * g_prev)
        g_prev = upper[k] * inv
        v_prev = (side[k] + lower[k] * v_prev) * inv
        ratios.append(g_prev)
        values.append(v_prev)
    solved = [None] * size
    following = jnp.zeros_like(diag[0])
    for k in reversed(range(size)):
        following = values[k] + ratios[k] * following
        solved[k] = following
    return solved


def finish_kernel(rank_ref, y_ref, a_ref, b_ref, *rest):
    recv = rest[:-1]
    t_ref = rest[-1]
    count = len(recv)
    rank = rank_ref[0]
    red_all = []
    for j in range(count):
        source = (rank - j + count) % count
        planes = []
        for k in range(8):
            v = recv[count - 1][k]
            for m in reversed(range(count - 1)):
                v = jnp.where(source == m, recv[m][k], v)
            planes.append(v)
        red_all.append(planes)
    solved = reduced_solve(red_all)
    first = solved[2 * (count - 1)]
    last = solved[2 * (count - 1) + 1]
    for j in reversed(range(count - 1)):
        first = jnp.where(rank == j, solved[2 * j], first)
        last = jnp.where(rank == j, solved[2 * j + 1], last)

    def combine(i, carry):
        t_ref[i] = y_ref[i] + a_ref[i] * first + b_ref[i] * last
        return carry

    lax.fori_loop(0, y_ref.shape[0], combine, 0, unroll=8)


def sds(shape):
    return jax.ShapeDtypeStruct(shape, f32)


def exchange(xf, xl, ys):
    east_fwd, east_bwd = ring_perms("east")
    north_fwd, north_bwd = ring_perms("north")
    xlo = lax.ppermute(xl, "east", east_fwd)
    xhi = lax.ppermute(xf, "east", east_bwd)
    ylo = lax.ppermute(ys, "north", north_fwd)
    if lax.axis_size("north") == 2:
        yhi = ylo
    else:
        yhi = lax.ppermute(ys, "north", north_bwd)
    return xlo, xhi, ylo, yhi


def full_spec(shape):
    zeros = (0,) * len(shape)
    return pl.BlockSpec(shape, lambda i: zeros)


def local(
    thermal_field,
    liquid_fraction,
    steam_content_grid,
    carbonic_gas_grid,
    stratum_number_grid,
    injection_flags,
    lateral_transmissivity,
    vertical_transmissivity,
    stratum_advection_offsets,
):
    shape = thermal_field.shape
    n = shape[0]
    groups = n // ROWS
    assert shape[1:] == (ROWS, LANES) and n % ROWS == 0 and n <= LANES
    chunks = CHUNKS if groups % CHUNKS == 0 else 1
    depth = n // chunks
    cgroups = depth // ROWS
    smem_spec = pl.BlockSpec(memory_space=pltpu.SMEM)
    vspec = pl.BlockSpec(memory_space=pltpu.MemorySpace.VMEM)
    heat, water, carbon, melt, co, xf0, xl0, y0 = pl.pallas_call(
        prep_kernel,
        out_shape=(sds(shape), sds(shape), sds(shape), sds(shape), sds((5,) + shape),
                   sds((5, groups, ROWS, LANES)), sds((5, groups, ROWS, LANES)),
                   sds((2, 5, ROWS, LANES))),
        in_specs=[smem_spec] * 3 + [vspec] * 5,
    )(lateral_transmissivity, vertical_transmissivity, stratum_advection_offsets, stratum_number_grid, thermal_field, steam_content_grid, carbonic_gas_grid,
      liquid_fraction)
    xflo, xfhi, yflo, yfhi = exchange(xf0, xl0, y0)

    def block_spec(k):
        return pl.BlockSpec((depth, ROWS, LANES), lambda i: (k, 0, 0))

    halos = [None] * chunks
    nears = [None] * chunks
    x3 = full_spec((3, cgroups, ROWS, LANES))
    y3 = full_spec((2, 3, ROWS, LANES))
    near_spec = full_spec((8, depth, ROWS, LANES))
    for section_no in range(SECTIONS):
        first = section_no == 0
        for k in range(chunks):
            last = section_no + 1 == SECTIONS
            args = [heat, water, carbon, melt, injection_flags, co]
            in_specs = [block_spec(k)] * 5
            out_shape = [sds(shape)] * 4
            out_specs = [block_spec(k)] * 4
            if first:
                x5 = pl.BlockSpec((5, cgroups, ROWS, LANES), lambda i, k=k: (0, k, 0, 0))
                y5 = full_spec((2, 5, ROWS, LANES))
                in_specs += [pl.BlockSpec((4, depth, ROWS, LANES), lambda i, k=k: (0, k, 0, 0)),
                             x5, x5, y5, y5]
                args += [xflo, xfhi, yflo, yfhi]
                out_shape += [sds((8, depth, ROWS, LANES))]
                out_specs += [near_spec]
            else:
                in_specs += [pl.BlockSpec((2, depth, ROWS, LANES), lambda i, k=k: (0, k, 0, 0)),
                             near_spec, x3, x3, y3, y3]
                args += [nears[k]] + list(halos[k])
            if not last:
                out_shape += [sds((3, cgroups, ROWS, LANES))] * 2 + [sds((2, 3, ROWS, LANES))]
                out_specs += [x3, x3, y3]
            outs = pl.pallas_call(
                make_section_kernel(k, first, last),
                grid=(1,),
                out_shape=tuple(out_shape),
                in_specs=in_specs,
                out_specs=out_specs,
                input_output_aliases={0: 0, 1: 1, 2: 2, 3: 3},
            )(*args)
            heat, water, carbon, melt = outs[:4]
            rest = list(outs[4:])
            if first:
                nears[k] = rest.pop(0)
            if not last:
                halos[k] = exchange(*rest)

    y, a, b, red = pl.pallas_call(
        sweep_kernel,
        grid=(1,),
        out_shape=(sds(shape), sds(shape), sds(shape), sds((8,) + shape[1:])),
        in_specs=[full_spec(shape), pl.BlockSpec((1,) + shape, lambda i: (4, 0, 0, 0))],
        out_specs=[full_spec(shape)] * 3 + [full_spec((8,) + shape[1:])],
        scratch_shapes=[pltpu.VMEM(shape, f32)] * 4,
    )(heat, co)
    count = lax.axis_size("depth")
    rank = lax.axis_index("depth")
    received = [red]
    for k in range(1, count):
        received.append(lax.ppermute(red, "depth", [(i, (i + k) % count) for i in range(count)]))
    rank_arr = jnp.full((1,), rank, jnp.int32)
    heat_next = pl.pallas_call(
        finish_kernel,
        out_shape=sds(shape),
        in_specs=[smem_spec] + [vspec] * (3 + count),
    )(rank_arr, y, a, b, *received)
    return (heat_next, melt, water, carbon)


def solution(mesh):
    placed = (
        P("depth", "east", "north"),
        P("depth", "east", "north"),
        P("depth", "east", "north"),
        P("depth", "east", "north"),
        P("depth", "east", "north"),
        P("depth", "east", "north"),
        P(),
        P(),
        P(),
    )
    return jax.shard_map(
        local,
        mesh=mesh,
        in_specs=placed,
        out_specs=(
            P("depth", "east", "north"),
            P("depth", "east", "north"),
            P("depth", "east", "north"),
            P("depth", "east", "north"),
        ),
        check_vma=False,
    )
```

```python
import jax
import jax.numpy as jnp
from jax import lax
from jax.experimental import pallas as pl
from jax.experimental.pallas import tpu as pltpu
from jax.sharding import PartitionSpec as P

SECTIONS = 4


SOFTEN = 0.5
HEAT_CARRY = 0.5
SILL_RATE = 0.3
SILL_HEAT = 2.5
WATER_INPUT = 0.2
CARBON_INPUT = 0.1
MELT_SHARPNESS = 4.0
SOLIDUS = 1.0
DEPRESSION = 0.5
MELT_RATE = 0.5
LATENT = 0.3

ROWS = 8
CHUNKS = 2
LANES = 128
f32 = jnp.float32


def ring_perms(axis):
    count = lax.axis_size(axis)
    forward = [(i, (i + 1) % count) for i in range(count)]
    backward = [((i + 1) % count, i) for i in range(count)]
    return forward, backward


def iotas():
    sub = lax.broadcasted_iota(jnp.int32, (ROWS, LANES), 0)
    lane = lax.broadcasted_iota(jnp.int32, (ROWS, LANES), 1)
    return sub, lane


class EdgeAcc:
    def __init__(self, count, y_first, y_last):
        zero = jnp.zeros((ROWS, LANES), f32)
        self.xf = [zero] * count
        self.xl = [zero] * count
        self.yf = list(y_first)
        self.yl = list(y_last)

    def add_x(self, planes, b):
        at_b = lax.broadcasted_iota(jnp.int32, (ROWS, LANES), 0) == b
        for f, v in enumerate(planes):
            self.xf[f] = jnp.where(at_b, pltpu.roll(v, b, 0), self.xf[f])
            self.xl[f] = jnp.where(at_b, pltpu.roll(v, (b + 1) % ROWS, 0), self.xl[f])

    def add_y(self, planes, d, lane):
        at_d = lane == d
        for f, v in enumerate(planes):
            self.yf[f] = jnp.where(at_d, pltpu.roll(v, d % LANES, 1), self.yf[f])
            self.yl[f] = jnp.where(at_d, pltpu.roll(v, (d + 1) % LANES, 1), self.yl[f])


def x_minus(v, lo_row, b, sub):
    return jnp.where(sub == 0, lo_row, pltpu.roll(v, 1, 0))


def x_plus(v, hi_row, b, sub):
    return jnp.where(sub == ROWS - 1, hi_row, pltpu.roll(v, ROWS - 1, 0))


def y_minus(v, lo_cols, d, lane):
    return jnp.where(lane == 0, pltpu.roll(lo_cols, (LANES - d) % LANES, 1), pltpu.roll(v, 1, 1))


def y_plus(v, hi_cols, d, lane):
    return jnp.where(
        lane == LANES - 1,
        pltpu.roll(hi_cols, (LANES - 1 - d) % LANES, 1),
        pltpu.roll(v, LANES - 1, 1),
    )


def prep_kernel(lat_ref, vert_ref, adv_ref, layer_ref, h_ref, w_ref, c_ref, m_ref,
                ho_ref, wo_ref, cbo_ref, mo_ref, co_ref, xf_ref, xl_ref, y_ref):
    groups = layer_ref.shape[0] // ROWS
    layers_count = vert_ref.shape[0]
    sub, lane = iotas()
    zero = jnp.zeros((ROWS, LANES), f32)

    def group(a, carry):
        y_f, y_l = carry
        acc = EdgeAcc(5, y_f, y_l)
        for b in range(ROWS):
            d = a * ROWS + b
            layer = layer_ref[d]
            vals = [zero] * 5
            for l in range(layers_count):
                hit = layer == l
                entries = (lat_ref[0, l], lat_ref[1, l], adv_ref[0, l], adv_ref[1, l], vert_ref[l])
                vals = [jnp.where(hit, entries[k], vals[k]) for k in range(5)]
            for k in range(5):
                co_ref[k, d] = vals[k]
            heat, water, carbon = h_ref[d], w_ref[d], c_ref[d]
            ho_ref[d] = heat
            wo_ref[d] = water
            cbo_ref[d] = carbon
            mo_ref[d] = m_ref[d]
            acc.add_y([heat, water, carbon, vals[1], vals[3]], d, lane)
        planes = pl.ds(a * ROWS, ROWS)
        sources = ((ho_ref, None), (wo_ref, None), (cbo_ref, None), (co_ref, 0), (co_ref, 2))
        for f, (out, field) in enumerate(sources):
            if field is None:
                xf_ref[f, a] = out[planes, 0, :]
                xl_ref[f, a] = out[planes, ROWS - 1, :]
            else:
                xf_ref[f, a] = out[field, planes, 0, :]
                xl_ref[f, a] = out[field, planes, ROWS - 1, :]
        return (tuple(acc.yf), tuple(acc.yl))

    y_f, y_l = lax.fori_loop(0, groups, group, ((zero,) * 5, (zero,) * 5))
    for f in range(5):
        y_ref[0, f] = y_f[f]
        y_ref[1, f] = y_l[f]


def make_section_kernel(chunk, first, last):
    def kernel(h_ref, w_ref, c_ref, m_ref, sill_ref, co_ref, *rest):
        if last:
            rest = rest + (None, None, None)
        if first:
            xflo_ref, xfhi_ref, yflo_ref, yfhi_ref = rest[:4]
            ho_ref, wo_ref, cbo_ref, mo_ref, nb_ref, xf_ref, xl_ref, y_ref = rest[4:]
            xslo_ref, xshi_ref, yslo_ref, yshi_ref = xflo_ref, xfhi_ref, yflo_ref, yfhi_ref
            cylo = [yflo_ref[1, f] for f in (3, 4)]
            cyhi = [yfhi_ref[0, f] for f in (3, 4)]
        else:
            nb_ref, xslo_ref, xshi_ref, yslo_ref, yshi_ref = rest[:5]
            ho_ref, wo_ref, cbo_ref, mo_ref, xf_ref, xl_ref, y_ref = rest[5:]
        depth = h_ref.shape[0]
        groups = depth // ROWS
        sub, lane = iotas()
        zero = jnp.zeros((ROWS, LANES), f32)
        sylo = [yslo_ref[1, f] for f in range(3)]
        syhi = [yshi_ref[0, f] for f in range(3)]

        def group(a, carry):
            y_f, y_l = carry
            acc = EdgeAcc(3, y_f, y_l)
            for b in range(ROWS):
                i = a * ROWS + b
                row = pl.ds(b, ROWS, stride=0)
                sxlo = [xslo_ref[f, a, row, :] for f in range(3)]
                sxhi = [xshi_ref[f, a, row, :] for f in range(3)]
                d = chunk * depth + i
                heat = h_ref[i]
                water = w_ref[i]
                carbon = c_ref[i]
                melt = m_ref[i]
                sill = sill_ref[i].astype(f32)
                cx = co_ref[0, i]
                cy = co_ref[1, i]
                mobile = [heat, water, carbon]
                q_xm = [x_minus(mobile[f], sxlo[f], b, sub) for f in range(3)]
                q_xp = [x_plus(mobile[f], sxhi[f], b, sub) for f in range(3)]
                q_ym = [y_minus(mobile[f], sylo[f], d, lane) for f in range(3)]
                q_yp = [y_plus(mobile[f], syhi[f], d, lane) for f in range(3)]
                if first:
                    cxlo = [xflo_ref[f, a, row, :] for f in (3, 4)]
                    cxhi = [xfhi_ref[f, a, row, :] for f in (3, 4)]
                    vx = co_ref[2, i]
                    vy = co_ref[3, i]
                    cx_m = x_minus(cx, cxlo[0], b, sub)
                    cx_p = x_plus(cx, cxhi[0], b, sub)
                    vx_m = x_minus(vx, cxlo[1], b, sub)
                    vx_p = x_plus(vx, cxhi[1], b, sub)
                    cy_m = y_minus(cy, cylo[0], d, lane)
                    cy_p = y_plus(cy, cyhi[0], d, lane)
                    vy_m = y_minus(vy, cylo[1], d, lane)
                    vy_p = y_plus(vy, cyhi[1], d, lane)
                    fvx_m = 0.5 * (vx_m + vx)
                    fvx_p = 0.5 * (vx + vx_p)
                    fvy_m = 0.5 * (vy_m + vy)
                    fvy_p = 0.5 * (vy + vy_p)
                    near = (cx_m, cx_p, cy_m, cy_p, fvx_m, fvx_p, fvy_m, fvy_p)
                    for f, v in enumerate(near):
                        nb_ref[f, i] = v
                else:
                    cx_m, cx_p, cy_m, cy_p, fvx_m, fvx_p, fvy_m, fvy_p = [
                        nb_ref[f, i] for f in range(8)
                    ]
                soft = jnp.exp(-SOFTEN * heat)
                kx = cx * soft
                ky = cy * soft
                kx_m = cx_m * jnp.exp(-SOFTEN * q_xm[0])
                kx_p = cx_p * jnp.exp(-SOFTEN * q_xp[0])
                ky_m = cy_m * jnp.exp(-SOFTEN * q_ym[0])
                ky_p = cy_p * jnp.exp(-SOFTEN * q_yp[0])
                flux_x_lo = 0.5 * (kx_m + kx) * (heat - q_xm[0])
                flux_x_hi = 0.5 * (kx + kx_p) * (q_xp[0] - heat)
                flux_y_lo = 0.5 * (ky_m + ky) * (heat - q_ym[0])
                flux_y_hi = 0.5 * (ky + ky_p) * (q_yp[0] - heat)
                diffused = flux_x_hi - flux_x_lo + flux_y_hi - flux_y_lo
                inflow = []
                for f in range(3):
                    lo_x = jnp.maximum(fvx_m, 0.0) * q_xm[f] + jnp.minimum(fvx_m, 0.0) * mobile[f]
                    hi_x = jnp.maximum(fvx_p, 0.0) * mobile[f] + jnp.minimum(fvx_p, 0.0) * q_xp[f]
                    lo_y = jnp.maximum(fvy_m, 0.0) * q_ym[f] + jnp.minimum(fvy_m, 0.0) * mobile[f]
                    hi_y = jnp.maximum(fvy_p, 0.0) * mobile[f] + jnp.minimum(fvy_p, 0.0) * q_yp[f]
                    inflow.append(lo_x - hi_x + lo_y - hi_y)
                heat_one = heat + diffused + HEAT_CARRY * inflow[0]
                water_two = water + inflow[1] + sill * WATER_INPUT
                carbon_two = carbon + inflow[2] + sill * CARBON_INPUT
                heat_two = heat_one + sill * SILL_RATE * (SILL_HEAT - heat_one)
                z = MELT_SHARPNESS * (heat_two - SOLIDUS + DEPRESSION * water_two)
                target = 1.0 / (1.0 + jnp.exp(-z))
                melt_two = melt + MELT_RATE * (target - melt)
                heat_three = heat_two - LATENT * (melt_two - melt)
                ho_ref[i] = heat_three
                wo_ref[i] = water_two
                cbo_ref[i] = carbon_two
                mo_ref[i] = melt_two
                if not last:
                    acc.add_y([heat_three, water_two, carbon_two], d, lane)
            if not last:
                planes = pl.ds(a * ROWS, ROWS)
                for f, out in enumerate((ho_ref, wo_ref, cbo_ref)):
                    xf_ref[f, a] = out[planes, 0, :]
                    xl_ref[f, a] = out[planes, ROWS - 1, :]
            return (tuple(acc.yf), tuple(acc.yl))

        y_f, y_l = lax.fori_loop(0, groups, group, ((zero,) * 3, (zero,) * 3), unroll=2)
        if not last:
            for f in range(3):
                y_ref[0, f] = y_f[f]
                y_ref[1, f] = y_l[f]

    return kernel


def sweep_kernel(r_ref, cz_ref, y_ref, a_ref, b_ref, red_ref, c_s, g_s, vy_s, va_s):
    n = r_ref.shape[0]
    zero = jnp.zeros(r_ref.shape[1:], f32)
    one = jnp.ones(r_ref.shape[1:], f32)

    def conduct(i, carry):
        c_s[i] = cz_ref[0, i] * jnp.exp(-SOFTEN * r_ref[i])
        return carry

    lax.fori_loop(0, n, conduct, 0, unroll=8)

    def forward(i, carry):
        g_prev, vy_prev, va_prev = carry
        up = 0.5 * (c_s[i - 1] + c_s[i])
        down = 0.5 * (c_s[i] + c_s[i + 1])
        inv = 1.0 / (1.0 + up + down - up * g_prev)
        g = down * inv
        vy = (r_ref[i] + up * vy_prev) * inv
        va = (up * va_prev) * inv
        g_s[i] = g
        vy_s[i] = vy
        va_s[i] = va
        return g, vy, va

    lax.fori_loop(1, n - 1, forward, (zero, zero, one), unroll=2)

    def backward(k, carry):
        i = n - 2 - k
        y_next, a_next, b_next = carry
        g = g_s[i]
        y = vy_s[i] + g * y_next
        a = va_s[i] + g * a_next
        b = g * b_next
        y_ref[i] = y
        a_ref[i] = a
        b_ref[i] = b
        return y, a, b

    lax.fori_loop(0, n - 2, backward, (zero, zero, one), unroll=2)
    y_ref[0] = zero
    a_ref[0] = one
    b_ref[0] = zero
    y_ref[n - 1] = zero
    a_ref[n - 1] = zero
    b_ref[n - 1] = one
    up_first = 0.5 * (c_s[0] + c_s[1])
    up_last = 0.5 * (c_s[n - 2] + c_s[n - 1])
    red_ref[0] = 1.0 + up_first * (1.0 - a_ref[1])
    red_ref[1] = up_first * b_ref[1]
    red_ref[2] = r_ref[0] + up_first * y_ref[1]
    red_ref[3] = 1.0 + up_last * (1.0 - b_ref[n - 2])
    red_ref[4] = up_last * a_ref[n - 2]
    red_ref[5] = r_ref[n - 1] + up_last * y_ref[n - 2]
    red_ref[6] = c_s[0]
    red_ref[7] = c_s[n - 1]


def reduced_solve(red_all):
    count = len(red_all)
    lower, diag, upper, side = [], [], [], []
    for j in range(count):
        p0, q0, s0, p1, q1, s1, c_first, c_last = red_all[j]
        if j == 0:
            face = c_first
            lower.append(jnp.zeros_like(face))
        else:
            face = 0.5 * (red_all[j - 1][7] + c_first)
            lower.append(face)
        diag.append(p0 + face)
        upper.append(q0)
        side.append(s0)
        if j + 1 < count:
            below = 0.5 * (c_last + red_all[j + 1][6])
        else:
            below = jnp.zeros_like(c_last)
        lower.append(q1)
        diag.append(p1 + below)
        upper.append(below)
        side.append(s1)
    size = len(diag)
    ratios, values = [], []
    g_prev = jnp.zeros_like(diag[0])
    v_prev = jnp.zeros_like(diag[0])
    for k in range(size):
        inv = 1.0 / (diag[k] - lower[k] * g_prev)
        g_prev = upper[k] * inv
        v_prev = (side[k] + lower[k] * v_prev) * inv
        ratios.append(g_prev)
        values.append(v_prev)
    solved = [None] * size
    following = jnp.zeros_like(diag[0])
    for k in reversed(range(size)):
        following = values[k] + ratios[k] * following
        solved[k] = following
    return solved


def finish_kernel(rank_ref, y_ref, a_ref, b_ref, *rest):
    recv = rest[:-1]
    t_ref = rest[-1]
    count = len(recv)
    rank = rank_ref[0]
    red_all = []
    for j in range(count):
        source = (rank - j + count) % count
        planes = []
        for k in range(8):
            v = recv[count - 1][k]
            for m in reversed(range(count - 1)):
                v = jnp.where(source == m, recv[m][k], v)
            planes.append(v)
        red_all.append(planes)
    solved = reduced_solve(red_all)
    first = solved[2 * (count - 1)]
    last = solved[2 * (count - 1) + 1]
    for j in reversed(range(count - 1)):
        first = jnp.where(rank == j, solved[2 * j], first)
        last = jnp.where(rank == j, solved[2 * j + 1], last)

    def combine(i, carry):
        t_ref[i] = y_ref[i] + a_ref[i] * first + b_ref[i] * last
        return carry

    lax.fori_loop(0, y_ref.shape[0], combine, 0, unroll=8)


def sds(shape):
    return jax.ShapeDtypeStruct(shape, f32)


def exchange(xf, xl, ys):
    east_fwd, east_bwd = ring_perms("east")
    north_fwd, north_bwd = ring_perms("north")
    xlo = lax.ppermute(xl, "east", east_fwd)
    xhi = lax.ppermute(xf, "east", east_bwd)
    ylo = lax.ppermute(ys, "north", north_fwd)
    if lax.axis_size("north") == 2:
        yhi = ylo
    else:
        yhi = lax.ppermute(ys, "north", north_bwd)
    return xlo, xhi, ylo, yhi


def full_spec(shape):
    zeros = (0,) * len(shape)
    return pl.BlockSpec(shape, lambda i: zeros)


def local(
    thermal_field,
    liquid_fraction,
    steam_content_grid,
    carbonic_gas_grid,
    stratum_number_grid,
    injection_flags,
    lateral_transmissivity,
    vertical_transmissivity,
    stratum_advection_offsets,
):
    shape = thermal_field.shape
    n = shape[0]
    groups = n // ROWS
    assert shape[1:] == (ROWS, LANES) and n % ROWS == 0 and n <= LANES
    chunks = CHUNKS if groups % CHUNKS == 0 else 1
    depth = n // chunks
    cgroups = depth // ROWS
    smem_spec = pl.BlockSpec(memory_space=pltpu.SMEM)
    vspec = pl.BlockSpec(memory_space=pltpu.MemorySpace.VMEM)
    heat, water, carbon, melt, co, xf0, xl0, y0 = pl.pallas_call(
        prep_kernel,
        out_shape=(sds(shape), sds(shape), sds(shape), sds(shape), sds((5,) + shape),
                   sds((5, groups, ROWS, LANES)), sds((5, groups, ROWS, LANES)),
                   sds((2, 5, ROWS, LANES))),
        in_specs=[smem_spec] * 3 + [vspec] * 5,
    )(lateral_transmissivity, vertical_transmissivity, stratum_advection_offsets, stratum_number_grid, thermal_field, steam_content_grid, carbonic_gas_grid,
      liquid_fraction)
    xflo, xfhi, yflo, yfhi = exchange(xf0, xl0, y0)

    def block_spec(k):
        return pl.BlockSpec((depth, ROWS, LANES), lambda i: (k, 0, 0))

    halos = [None] * chunks
    nears = [None] * chunks
    x3 = full_spec((3, cgroups, ROWS, LANES))
    y3 = full_spec((2, 3, ROWS, LANES))
    near_spec = full_spec((8, depth, ROWS, LANES))
    for section_no in range(SECTIONS):
        first = section_no == 0
        for k in range(chunks):
            last = section_no + 1 == SECTIONS
            args = [heat, water, carbon, melt, injection_flags, co]
            in_specs = [block_spec(k)] * 5
            out_shape = [sds(shape)] * 4
            out_specs = [block_spec(k)] * 4
            if first:
                x5 = pl.BlockSpec((5, cgroups, ROWS, LANES), lambda i, k=k: (0, k, 0, 0))
                y5 = full_spec((2, 5, ROWS, LANES))
                in_specs += [pl.BlockSpec((4, depth, ROWS, LANES), lambda i, k=k: (0, k, 0, 0)),
                             x5, x5, y5, y5]
                args += [xflo, xfhi, yflo, yfhi]
                out_shape += [sds((8, depth, ROWS, LANES))]
                out_specs += [near_spec]
            else:
                in_specs += [pl.BlockSpec((2, depth, ROWS, LANES), lambda i, k=k: (0, k, 0, 0)),
                             near_spec, x3, x3, y3, y3]
                args += [nears[k]] + list(halos[k])
            if not last:
                out_shape += [sds((3, cgroups, ROWS, LANES))] * 2 + [sds((2, 3, ROWS, LANES))]
                out_specs += [x3, x3, y3]
            outs = pl.pallas_call(
                make_section_kernel(k, first, last),
                grid=(1,),
                out_shape=tuple(out_shape),
                in_specs=in_specs,
                out_specs=out_specs,
                input_output_aliases={0: 0, 1: 1, 2: 2, 3: 3},
            )(*args)
            heat, water, carbon, melt = outs[:4]
            rest = list(outs[4:])
            if first:
                nears[k] = rest.pop(0)
            if not last:
                halos[k] = exchange(*rest)

    y, a, b, red = pl.pallas_call(
        sweep_kernel,
        grid=(1,),
        out_shape=(sds(shape), sds(shape), sds(shape), sds((8,) + shape[1:])),
        in_specs=[full_spec(shape), pl.BlockSpec((1,) + shape, lambda i: (4, 0, 0, 0))],
        out_specs=[full_spec(shape)] * 3 + [full_spec((8,) + shape[1:])],
        scratch_shapes=[pltpu.VMEM(shape, f32)] * 4,
    )(heat, co)
    count = lax.axis_size("depth")
    rank = lax.axis_index("depth")
    received = [red]
    for k in range(1, count):
        received.append(lax.ppermute(red, "depth", [(i, (i + k) % count) for i in range(count)]))
    rank_arr = jnp.full((1,), rank, jnp.int32)
    heat_next = pl.pallas_call(
        finish_kernel,
        out_shape=sds(shape),
        in_specs=[smem_spec] + [vspec] * (3 + count),
    )(rank_arr, y, a, b, *received)
    return (heat_next, melt, water, carbon)


def solution(mesh):
    placed = (
        P("depth", "east", "north"),
        P("depth", "east", "north"),
        P("depth", "east", "north"),
        P("depth", "east", "north"),
        P("depth", "east", "north"),
        P("depth", "east", "north"),
        P(),
        P(),
        P(),
    )
    return jax.shard_map(
        local,
        mesh=mesh,
        in_specs=placed,
        out_specs=(
            P("depth", "east", "north"),
            P("depth", "east", "north"),
            P("depth", "east", "north"),
            P("depth", "east", "north"),
        ),
        check_vma=False,
    )
```
